32 devices in a mesh: groups: 2 (over x), tm: 8 (over z, y), pair: 2 (over core).
Axes of the slice: x: 2, y: 2, z: 4, core: 2. Of those that a mesh axis runs over, the one named last changes fastest.
Arguments:
- recording: bfloat16 [2048, 65536], P(('groups', 'pair'), 'tm'), parts along dimension 0
- fir_taps: bfloat16 [256], replicated, may hold values from -0.375 to 0.375
- kept_windows: int32 [16], P('groups'), parts along dimension 0, may hold values from 4 to 16, as said below
- pair_blocks: int32 [32, 2], P(('groups', 'pair')), parts along dimension 0, may hold values from 0 to 7
Outputs:
- cross_spectra: float32 [32, 128, 2, 128, 128], P(('groups', 'pair'), 'tm'), parts along dimension 0
The draws below stay inside these ranges and needn't reach their ends.
There are 2 independent parts, one for each index of `groups`. The reference program is written for one: setup_inputs(seed, part) draws one part's arguments, and reference() takes and returns one part's arrays. A program takes and returns all parts, laid end to end along the dimension named above; an argument that names none is the same for every part. Nothing has to cross between parts.
Inputs may be any that keep to these rules, and one draw needn't show every extreme that they name: Section s keeps its first kept_windows[s] windows; at least one section keeps all 16.
All inputs are finite; a program needn't handle non-finite values.
Results may differ from the reference program's by a relative error of at most 0.0056.
Values may be sent and summed in bfloat16 or wider, within the bound.
No kernel may reach another device: no remote copies, remote signals or barrier semaphores. Data moves between devices by JAX's collectives and lax.ppermute only.
A program may use at most 192 MiB of HBM per device.

```python
import math
import jax
import jax.numpy as jnp
from jax import lax

CH_BLK = 128
NBLK = 8
NCH = 1024
WIN = 512
TAPS = 256
NF = 128
FLO = 8
NWIN_DEV = 16
NT = 65536
NSEG = 8
NPB = 16


def draw_recording(key, part):
    key_base, key_gain, key_piece = jax.random.split(key, 3)
    gains = jnp.exp(jax.random.uniform(key_gain, (NCH, 1), jnp.float32, 0.0, math.log(10.0)))
    pieces = jnp.exp(jax.random.uniform(key_piece, (1, NT // WIN), jnp.float32, 0.0, math.log(4.0)))
    pieces = jnp.repeat(pieces, WIN, axis=1)
    base = jax.random.normal(key_base, (NCH, NT), jnp.float32)
    return (base * gains * pieces).astype(jnp.bfloat16)


def draw_kept_windows(key, part):
    key_counts, key_full = jax.random.split(jax.random.fold_in(key, 7), 2)
    counts = jax.random.randint(key_counts, (NSEG,), NWIN_DEV // 4, NWIN_DEV // 2 + 1)
    full_section = jax.random.randint(key_full, (), 0, NSEG)
    sections = jnp.arange(NSEG, dtype=jnp.int32)
    return jnp.where(sections == full_section, NWIN_DEV, counts).astype(jnp.int32)


def plant(drawn, key, smallest, top_value):
    index_at = [jax.random.randint(jax.random.fold_in(key, axis), (), 0, length) for axis, length in enumerate(drawn.shape)]
    main_axis = drawn.shape.index(max(drawn.shape))
    neighbour = index_at[:main_axis] + [(index_at[main_axis] + 1) % drawn.shape[main_axis]] + index_at[main_axis + 1:]
    return drawn.at[tuple(index_at)].set(smallest).at[tuple(neighbour)].set(top_value)


def centred(key, shape, deviation, limit, kind=jnp.bfloat16):
    return jnp.clip(deviation * jax.random.normal(key, shape, jnp.float32), -limit, limit).astype(kind)


def setup_inputs(seed: int = 0, part: int = 0) -> dict:
    streams_of = jax.random.split(jax.random.key(seed), 5)
    part_keys = jax.random.split(jax.random.fold_in(streams_of[4], part), 5)
    return {
        "recording": draw_recording(jax.random.fold_in(jax.random.fold_in(streams_of[4], part), 71), part),
        "fir_taps": centred(streams_of[1], (TAPS,), TAPS ** -0.5, 0.375),
        "kept_windows": draw_kept_windows(jax.random.fold_in(jax.random.fold_in(streams_of[4], part), 71), part),
        "pair_blocks": plant(jax.random.randint(part_keys[3], (NPB, 2), 0, NBLK), jax.random.fold_in(part_keys[3], 1), 0, NBLK - 1).astype(jnp.int32),
    }


whiten_eps = 1e-06

def toeplitz(fir_taps):
    length = fir_taps.shape[0]
    reversed_taps = fir_taps[::-1]
    base_column = jnp.concatenate([jnp.zeros((1,), fir_taps.dtype), reversed_taps, jnp.zeros((length,), fir_taps.dtype)])
    flattened = jnp.tile(base_column, length)[:2 * length * length]
    return flattened.reshape(length, 2 * length).T

def bandpass(recording, fir_taps, tail_rows):
    channels, length = recording.shape
    width = fir_taps.shape[0]
    current = recording.reshape(channels, length // width, width)
    previous = jnp.concatenate([tail_rows[:, None, :], current[:, :-1, :]], axis=1)
    extended = jnp.concatenate([previous, current], axis=2).reshape(channels * (length // width), 2 * width)
    product = jnp.dot(extended, toeplitz(fir_taps), preferred_element_type=jnp.float32)
    return product.reshape(channels, length).astype(jnp.bfloat16)

def dft_table(length, bins, lowest):
    samples = jnp.arange(length, dtype=jnp.int32)
    indices = lowest + jnp.arange(bins, dtype=jnp.int32)
    phase = (samples[:, None] * indices[None, :] % length).astype(jnp.float32) * (2.0 * math.pi / length)
    basis_table = jnp.stack([jnp.cos(phase), -jnp.sin(phase)], axis=2)
    return basis_table.reshape(length, 2 * bins).astype(jnp.bfloat16)

def reference(recording, fir_taps, kept_windows, pair_blocks):
    channels, length = recording.shape
    windows_all = length // WIN
    tail_rows = jnp.zeros((channels, TAPS), jnp.bfloat16)
    filtered = bandpass(recording, fir_taps, tail_rows)
    spectrum = jnp.dot(filtered.reshape(channels * windows_all, WIN), dft_table(WIN, NF, FLO), preferred_element_type=jnp.float32)
    spectrum = spectrum.reshape(channels, windows_all, 2 * NF)
    inverse_rms = lax.rsqrt(lax.optimization_barrier(jnp.mean(spectrum * spectrum, axis=2, keepdims=True)) + whiten_eps)
    window_ids = jnp.arange(windows_all, dtype=jnp.int32)
    window_mask = (window_ids % NWIN_DEV < kept_windows[window_ids // NWIN_DEV]).astype(jnp.float32)
    whitened = (spectrum * inverse_rms * window_mask[None, :, None]).astype(jnp.bfloat16)
    kept_total = jnp.sum(kept_windows).astype(jnp.float32)
    stack_scale = 1.0 / jnp.sqrt(kept_total)
    blocks = whitened.reshape(NBLK, CH_BLK, windows_all, NF, 2)

    def one_pair(pair_row):
        left_block = blocks[pair_row[0]].astype(jnp.float32)
        right_block = blocks[pair_row[1]].astype(jnp.float32)
        products = jnp.einsum('uwjr,vwjs->jrsuv', left_block, right_block, precision=lax.Precision.HIGHEST)
        real_part = products[:, 0, 0] + products[:, 1, 1]
        imag_part = products[:, 0, 1] - products[:, 1, 0]
        return jnp.stack([real_part, imag_part], axis=1) * stack_scale
    return lax.map(one_pair, pair_blocks)
```

```python
import functools
import math

import jax
import jax.numpy as jnp
from jax import lax
from jax.experimental import pallas as pl
from jax.experimental.pallas import tpu as pltpu
from jax.sharding import PartitionSpec as P

CH_BLK = 128
WIN = 512
NF = 128
FLO = 8


whiten_eps = 1e-06


def from_behind(array, axis, by):
    count = lax.axis_size(axis)
    pairs = [(i, i + by) for i in range(count) if 0 <= i + by < count]
    return lax.ppermute(array, axis, pairs)


def toeplitz(fir_taps):
    length = fir_taps.shape[0]
    reversed_taps = fir_taps[::-1]
    base_column = jnp.concatenate(
        [jnp.zeros((1,), fir_taps.dtype), reversed_taps, jnp.zeros((length,), fir_taps.dtype)]
    )
    flattened = jnp.tile(base_column, length)[: 2 * length * length]
    return flattened.reshape(length, 2 * length).T


def bandpass(recording, fir_taps, tail_rows):
    channels, length = recording.shape
    width = fir_taps.shape[0]
    current = recording.reshape(channels, length // width, width)
    previous = jnp.concatenate([tail_rows[:, None, :], current[:, :-1, :]], axis=1)
    extended = jnp.concatenate([previous, current], axis=2).reshape(
        channels * (length // width), 2 * width
    )
    product = jnp.dot(extended, toeplitz(fir_taps), preferred_element_type=jnp.float32)
    return product.reshape(channels, length).astype(jnp.bfloat16)


def dft_table(length, bins, lowest):
    samples = jnp.arange(length, dtype=jnp.int32)
    indices = lowest + jnp.arange(bins, dtype=jnp.int32)
    phase = (samples[:, None] * indices[None, :] % length).astype(jnp.float32) * (
        2.0 * math.pi / length
    )
    basis_table = jnp.stack([jnp.cos(phase), -jnp.sin(phase)], axis=2)
    return basis_table.reshape(length, 2 * bins).astype(jnp.bfloat16)


def stack_kernel(blocks_per_half, pb_ref, kw_ref, a_ref, b_ref, o_ref):
    sections = kw_ref.shape[0]
    total = kw_ref[0]
    for s in range(1, sections):
        total = total + kw_ref[s]
    scale = 1.0 / jnp.sqrt(jnp.full((1, 1), total, jnp.int32).astype(jnp.float32))
    segs, bins, _, wins, blk = a_ref.shape

    def one_bin(jl, carry):
        left = a_ref[:, jl].reshape(segs * 2 * wins, blk)
        right = b_ref[:, jl]
        swapped = jnp.concatenate([right[:, 1:2], -right[:, 0:1]], axis=1)
        rhs = jnp.concatenate(
            [right.reshape(segs * 2 * wins, blk), swapped.reshape(segs * 2 * wins, blk)], axis=1
        )
        out = lax.dot_general(
            left, rhs, (((0,), (0,)), ((), ())), preferred_element_type=jnp.float32
        )
        o_ref[0, jl, 0] = out[:, :blk] * scale
        o_ref[0, jl, 1] = out[:, blk:] * scale
        return carry

    lax.fori_loop(0, bins, one_bin, 0)


def stack_pairs(gathered, pair_blocks, kept_windows):
    halves, segs, bins, two, wins, chans = gathered.shape
    blocks_per_half = chans // CH_BLK
    npairs = pair_blocks.shape[0]

    def left_map(p, pb, kw):
        a = pb[p, 0]
        return (a // blocks_per_half, 0, 0, 0, 0, a % blocks_per_half)

    def right_map(p, pb, kw):
        b = pb[p, 1]
        return (b // blocks_per_half, 0, 0, 0, 0, b % blocks_per_half)

    block = (None, segs, bins, two, wins, CH_BLK)
    grid_spec = pltpu.PrefetchScalarGridSpec(
        num_scalar_prefetch=2,
        grid=(npairs,),
        in_specs=[pl.BlockSpec(block, left_map), pl.BlockSpec(block, right_map)],
        out_specs=pl.BlockSpec((1, bins, 2, CH_BLK, CH_BLK), lambda p, pb, kw: (p, 0, 0, 0, 0)),
    )
    flops = 2 * npairs * bins * CH_BLK * (2 * CH_BLK) * (segs * two * wins)
    out_bytes = npairs * bins * 2 * CH_BLK * CH_BLK * 4
    in_bytes = 2 * npairs * segs * bins * two * wins * CH_BLK * 2
    return pl.pallas_call(
        functools.partial(stack_kernel, blocks_per_half),
        grid_spec=grid_spec,
        out_shape=jax.ShapeDtypeStruct((npairs, bins, 2, CH_BLK, CH_BLK), jnp.float32),
        compiler_params=pltpu.CompilerParams(
            dimension_semantics=("arbitrary",), vmem_limit_bytes=48 * 1024 * 1024
        ),
        cost_estimate=pl.CostEstimate(
            flops=flops, bytes_accessed=out_bytes + in_bytes, transcendentals=0
        ),
    )(pair_blocks, kept_windows, gathered, gathered)


def per_device(recording, fir_taps, kept_windows, pair_blocks):
    channels, length = recording.shape
    width = fir_taps.shape[0]
    sections = lax.axis_size("tm")
    tail_rows = from_behind(recording[:, length - width :], "tm", 1)
    filtered = bandpass(recording, fir_taps, tail_rows)
    windows_dev = length // WIN
    spectrum = jnp.einsum(
        "cwt,tk->kwc",
        filtered.reshape(channels, windows_dev, WIN),
        dft_table(WIN, NF, FLO),
        preferred_element_type=jnp.float32,
    )
    inverse_rms = lax.rsqrt(jnp.mean(spectrum * spectrum, axis=0, keepdims=True) + whiten_eps)
    segment = lax.axis_index("tm")
    kept_count = lax.dynamic_index_in_dim(kept_windows, segment, 0, keepdims=False)
    window_mask = (jnp.arange(windows_dev, dtype=jnp.int32) < kept_count).astype(jnp.float32)
    whitened = (spectrum * inverse_rms * window_mask[None, :, None]).astype(jnp.bfloat16)
    bins_dev = NF // sections
    outgoing = whitened.reshape(sections, bins_dev, 2, windows_dev, channels)
    by_freq = lax.all_to_all(outgoing, "tm", split_axis=0, concat_axis=0, tiled=True)
    gathered = lax.all_gather(by_freq, "pair", axis=0, tiled=False)
    return stack_pairs(gathered, pair_blocks, kept_windows)


def solution(mesh):
    placed = (P(("groups", "pair"), "tm"), P(), P("groups"), P(("groups", "pair"), None))
    return jax.shard_map(
        per_device,
        mesh=mesh,
        in_specs=placed,
        out_specs=P(("groups", "pair"), "tm", None, None, None),
        check_vma=False,
    )
```

```python
import functools
import math

import jax
import jax.numpy as jnp
from jax import lax
from jax.experimental import pallas as pl
from jax.experimental.pallas import tpu as pltpu
from jax.sharding import PartitionSpec as P

CH_BLK = 128
WIN = 512
NF = 128
FLO = 8


whiten_eps = 1e-06


def from_behind(array, axis, by):
    count = lax.axis_size(axis)
    pairs = [(i, i + by) for i in range(count) if 0 <= i + by < count]
    return lax.ppermute(array, axis, pairs)


def toeplitz(fir_taps):
    length = fir_taps.shape[0]
    reversed_taps = fir_taps[::-1]
    base_column = jnp.concatenate(
        [jnp.zeros((1,), fir_taps.dtype), reversed_taps, jnp.zeros((length,), fir_taps.dtype)]
    )
    flattened = jnp.tile(base_column, length)[: 2 * length * length]
    return flattened.reshape(length, 2 * length).T


def bandpass(recording, fir_taps, tail_rows):
    channels, length = recording.shape
    width = fir_taps.shape[0]
    current = recording.reshape(channels, length // width, width)
    previous = jnp.concatenate([tail_rows[:, None, :], current[:, :-1, :]], axis=1)
    extended = jnp.concatenate([previous, current], axis=2).reshape(
        channels * (length // width), 2 * width
    )
    product = jnp.dot(extended, toeplitz(fir_taps), preferred_element_type=jnp.float32)
    return product.reshape(channels, length).astype(jnp.bfloat16)


def dft_table(length, bins, lowest):
    samples = jnp.arange(length, dtype=jnp.int32)
    indices = lowest + jnp.arange(bins, dtype=jnp.int32)
    phase = (samples[:, None] * indices[None, :] % length).astype(jnp.float32) * (
        2.0 * math.pi / length
    )
    basis_table = jnp.stack([jnp.cos(phase), -jnp.sin(phase)], axis=2)
    return basis_table.reshape(length, 2 * bins).astype(jnp.bfloat16)


def front_kernel(cnt_ref, rec_ref, tail_ref, toep_ref, basis_ref, o_ref, scr_ref, inv_ref):
    tile, length = rec_ref.shape
    width = tail_ref.shape[1]
    bins2 = basis_ref.shape[1]
    windows = length // WIN
    toep = toep_ref[...]
    basis = basis_ref[...]
    count = cnt_ref[0]
    for w in range(windows):
        if w == 0:
            ext0 = jnp.concatenate([tail_ref[...], rec_ref[:, 0:width]], axis=1)
        else:
            ext0 = rec_ref[:, WIN * w - width : WIN * w + width]
        ext1 = rec_ref[:, WIN * w : WIN * w + 2 * width]
        f0 = jnp.dot(ext0, toep, preferred_element_type=jnp.float32).astype(jnp.bfloat16)
        f1 = jnp.dot(ext1, toep, preferred_element_type=jnp.float32).astype(jnp.bfloat16)
        spec = jnp.dot(
            jnp.concatenate([f0, f1], axis=1), basis, preferred_element_type=jnp.float32
        ).T
        for h in range(tile // CH_BLK):
            scr_ref[h, pl.ds(bins2 * w, bins2), :] = spec[:, CH_BLK * h : CH_BLK * (h + 1)]
        power = jnp.sum(spec * spec, axis=0, keepdims=True) * (1.0 / bins2)
        keep = jnp.where(count > w, 1.0, 0.0).astype(jnp.float32)
        inv_ref[pl.ds(w, 1), :] = lax.rsqrt(power + whiten_eps) * keep
    scales = inv_ref[...]

    def one_row(k, carry):
        for h in range(tile // CH_BLK):
            rows = scr_ref[h, pl.ds(k, windows, stride=bins2), :]
            part = rows * scales[:, CH_BLK * h : CH_BLK * (h + 1)]
            o_ref[k, :, CH_BLK * h : CH_BLK * (h + 1)] = part.astype(o_ref.dtype)
        return carry

    lax.fori_loop(0, bins2, one_row, 0)


def whiten_front(recording, tail_rows, fir_taps, kept_count, tile=256):
    channels, length = recording.shape
    width = tail_rows.shape[1]
    windows = length // WIN
    toep = toeplitz(fir_taps)
    basis = dft_table(WIN, NF, FLO)
    bins2 = basis.shape[1]
    grid_spec = pltpu.PrefetchScalarGridSpec(
        num_scalar_prefetch=1,
        grid=(channels // tile,),
        in_specs=[
            pl.BlockSpec((tile, length), lambda i, c: (i, 0)),
            pl.BlockSpec((tile, width), lambda i, c: (i, 0)),
            pl.BlockSpec(toep.shape, lambda i, c: (0, 0)),
            pl.BlockSpec(basis.shape, lambda i, c: (0, 0)),
        ],
        out_specs=pl.BlockSpec((bins2, windows, tile), lambda i, c: (0, 0, i)),
        scratch_shapes=[
            pltpu.VMEM((tile // CH_BLK, windows * bins2, CH_BLK), jnp.float32),
            pltpu.VMEM((windows, tile), jnp.float32),
        ],
    )
    flops = 2 * channels * windows * 3 * (2 * width) * bins2 * 2
    return pl.pallas_call(
        front_kernel,
        grid_spec=grid_spec,
        out_shape=jax.ShapeDtypeStruct((bins2, windows, channels), jnp.bfloat16),
        compiler_params=pltpu.CompilerParams(
            dimension_semantics=("arbitrary",), vmem_limit_bytes=48 * 1024 * 1024
        ),
        cost_estimate=pl.CostEstimate(
            flops=flops,
            bytes_accessed=channels * length * 2 + bins2 * windows * channels * 2,
            transcendentals=channels * windows,
        ),
    )(kept_count, recording, tail_rows, toep, basis)


def stack_kernel(pb_ref, kw_ref, a_ref, b_ref, o_ref):
    sections = kw_ref.shape[0]
    total = kw_ref[0]
    for s in range(1, sections):
        total = total + kw_ref[s]
    scale = 1.0 / jnp.sqrt(jnp.full((1, 1), total, jnp.int32).astype(jnp.float32))
    bins, blk, depth = a_ref.shape
    half = depth // 2

    def one_bin(jl, carry):
        left = a_ref[jl]
        right = b_ref[jl]
        swapped = jnp.concatenate([right[:, half:], -right[:, :half]], axis=1)
        rhs = jnp.concatenate([right, swapped], axis=0)
        out = lax.dot_general(
            left, rhs, (((1,), (1,)), ((), ())), preferred_element_type=jnp.float32
        )
        o_ref[0, jl, 0] = out[:, :blk] * scale
        o_ref[0, jl, 1] = out[:, blk:] * scale
        return carry

    lax.fori_loop(0, bins, one_bin, 0)


def stack_pairs(gathered, pair_blocks, kept_windows):
    halves, bins, chans, depth = gathered.shape
    blocks_per_half = chans // CH_BLK
    npairs = pair_blocks.shape[0]

    def left_map(p, pb, kw):
        a = pb[p, 0]
        return (a // blocks_per_half, 0, a % blocks_per_half, 0)

    def right_map(p, pb, kw):
        b = pb[p, 1]
        return (b // blocks_per_half, 0, b % blocks_per_half, 0)

    block = (None, bins, CH_BLK, depth)
    grid_spec = pltpu.PrefetchScalarGridSpec(
        num_scalar_prefetch=2,
        grid=(npairs,),
        in_specs=[pl.BlockSpec(block, left_map), pl.BlockSpec(block, right_map)],
        out_specs=pl.BlockSpec((1, bins, 2, CH_BLK, CH_BLK), lambda p, pb, kw: (p, 0, 0, 0, 0)),
    )
    flops = 2 * npairs * bins * CH_BLK * (2 * CH_BLK) * depth
    out_bytes = npairs * bins * 2 * CH_BLK * CH_BLK * 4
    in_bytes = 2 * npairs * bins * CH_BLK * depth * 2
    return pl.pallas_call(
        stack_kernel,
        grid_spec=grid_spec,
        out_shape=jax.ShapeDtypeStruct((npairs, bins, 2, CH_BLK, CH_BLK), jnp.float32),
        compiler_params=pltpu.CompilerParams(
            dimension_semantics=("arbitrary",), vmem_limit_bytes=48 * 1024 * 1024
        ),
        cost_estimate=pl.CostEstimate(
            flops=flops, bytes_accessed=out_bytes + in_bytes, transcendentals=0
        ),
    )(pair_blocks, kept_windows, gathered, gathered)


def per_device(recording, fir_taps, kept_windows, pair_blocks):
    channels, length = recording.shape
    width = fir_taps.shape[0]
    sections = lax.axis_size("tm")
    tail_rows = from_behind(recording[:, length - width :], "tm", 1)
    windows_dev = length // WIN
    segment = lax.axis_index("tm")
    kept_count = lax.dynamic_slice_in_dim(kept_windows, segment, 1, 0)
    whitened = whiten_front(recording, tail_rows, fir_taps, kept_count)
    bins_dev = NF // sections
    outgoing = whitened.reshape(sections, bins_dev, 2, windows_dev, channels)
    by_freq = lax.all_to_all(outgoing, "tm", split_axis=0, concat_axis=0, tiled=True)
    by_chan = jnp.transpose(by_freq, (1, 4, 2, 0, 3)).reshape(
        bins_dev, channels, 2 * sections * windows_dev
    )
    gathered = lax.all_gather(by_chan, "pair", axis=0, tiled=False)
    return stack_pairs(gathered, pair_blocks, kept_windows)


def solution(mesh):
    placed = (P(("groups", "pair"), "tm"), P(), P("groups"), P(("groups", "pair"), None))
    return jax.shard_map(
        per_device,
        mesh=mesh,
        in_specs=placed,
        out_specs=P(("groups", "pair"), "tm", None, None, None),
        check_vma=False,
    )
```

```python
import functools
import math

import jax
import jax.numpy as jnp
from jax import lax
from jax.experimental import pallas as pl
from jax.experimental.pallas import tpu as pltpu
from jax.sharding import PartitionSpec as P

CH_BLK = 128
WIN = 512
NF = 128
FLO = 8


whiten_eps = 1e-06


def from_behind(array, axis, by):
    count = lax.axis_size(axis)
    pairs = [(i, i + by) for i in range(count) if 0 <= i + by < count]
    return lax.ppermute(array, axis, pairs)


def exchange(outgoing, axis):
    count = lax.axis_size(axis)
    me = lax.axis_index(axis)
    pieces = [lax.dynamic_index_in_dim(outgoing, me, 0, keepdims=False)]
    for shift in range(1, count):
        piece = lax.dynamic_index_in_dim(outgoing, (me + shift) % count, 0, keepdims=False)
        pairs = [(i, (i + shift) % count) for i in range(count)]
        pieces.append(lax.ppermute(piece, axis, pairs))
    return jnp.stack(pieces)


def toeplitz(fir_taps):
    length = fir_taps.shape[0]
    reversed_taps = fir_taps[::-1]
    base_column = jnp.concatenate(
        [jnp.zeros((1,), fir_taps.dtype), reversed_taps, jnp.zeros((length,), fir_taps.dtype)]
    )
    flattened = jnp.tile(base_column, length)[: 2 * length * length]
    return flattened.reshape(length, 2 * length).T


def bandpass(recording, fir_taps, tail_rows):
    channels, length = recording.shape
    width = fir_taps.shape[0]
    current = recording.reshape(channels, length // width, width)
    previous = jnp.concatenate([tail_rows[:, None, :], current[:, :-1, :]], axis=1)
    extended = jnp.concatenate([previous, current], axis=2).reshape(
        channels * (length // width), 2 * width
    )
    product = jnp.dot(extended, toeplitz(fir_taps), preferred_element_type=jnp.float32)
    return product.reshape(channels, length).astype(jnp.bfloat16)


def dft_table(length, bins, lowest):
    samples = jnp.arange(length, dtype=jnp.int32)
    indices = lowest + jnp.arange(bins, dtype=jnp.int32)
    phase = (samples[:, None] * indices[None, :] % length).astype(jnp.float32) * (
        2.0 * math.pi / length
    )
    basis_table = jnp.stack([jnp.cos(phase), -jnp.sin(phase)], axis=2)
    return basis_table.reshape(length, 2 * bins).astype(jnp.bfloat16)


def front_kernel(cnt_ref, rec_ref, tail_ref, toep_ref, basis_ref, o_ref, scr_ref, inv_ref):
    tile, length = rec_ref.shape
    width = tail_ref.shape[1]
    bins2 = basis_ref.shape[1]
    windows = length // WIN
    toep = toep_ref[...]
    basis = basis_ref[...]
    count = cnt_ref[0]
    for w in range(windows):
        if w == 0:
            ext0 = jnp.concatenate([tail_ref[...], rec_ref[:, 0:width]], axis=1)
        else:
            ext0 = rec_ref[:, WIN * w - width : WIN * w + width]
        ext1 = rec_ref[:, WIN * w : WIN * w + 2 * width]
        f0 = jnp.dot(ext0, toep, preferred_element_type=jnp.float32).astype(jnp.bfloat16)
        f1 = jnp.dot(ext1, toep, preferred_element_type=jnp.float32).astype(jnp.bfloat16)
        spec = jnp.dot(
            jnp.concatenate([f0, f1], axis=1), basis, preferred_element_type=jnp.float32
        ).T
        for h in range(tile // CH_BLK):
            scr_ref[h, pl.ds(bins2 * w, bins2), :] = spec[:, CH_BLK * h : CH_BLK * (h + 1)]
        power = jnp.sum(spec * spec, axis=0, keepdims=True) * (1.0 / bins2)
        keep = jnp.where(count > w, 1.0, 0.0).astype(jnp.float32)
        inv_ref[pl.ds(w, 1), :] = lax.rsqrt(power + whiten_eps) * keep
    scales = inv_ref[...]

    def one_row(k, carry):
        for h in range(tile // CH_BLK):
            rows = scr_ref[h, pl.ds(k, windows, stride=bins2), :]
            part = rows * scales[:, CH_BLK * h : CH_BLK * (h + 1)]
            o_ref[k, :, CH_BLK * h : CH_BLK * (h + 1)] = part.astype(o_ref.dtype)
        return carry

    lax.fori_loop(0, bins2, one_row, 0)


def whiten_front(recording, tail_rows, fir_taps, kept_count, chunks, tile=256):
    channels, length = recording.shape
    width = tail_rows.shape[1]
    windows = length // WIN
    toep = toeplitz(fir_taps)
    sections = lax.axis_size("tm")
    basis = dft_table(WIN, NF, FLO).reshape(WIN, sections, chunks, NF // sections // chunks, 2)
    basis = jnp.transpose(basis, (0, 2, 1, 3, 4)).reshape(WIN, 2 * NF)
    bins2 = basis.shape[1]
    grid_spec = pltpu.PrefetchScalarGridSpec(
        num_scalar_prefetch=1,
        grid=(channels // tile,),
        in_specs=[
            pl.BlockSpec((tile, length), lambda i, c: (i, 0)),
            pl.BlockSpec((tile, width), lambda i, c: (i, 0)),
            pl.BlockSpec(toep.shape, lambda i, c: (0, 0)),
            pl.BlockSpec(basis.shape, lambda i, c: (0, 0)),
        ],
        out_specs=pl.BlockSpec((bins2, windows, tile), lambda i, c: (0, 0, i)),
        scratch_shapes=[
            pltpu.VMEM((tile // CH_BLK, windows * bins2, CH_BLK), jnp.float32),
            pltpu.VMEM((windows, tile), jnp.float32),
        ],
    )
    flops = 2 * channels * windows * 3 * (2 * width) * bins2 * 2
    return pl.pallas_call(
        front_kernel,
        grid_spec=grid_spec,
        out_shape=jax.ShapeDtypeStruct((bins2, windows, channels), jnp.bfloat16),
        compiler_params=pltpu.CompilerParams(
            dimension_semantics=("arbitrary",), vmem_limit_bytes=48 * 1024 * 1024
        ),
        cost_estimate=pl.CostEstimate(
            flops=flops,
            bytes_accessed=channels * length * 2 + bins2 * windows * channels * 2,
            transcendentals=channels * windows,
        ),
    )(kept_count, recording, tail_rows, toep, basis)


def stack_kernel(pb_ref, kw_ref, a_ref, b_ref, *rest):
    o_ref = rest[-1]
    sections = kw_ref.shape[0]
    total = kw_ref[0]
    for s in range(1, sections):
        total = total + kw_ref[s]
    scale = 1.0 / jnp.sqrt(jnp.full((1, 1), total, jnp.int32).astype(jnp.float32))
    segs, bins, _, wins, blk = a_ref.shape

    def one_bin(jl, carry):
        left = a_ref[:, jl].reshape(segs * 2 * wins, blk)
        right = b_ref[:, jl]
        swapped = jnp.concatenate([right[:, 1:2], -right[:, 0:1]], axis=1)
        rhs = jnp.concatenate(
            [right.reshape(segs * 2 * wins, blk), swapped.reshape(segs * 2 * wins, blk)], axis=1
        )
        out = lax.dot_general(
            left, rhs, (((0,), (0,)), ((), ())), preferred_element_type=jnp.float32
        )
        o_ref[0, jl, 0] = out[:, :blk] * scale
        o_ref[0, jl, 1] = out[:, blk:] * scale
        return carry

    lax.fori_loop(0, bins, one_bin, 0)


def stack_pairs(gathered, pair_blocks, kept_windows, chunk, chunks, previous=None):
    halves, segs, bins, two, wins, chans = gathered.shape
    blocks_per_half = chans // CH_BLK
    npairs = pair_blocks.shape[0]

    def left_map(p, pb, kw):
        a = pb[p, 0]
        return (a // blocks_per_half, 0, 0, 0, 0, a % blocks_per_half)

    def right_map(p, pb, kw):
        b = pb[p, 1]
        return (b // blocks_per_half, 0, 0, 0, 0, b % blocks_per_half)

    block = (None, segs, bins, two, wins, CH_BLK)
    in_specs = [pl.BlockSpec(block, left_map), pl.BlockSpec(block, right_map)]
    operands = [pair_blocks, kept_windows, gathered, gathered]
    aliases = {}
    if previous is not None:
        in_specs.append(pl.BlockSpec(memory_space=pl.ANY))
        operands.append(previous)
        aliases = {4: 0}
    grid_spec = pltpu.PrefetchScalarGridSpec(
        num_scalar_prefetch=2,
        grid=(npairs,),
        in_specs=in_specs,
        out_specs=pl.BlockSpec(
            (1, bins, 2, CH_BLK, CH_BLK), lambda p, pb, kw: (p, chunk, 0, 0, 0)
        ),
    )
    flops = 2 * npairs * bins * CH_BLK * (2 * CH_BLK) * (segs * two * wins)
    out_bytes = npairs * bins * 2 * CH_BLK * CH_BLK * 4
    in_bytes = 2 * npairs * segs * bins * two * wins * CH_BLK * 2
    return pl.pallas_call(
        stack_kernel,
        grid_spec=grid_spec,
        out_shape=jax.ShapeDtypeStruct((npairs, bins * chunks, 2, CH_BLK, CH_BLK), jnp.float32),
        input_output_aliases=aliases,
        compiler_params=pltpu.CompilerParams(
            dimension_semantics=("arbitrary",), vmem_limit_bytes=48 * 1024 * 1024
        ),
        cost_estimate=pl.CostEstimate(
            flops=flops, bytes_accessed=out_bytes + in_bytes, transcendentals=0
        ),
    )(*operands)


def per_device(recording, fir_taps, kept_windows, pair_blocks, chunks=2):
    channels, length = recording.shape
    width = fir_taps.shape[0]
    sections = lax.axis_size("tm")
    tail_rows = from_behind(recording[:, length - width :], "tm", 1)
    windows_dev = length // WIN
    segment = lax.axis_index("tm")
    kept_count = lax.dynamic_slice_in_dim(kept_windows, segment, 1, 0)
    bins_dev = NF // sections
    chunks = math.gcd(chunks, bins_dev)
    whitened = whiten_front(recording, tail_rows, fir_taps, kept_count, chunks)
    outgoing = whitened.reshape(chunks, sections, bins_dev // chunks, 2, windows_dev, channels)
    result = None
    for h in range(chunks):
        by_freq = exchange(outgoing[h], "tm")
        gathered = lax.all_gather(by_freq, "pair", axis=0, tiled=False)
        result = stack_pairs(gathered, pair_blocks, kept_windows, h, chunks, result)
    return result


def solution(mesh):
    placed = (P(("groups", "pair"), "tm"), P(), P("groups"), P(("groups", "pair"), None))
    return jax.shard_map(
        per_device,
        mesh=mesh,
        in_specs=placed,
        out_specs=P(("groups", "pair"), "tm", None, None, None),
        check_vma=False,
    )
```

```python
import functools
import math

import jax
import jax.numpy as jnp
from jax import lax
from jax.experimental import pallas as pl
from jax.experimental.pallas import tpu as pltpu
from jax.sharding import PartitionSpec as P

CH_BLK = 128
WIN = 512
NF = 128
FLO = 8


whiten_eps = 1e-06


def from_behind(array, axis, by):
    count = lax.axis_size(axis)
    pairs = [(i, i + by) for i in range(count) if 0 <= i + by < count]
    return lax.ppermute(array, axis, pairs)


def exchange(outgoing, axis):
    count = lax.axis_size(axis)
    me = lax.axis_index(axis)
    pieces = [lax.dynamic_index_in_dim(outgoing, me, 0, keepdims=False)]
    for shift in range(1, count):
        piece = lax.dynamic_index_in_dim(outgoing, (me + shift) % count, 0, keepdims=False)
        pairs = [(i, (i + shift) % count) for i in range(count)]
        pieces.append(lax.ppermute(piece, axis, pairs))
    return jnp.stack(pieces)


def toeplitz(fir_taps):
    length = fir_taps.shape[0]
    reversed_taps = fir_taps[::-1]
    base_column = jnp.concatenate(
        [jnp.zeros((1,), fir_taps.dtype), reversed_taps, jnp.zeros((length,), fir_taps.dtype)]
    )
    flattened = jnp.tile(base_column, length)[: 2 * length * length]
    return flattened.reshape(length, 2 * length).T


def bandpass(recording, fir_taps, tail_rows):
    channels, length = recording.shape
    width = fir_taps.shape[0]
    current = recording.reshape(channels, length // width, width)
    previous = jnp.concatenate([tail_rows[:, None, :], current[:, :-1, :]], axis=1)
    extended = jnp.concatenate([previous, current], axis=2).reshape(
        channels * (length // width), 2 * width
    )
    product = jnp.dot(extended, toeplitz(fir_taps), preferred_element_type=jnp.float32)
    return product.reshape(channels, length).astype(jnp.bfloat16)


def dft_table(length, bins, lowest):
    samples = jnp.arange(length, dtype=jnp.int32)
    indices = lowest + jnp.arange(bins, dtype=jnp.int32)
    phase = (samples[:, None] * indices[None, :] % length).astype(jnp.float32) * (
        2.0 * math.pi / length
    )
    basis_table = jnp.stack([jnp.cos(phase), -jnp.sin(phase)], axis=2)
    return basis_table.reshape(length, 2 * bins).astype(jnp.bfloat16)


def front_kernel(cnt_ref, rec_ref, tail_ref, toep_ref, basis_ref, o_ref, scr_ref, inv_ref):
    tile, length = rec_ref.shape
    width = tail_ref.shape[1]
    bins2 = basis_ref.shape[1]
    windows = length // WIN
    toep = toep_ref[...]
    basis = basis_ref[...]
    count = cnt_ref[0]
    for w in range(windows):
        if w == 0:
            ext0 = jnp.concatenate([tail_ref[...], rec_ref[:, 0:width]], axis=1)
        else:
            ext0 = rec_ref[:, WIN * w - width : WIN * w + width]
        ext1 = rec_ref[:, WIN * w : WIN * w + 2 * width]
        f0 = jnp.dot(ext0, toep, preferred_element_type=jnp.float32).astype(jnp.bfloat16)
        f1 = jnp.dot(ext1, toep, preferred_element_type=jnp.float32).astype(jnp.bfloat16)
        spec = jnp.dot(
            jnp.concatenate([f0, f1], axis=1), basis, preferred_element_type=jnp.float32
        ).T
        for h in range(tile // CH_BLK):
            scr_ref[h, pl.ds(bins2 * w, bins2), :] = spec[:, CH_BLK * h : CH_BLK * (h + 1)]
        power = jnp.sum(spec * spec, axis=0, keepdims=True) * (1.0 / bins2)
        keep = jnp.where(count > w, 1.0, 0.0).astype(jnp.float32)
        inv_ref[pl.ds(w, 1), :] = lax.rsqrt(power + whiten_eps) * keep
    scales = inv_ref[...]

    def one_row(k, carry):
        for h in range(tile // CH_BLK):
            rows = scr_ref[h, pl.ds(k, windows, stride=bins2), :]
            part = rows * scales[:, CH_BLK * h : CH_BLK * (h + 1)]
            o_ref[k, :, CH_BLK * h : CH_BLK * (h + 1)] = part.astype(o_ref.dtype)
        return carry

    lax.fori_loop(0, bins2, one_row, 0)


def whiten_front(recording, tail_rows, fir_taps, kept_count, chunks, tile=256):
    channels, length = recording.shape
    width = tail_rows.shape[1]
    windows = length // WIN
    toep = toeplitz(fir_taps)
    sections = lax.axis_size("tm")
    basis = dft_table(WIN, NF, FLO).reshape(WIN, sections, chunks, NF // sections // chunks, 2)
    basis = jnp.transpose(basis, (0, 2, 1, 3, 4)).reshape(WIN, 2 * NF)
    bins2 = basis.shape[1]
    grid_spec = pltpu.PrefetchScalarGridSpec(
        num_scalar_prefetch=1,
        grid=(channels // tile,),
        in_specs=[
            pl.BlockSpec((tile, length), lambda i, c: (i, 0)),
            pl.BlockSpec((tile, width), lambda i, c: (i, 0)),
            pl.BlockSpec(toep.shape, lambda i, c: (0, 0)),
            pl.BlockSpec(basis.shape, lambda i, c: (0, 0)),
        ],
        out_specs=pl.BlockSpec((bins2, windows, tile), lambda i, c: (0, 0, i)),
        scratch_shapes=[
            pltpu.VMEM((tile // CH_BLK, windows * bins2, CH_BLK), jnp.float32),
            pltpu.VMEM((windows, tile), jnp.float32),
        ],
    )
    flops = 2 * channels * windows * 3 * (2 * width) * bins2 * 2
    return pl.pallas_call(
        front_kernel,
        grid_spec=grid_spec,
        out_shape=jax.ShapeDtypeStruct((bins2, windows, channels), jnp.bfloat16),
        compiler_params=pltpu.CompilerParams(
            dimension_semantics=("arbitrary",), vmem_limit_bytes=48 * 1024 * 1024
        ),
        cost_estimate=pl.CostEstimate(
            flops=flops,
            bytes_accessed=channels * length * 2 + bins2 * windows * channels * 2,
            transcendentals=channels * windows,
        ),
    )(kept_count, recording, tail_rows, toep, basis)


def stack_kernel(pb_ref, kw_ref, q_ref, a_ref, b_ref, *rest):
    o_ref = rest[-1]
    sections = kw_ref.shape[0]
    total = kw_ref[0]
    for s in range(1, sections):
        total = total + kw_ref[s]
    scale = 1.0 / jnp.sqrt(jnp.full((1, 1), total, jnp.int32).astype(jnp.float32))
    segs, bins, _, wins, blk = a_ref.shape

    def one_bin(jl, carry):
        left = a_ref[:, jl].reshape(segs * 2 * wins, blk)
        right = b_ref[:, jl]
        swapped = jnp.concatenate([right[:, 1:2], -right[:, 0:1]], axis=1)
        rhs = jnp.concatenate(
            [right.reshape(segs * 2 * wins, blk), swapped.reshape(segs * 2 * wins, blk)], axis=1
        )
        out = lax.dot_general(
            left, rhs, (((0,), (0,)), ((), ())), preferred_element_type=jnp.float32
        )
        o_ref[0, jl, 0] = out[:, :blk] * scale
        o_ref[0, jl, 1] = out[:, blk:] * scale
        return carry

    lax.fori_loop(0, bins, one_bin, 0, unroll=2)


def stack_pairs(gathered, pair_blocks, kept_windows, half, chunk, chunks, previous=None):
    halves, segs, bins, two, wins, chans = gathered.shape
    blocks_per_half = chans // CH_BLK
    npairs = pair_blocks.shape[0]

    def left_map(p, pb, kw, q):
        a = pb[p, 0]
        return ((a // blocks_per_half + q[0]) % halves, 0, 0, 0, 0, a % blocks_per_half)

    def right_map(p, pb, kw, q):
        b = pb[p, 1]
        return ((b // blocks_per_half + q[0]) % halves, 0, 0, 0, 0, b % blocks_per_half)

    block = (None, segs, bins, two, wins, CH_BLK)
    in_specs = [pl.BlockSpec(block, left_map), pl.BlockSpec(block, right_map)]
    operands = [pair_blocks, kept_windows, half, gathered, gathered]
    aliases = {}
    if previous is not None:
        in_specs.append(pl.BlockSpec(memory_space=pl.ANY))
        operands.append(previous)
        aliases = {5: 0}
    grid_spec = pltpu.PrefetchScalarGridSpec(
        num_scalar_prefetch=3,
        grid=(npairs,),
        in_specs=in_specs,
        out_specs=pl.BlockSpec(
            (1, bins, 2, CH_BLK, CH_BLK), lambda p, pb, kw, q: (p, chunk, 0, 0, 0)
        ),
    )
    flops = 2 * npairs * bins * CH_BLK * (2 * CH_BLK) * (segs * two * wins)
    out_bytes = npairs * bins * 2 * CH_BLK * CH_BLK * 4
    in_bytes = 2 * npairs * segs * bins * two * wins * CH_BLK * 2
    return pl.pallas_call(
        stack_kernel,
        grid_spec=grid_spec,
        out_shape=jax.ShapeDtypeStruct((npairs, bins * chunks, 2, CH_BLK, CH_BLK), jnp.float32),
        input_output_aliases=aliases,
        compiler_params=pltpu.CompilerParams(
            dimension_semantics=("arbitrary",), vmem_limit_bytes=48 * 1024 * 1024
        ),
        cost_estimate=pl.CostEstimate(
            flops=flops, bytes_accessed=out_bytes + in_bytes, transcendentals=0
        ),
    )(*operands)


def per_device(recording, fir_taps, kept_windows, pair_blocks, chunks=2):
    channels, length = recording.shape
    width = fir_taps.shape[0]
    sections = lax.axis_size("tm")
    tail_rows = from_behind(recording[:, length - width :], "tm", 1)
    windows_dev = length // WIN
    segment = lax.axis_index("tm")
    kept_count = lax.dynamic_slice_in_dim(kept_windows, segment, 1, 0)
    bins_dev = NF // sections
    chunks = math.gcd(chunks, bins_dev)
    whitened = whiten_front(recording, tail_rows, fir_taps, kept_count, chunks)
    outgoing = whitened.reshape(chunks, sections, bins_dev // chunks, 2, windows_dev, channels)
    half = jnp.zeros((1,), jnp.int32)
    result = None
    for h in range(chunks):
        by_freq = lax.all_to_all(outgoing[h], "tm", split_axis=0, concat_axis=0, tiled=True)
        gathered = lax.all_gather(by_freq, "pair", axis=0, tiled=False)
        result = stack_pairs(gathered, pair_blocks, kept_windows, half, h, chunks, result)
    return result


def solution(mesh):
    placed = (P(("groups", "pair"), "tm"), P(), P("groups"), P(("groups", "pair"), None))
    return jax.shard_map(
        per_device,
        mesh=mesh,
        in_specs=placed,
        out_specs=P(("groups", "pair"), "tm", None, None, None),
        check_vma=False,
    )
```

```python
import functools
import math

import jax
import jax.numpy as jnp
from jax import lax
from jax.experimental import pallas as pl
from jax.experimental.pallas import tpu as pltpu
from jax.sharding import PartitionSpec as P

CH_BLK = 128
WIN = 512
NF = 128
FLO = 8


whiten_eps = 1e-06


def from_behind(array, axis, by):
    count = lax.axis_size(axis)
    pairs = [(i, i + by) for i in range(count) if 0 <= i + by < count]
    return lax.ppermute(array, axis, pairs)


def exchange(outgoing, axis):
    count = lax.axis_size(axis)
    me = lax.axis_index(axis)
    pieces = [lax.dynamic_index_in_dim(outgoing, me, 0, keepdims=False)]
    for shift in range(1, count):
        piece = lax.dynamic_index_in_dim(outgoing, (me + shift) % count, 0, keepdims=False)
        pairs = [(i, (i + shift) % count) for i in range(count)]
        pieces.append(lax.ppermute(piece, axis, pairs))
    return jnp.stack(pieces)


def toeplitz(fir_taps):
    length = fir_taps.shape[0]
    reversed_taps = fir_taps[::-1]
    base_column = jnp.concatenate(
        [jnp.zeros((1,), fir_taps.dtype), reversed_taps, jnp.zeros((length,), fir_taps.dtype)]
    )
    flattened = jnp.tile(base_column, length)[: 2 * length * length]
    return flattened.reshape(length, 2 * length).T


def bandpass(recording, fir_taps, tail_rows):
    channels, length = recording.shape
    width = fir_taps.shape[0]
    current = recording.reshape(channels, length // width, width)
    previous = jnp.concatenate([tail_rows[:, None, :], current[:, :-1, :]], axis=1)
    extended = jnp.concatenate([previous, current], axis=2).reshape(
        channels * (length // width), 2 * width
    )
    product = jnp.dot(extended, toeplitz(fir_taps), preferred_element_type=jnp.float32)
    return product.reshape(channels, length).astype(jnp.bfloat16)


def dft_table(length, bins, lowest):
    samples = jnp.arange(length, dtype=jnp.int32)
    indices = lowest + jnp.arange(bins, dtype=jnp.int32)
    phase = (samples[:, None] * indices[None, :] % length).astype(jnp.float32) * (
        2.0 * math.pi / length
    )
    basis_table = jnp.stack([jnp.cos(phase), -jnp.sin(phase)], axis=2)
    return basis_table.reshape(length, 2 * bins).astype(jnp.bfloat16)


def front_kernel(cnt_ref, rec_ref, tail_ref, toep_ref, basis_ref, o_ref, scr_ref, inv_ref):
    tile, length = rec_ref.shape
    width = tail_ref.shape[1]
    bins2 = basis_ref.shape[1]
    windows = length // WIN
    toep = toep_ref[...]
    basis = basis_ref[...]
    count = cnt_ref[0]
    pair = 2
    for w0 in range(0, windows, pair):
        exts = []
        for w in range(w0, w0 + pair):
            if w == 0:
                exts.append(jnp.concatenate([tail_ref[...], rec_ref[:, 0:width]], axis=1))
            else:
                exts.append(rec_ref[:, WIN * w - width : WIN * w + width])
            exts.append(rec_ref[:, WIN * w : WIN * w + 2 * width])
        filt = jnp.dot(
            jnp.concatenate(exts, axis=0), toep, preferred_element_type=jnp.float32
        ).astype(jnp.bfloat16)
        frames = [
            jnp.concatenate(
                [filt[2 * i * tile : (2 * i + 1) * tile], filt[(2 * i + 1) * tile : (2 * i + 2) * tile]],
                axis=1,
            )
            for i in range(pair)
        ]
        specs = jnp.dot(jnp.concatenate(frames, axis=0), basis, preferred_element_type=jnp.float32)
        for i in range(pair):
            w = w0 + i
            spec = specs[i * tile : (i + 1) * tile].T
            for h in range(tile // CH_BLK):
                scr_ref[h, pl.ds(bins2 * w, bins2), :] = spec[:, CH_BLK * h : CH_BLK * (h + 1)]
            power = jnp.sum(spec * spec, axis=0, keepdims=True) * (1.0 / bins2)
            keep = jnp.where(count > w, 1.0, 0.0).astype(jnp.float32)
            inv_ref[pl.ds(w, 1), :] = lax.rsqrt(power + whiten_eps) * keep
    scales = inv_ref[...]

    def one_row(k, carry):
        for h in range(tile // CH_BLK):
            rows = scr_ref[h, pl.ds(k, windows, stride=bins2), :]
            part = rows * scales[:, CH_BLK * h : CH_BLK * (h + 1)]
            o_ref[k, :, CH_BLK * h : CH_BLK * (h + 1)] = part.astype(o_ref.dtype)
        return carry

    lax.fori_loop(0, bins2, one_row, 0)


def whiten_front(recording, tail_rows, fir_taps, kept_count, chunks, tile=256):
    channels, length = recording.shape
    width = tail_rows.shape[1]
    windows = length // WIN
    toep = toeplitz(fir_taps)
    sections = lax.axis_size("tm")
    basis = dft_table(WIN, NF, FLO).reshape(WIN, sections, chunks, NF // sections // chunks, 2)
    basis = jnp.transpose(basis, (0, 2, 1, 3, 4)).reshape(WIN, 2 * NF)
    bins2 = basis.shape[1]
    grid_spec = pltpu.PrefetchScalarGridSpec(
        num_scalar_prefetch=1,
        grid=(channels // tile,),
        in_specs=[
            pl.BlockSpec((tile, length), lambda i, c: (i, 0)),
            pl.BlockSpec((tile, width), lambda i, c: (i, 0)),
            pl.BlockSpec(toep.shape, lambda i, c: (0, 0)),
            pl.BlockSpec(basis.shape, lambda i, c: (0, 0)),
        ],
        out_specs=pl.BlockSpec((bins2, windows, tile), lambda i, c: (0, 0, i)),
        scratch_shapes=[
            pltpu.VMEM((tile // CH_BLK, windows * bins2, CH_BLK), jnp.float32),
            pltpu.VMEM((windows, tile), jnp.float32),
        ],
    )
    flops = 2 * channels * windows * 3 * (2 * width) * bins2 * 2
    return pl.pallas_call(
        front_kernel,
        grid_spec=grid_spec,
        out_shape=jax.ShapeDtypeStruct((bins2, windows, channels), jnp.bfloat16),
        compiler_params=pltpu.CompilerParams(
            dimension_semantics=("arbitrary",), vmem_limit_bytes=48 * 1024 * 1024
        ),
        cost_estimate=pl.CostEstimate(
            flops=flops,
            bytes_accessed=channels * length * 2 + bins2 * windows * channels * 2,
            transcendentals=channels * windows,
        ),
    )(kept_count, recording, tail_rows, toep, basis)


def stack_kernel(pb_ref, kw_ref, q_ref, a_ref, b_ref, *rest):
    o_ref = rest[-1]
    sections = kw_ref.shape[0]
    total = kw_ref[0]
    for s in range(1, sections):
        total = total + kw_ref[s]
    scale = 1.0 / jnp.sqrt(jnp.full((1, 1), total, jnp.int32).astype(jnp.float32))
    segs, bins, _, wins, blk = a_ref.shape

    def one_bin(jl, carry):
        left = a_ref[:, jl].reshape(segs * 2 * wins, blk)
        right = b_ref[:, jl]
        swapped = jnp.concatenate([right[:, 1:2], -right[:, 0:1]], axis=1)
        rhs = jnp.concatenate(
            [right.reshape(segs * 2 * wins, blk), swapped.reshape(segs * 2 * wins, blk)], axis=1
        )
        out = lax.dot_general(
            left, rhs, (((0,), (0,)), ((), ())), preferred_element_type=jnp.float32
        )
        o_ref[0, jl, 0] = out[:, :blk] * scale
        o_ref[0, jl, 1] = out[:, blk:] * scale
        return carry

    lax.fori_loop(0, bins, one_bin, 0, unroll=True)


def stack_pairs(gathered, pair_blocks, kept_windows, half, chunk, chunks, previous=None):
    halves, segs, bins, two, wins, chans = gathered.shape
    blocks_per_half = chans // CH_BLK
    npairs = pair_blocks.shape[0]

    def left_map(p, pb, kw, q):
        a = pb[p, 0]
        return ((a // blocks_per_half + q[0]) % halves, 0, 0, 0, 0, a % blocks_per_half)

    def right_map(p, pb, kw, q):
        b = pb[p, 1]
        return ((b // blocks_per_half + q[0]) % halves, 0, 0, 0, 0, b % blocks_per_half)

    block = (None, segs, bins, two, wins, CH_BLK)
    in_specs = [pl.BlockSpec(block, left_map), pl.BlockSpec(block, right_map)]
    operands = [pair_blocks, kept_windows, half, gathered, gathered]
    aliases = {}
    if previous is not None:
        in_specs.append(pl.BlockSpec(memory_space=pl.ANY))
        operands.append(previous)
        aliases = {5: 0}
    grid_spec = pltpu.PrefetchScalarGridSpec(
        num_scalar_prefetch=3,
        grid=(npairs,),
        in_specs=in_specs,
        out_specs=pl.BlockSpec(
            (1, bins, 2, CH_BLK, CH_BLK), lambda p, pb, kw, q: (p, chunk, 0, 0, 0)
        ),
    )
    flops = 2 * npairs * bins * CH_BLK * (2 * CH_BLK) * (segs * two * wins)
    out_bytes = npairs * bins * 2 * CH_BLK * CH_BLK * 4
    in_bytes = 2 * npairs * segs * bins * two * wins * CH_BLK * 2
    return pl.pallas_call(
        stack_kernel,
        grid_spec=grid_spec,
        out_shape=jax.ShapeDtypeStruct((npairs, bins * chunks, 2, CH_BLK, CH_BLK), jnp.float32),
        input_output_aliases=aliases,
        compiler_params=pltpu.CompilerParams(
            dimension_semantics=("arbitrary",), vmem_limit_bytes=48 * 1024 * 1024
        ),
        cost_estimate=pl.CostEstimate(
            flops=flops, bytes_accessed=out_bytes + in_bytes, transcendentals=0
        ),
    )(*operands)


def per_device(recording, fir_taps, kept_windows, pair_blocks, chunks=2):
    channels, length = recording.shape
    width = fir_taps.shape[0]
    sections = lax.axis_size("tm")
    tail_rows = from_behind(recording[:, length - width :], "tm", 1)
    windows_dev = length // WIN
    segment = lax.axis_index("tm")
    kept_count = lax.dynamic_slice_in_dim(kept_windows, segment, 1, 0)
    bins_dev = NF // sections
    chunks = math.gcd(chunks, bins_dev)
    whitened = whiten_front(recording, tail_rows, fir_taps, kept_count, chunks)
    outgoing = whitened.reshape(chunks, sections, bins_dev // chunks, 2, windows_dev, channels)
    half = jnp.zeros((1,), jnp.int32)
    result = None
    for h in range(chunks):
        by_freq = lax.all_to_all(outgoing[h], "tm", split_axis=0, concat_axis=0, tiled=True)
        gathered = lax.all_gather(by_freq, "pair", axis=0, tiled=False)
        result = stack_pairs(gathered, pair_blocks, kept_windows, half, h, chunks, result)
    return result


def solution(mesh):
    placed = (P(("groups", "pair"), "tm"), P(), P("groups"), P(("groups", "pair"), None))
    return jax.shard_map(
        per_device,
        mesh=mesh,
        in_specs=placed,
        out_specs=P(("groups", "pair"), "tm", None, None, None),
        check_vma=False,
    )
```

```python
import functools
import math

import jax
import jax.numpy as jnp
from jax import lax
from jax.experimental import pallas as pl
from jax.experimental.pallas import tpu as pltpu
from jax.sharding import PartitionSpec as P

CH_BLK = 128
WIN = 512
NF = 128
FLO = 8


whiten_eps = 1e-06


def from_behind(array, axis, by):
    count = lax.axis_size(axis)
    pairs = [(i, i + by) for i in range(count) if 0 <= i + by < count]
    return lax.ppermute(array, axis, pairs)


def exchange(outgoing, axis):
    count = lax.axis_size(axis)
    me = lax.axis_index(axis)
    pieces = [lax.dynamic_index_in_dim(outgoing, me, 0, keepdims=False)]
    for shift in range(1, count):
        piece = lax.dynamic_index_in_dim(outgoing, (me + shift) % count, 0, keepdims=False)
        pairs = [(i, (i + shift) % count) for i in range(count)]
        pieces.append(lax.ppermute(piece, axis, pairs))
    return jnp.stack(pieces)


def toeplitz(fir_taps):
    length = fir_taps.shape[0]
    reversed_taps = fir_taps[::-1]
    base_column = jnp.concatenate(
        [jnp.zeros((1,), fir_taps.dtype), reversed_taps, jnp.zeros((length,), fir_taps.dtype)]
    )
    flattened = jnp.tile(base_column, length)[: 2 * length * length]
    return flattened.reshape(length, 2 * length).T


def bandpass(recording, fir_taps, tail_rows):
    channels, length = recording.shape
    width = fir_taps.shape[0]
    current = recording.reshape(channels, length // width, width)
    previous = jnp.concatenate([tail_rows[:, None, :], current[:, :-1, :]], axis=1)
    extended = jnp.concatenate([previous, current], axis=2).reshape(
        channels * (length // width), 2 * width
    )
    product = jnp.dot(extended, toeplitz(fir_taps), preferred_element_type=jnp.float32)
    return product.reshape(channels, length).astype(jnp.bfloat16)


def dft_table(length, bins, lowest):
    samples = jnp.arange(length, dtype=jnp.int32)
    indices = lowest + jnp.arange(bins, dtype=jnp.int32)
    phase = (samples[:, None] * indices[None, :] % length).astype(jnp.float32) * (
        2.0 * math.pi / length
    )
    basis_table = jnp.stack([jnp.cos(phase), -jnp.sin(phase)], axis=2)
    return basis_table.reshape(length, 2 * bins).astype(jnp.bfloat16)


def front_kernel(cnt_ref, rec_ref, tail_ref, toep_ref, basis_ref, o_ref, scr_ref, inv_ref):
    tile, length = rec_ref.shape
    width = tail_ref.shape[1]
    bins2 = basis_ref.shape[1]
    windows = length // WIN
    toep = toep_ref[...]
    basis = basis_ref[...]
    count = cnt_ref[0]
    for w in range(windows):
        if w == 0:
            ext0 = jnp.concatenate([tail_ref[...], rec_ref[:, 0:width]], axis=1)
        else:
            ext0 = rec_ref[:, WIN * w - width : WIN * w + width]
        ext1 = rec_ref[:, WIN * w : WIN * w + 2 * width]
        f0 = jnp.dot(ext0, toep, preferred_element_type=jnp.float32).astype(jnp.bfloat16)
        f1 = jnp.dot(ext1, toep, preferred_element_type=jnp.float32).astype(jnp.bfloat16)
        spec = jnp.dot(
            jnp.concatenate([f0, f1], axis=1), basis, preferred_element_type=jnp.float32
        ).T
        for h in range(tile // CH_BLK):
            scr_ref[h, pl.ds(bins2 * w, bins2), :] = spec[:, CH_BLK * h : CH_BLK * (h + 1)]
        power = jnp.sum(spec * spec, axis=0, keepdims=True) * (1.0 / bins2)
        keep = jnp.where(count > w, 1.0, 0.0).astype(jnp.float32)
        inv_ref[pl.ds(w, 1), :] = lax.rsqrt(power + whiten_eps) * keep
    scales = inv_ref[...]

    def one_row(k, carry):
        for h in range(tile // CH_BLK):
            rows = scr_ref[h, pl.ds(k, windows, stride=bins2), :]
            part = rows * scales[:, CH_BLK * h : CH_BLK * (h + 1)]
            o_ref[k, :, CH_BLK * h : CH_BLK * (h + 1)] = part.astype(o_ref.dtype)
        return carry

    lax.fori_loop(0, bins2, one_row, 0)


def whiten_front(recording, tail_rows, fir_taps, kept_count, chunks, tile=512):
    channels, length = recording.shape
    width = tail_rows.shape[1]
    windows = length // WIN
    toep = toeplitz(fir_taps)
    sections = lax.axis_size("tm")
    basis = dft_table(WIN, NF, FLO).reshape(WIN, sections, chunks, NF // sections // chunks, 2)
    basis = jnp.transpose(basis, (0, 2, 1, 3, 4)).reshape(WIN, 2 * NF)
    bins2 = basis.shape[1]
    grid_spec = pltpu.PrefetchScalarGridSpec(
        num_scalar_prefetch=1,
        grid=(channels // tile,),
        in_specs=[
            pl.BlockSpec((tile, length), lambda i, c: (i, 0)),
            pl.BlockSpec((tile, width), lambda i, c: (i, 0)),
            pl.BlockSpec(toep.shape, lambda i, c: (0, 0)),
            pl.BlockSpec(basis.shape, lambda i, c: (0, 0)),
        ],
        out_specs=pl.BlockSpec((bins2, windows, tile), lambda i, c: (0, 0, i)),
        scratch_shapes=[
            pltpu.VMEM((tile // CH_BLK, windows * bins2, CH_BLK), jnp.float32),
            pltpu.VMEM((windows, tile), jnp.float32),
        ],
    )
    flops = 2 * channels * windows * 3 * (2 * width) * bins2 * 2
    return pl.pallas_call(
        front_kernel,
        grid_spec=grid_spec,
        out_shape=jax.ShapeDtypeStruct((bins2, windows, channels), jnp.bfloat16),
        compiler_params=pltpu.CompilerParams(
            dimension_semantics=("arbitrary",), vmem_limit_bytes=48 * 1024 * 1024
        ),
        cost_estimate=pl.CostEstimate(
            flops=flops,
            bytes_accessed=channels * length * 2 + bins2 * windows * channels * 2,
            transcendentals=channels * windows,
        ),
    )(kept_count, recording, tail_rows, toep, basis)


def stack_kernel(pb_ref, kw_ref, q_ref, a_ref, b_ref, *rest):
    o_ref = rest[-1]
    sections = kw_ref.shape[0]
    total = kw_ref[0]
    for s in range(1, sections):
        total = total + kw_ref[s]
    scale = 1.0 / jnp.sqrt(jnp.full((1, 1), total, jnp.int32).astype(jnp.float32))
    segs, bins, _, wins, blk = a_ref.shape

    def one_bin(jl, carry):
        left = a_ref[:, jl].reshape(segs * 2 * wins, blk)
        right = b_ref[:, jl]
        swapped = jnp.concatenate([right[:, 1:2], -right[:, 0:1]], axis=1)
        rhs = jnp.concatenate(
            [right.reshape(segs * 2 * wins, blk), swapped.reshape(segs * 2 * wins, blk)], axis=1
        )
        out = lax.dot_general(
            left, rhs, (((0,), (0,)), ((), ())), preferred_element_type=jnp.float32
        )
        o_ref[0, jl, 0] = out[:, :blk] * scale
        o_ref[0, jl, 1] = out[:, blk:] * scale
        return carry

    lax.fori_loop(0, bins, one_bin, 0, unroll=True)


def stack_pairs(gathered, pair_blocks, kept_windows, half, chunk, chunks, previous=None):
    halves, segs, bins, two, wins, chans = gathered.shape
    blocks_per_half = chans // CH_BLK
    npairs = pair_blocks.shape[0]

    def left_map(p, pb, kw, q):
        a = pb[p, 0]
        return ((a // blocks_per_half + q[0]) % halves, 0, 0, 0, 0, a % blocks_per_half)

    def right_map(p, pb, kw, q):
        b = pb[p, 1]
        return ((b // blocks_per_half + q[0]) % halves, 0, 0, 0, 0, b % blocks_per_half)

    block = (None, segs, bins, two, wins, CH_BLK)
    in_specs = [pl.BlockSpec(block, left_map), pl.BlockSpec(block, right_map)]
    operands = [pair_blocks, kept_windows, half, gathered, gathered]
    aliases = {}
    if previous is not None:
        in_specs.append(pl.BlockSpec(memory_space=pl.ANY))
        operands.append(previous)
        aliases = {5: 0}
    grid_spec = pltpu.PrefetchScalarGridSpec(
        num_scalar_prefetch=3,
        grid=(npairs,),
        in_specs=in_specs,
        out_specs=pl.BlockSpec(
            (1, bins, 2, CH_BLK, CH_BLK), lambda p, pb, kw, q: (p, chunk, 0, 0, 0)
        ),
    )
    flops = 2 * npairs * bins * CH_BLK * (2 * CH_BLK) * (segs * two * wins)
    out_bytes = npairs * bins * 2 * CH_BLK * CH_BLK * 4
    in_bytes = 2 * npairs * segs * bins * two * wins * CH_BLK * 2
    return pl.pallas_call(
        stack_kernel,
        grid_spec=grid_spec,
        out_shape=jax.ShapeDtypeStruct((npairs, bins * chunks, 2, CH_BLK, CH_BLK), jnp.float32),
        input_output_aliases=aliases,
        compiler_params=pltpu.CompilerParams(
            dimension_semantics=("arbitrary",), vmem_limit_bytes=48 * 1024 * 1024
        ),
        cost_estimate=pl.CostEstimate(
            flops=flops, bytes_accessed=out_bytes + in_bytes, transcendentals=0
        ),
    )(*operands)


def per_device(recording, fir_taps, kept_windows, pair_blocks, chunks=2):
    channels, length = recording.shape
    width = fir_taps.shape[0]
    sections = lax.axis_size("tm")
    tail_rows = from_behind(recording[:, length - width :], "tm", 1)
    windows_dev = length // WIN
    segment = lax.axis_index("tm")
    kept_count = lax.dynamic_slice_in_dim(kept_windows, segment, 1, 0)
    bins_dev = NF // sections
    chunks = math.gcd(chunks, bins_dev)
    whitened = whiten_front(recording, tail_rows, fir_taps, kept_count, chunks)
    outgoing = whitened.reshape(chunks, sections, bins_dev // chunks, 2, windows_dev, channels)
    half = jnp.zeros((1,), jnp.int32)
    result = None
    for h in range(chunks):
        by_freq = lax.all_to_all(outgoing[h], "tm", split_axis=0, concat_axis=0, tiled=True)
        gathered = lax.all_gather(by_freq, "pair", axis=0, tiled=False)
        result = stack_pairs(gathered, pair_blocks, kept_windows, half, h, chunks, result)
    return result


def solution(mesh):
    placed = (P(("groups", "pair"), "tm"), P(), P("groups"), P(("groups", "pair"), None))
    return jax.shard_map(
        per_device,
        mesh=mesh,
        in_specs=placed,
        out_specs=P(("groups", "pair"), "tm", None, None, None),
        check_vma=False,
    )
```

```python
import functools
import math

import jax
import jax.numpy as jnp
import ml_dtypes
import numpy as np
from jax import lax
from jax.experimental import pallas as pl
from jax.experimental.pallas import tpu as pltpu
from jax.sharding import PartitionSpec as P

CH_BLK = 128
WIN = 512
NF = 128
FLO = 8


whiten_eps = 1e-06


def from_behind(array, axis, by):
    count = lax.axis_size(axis)
    pairs = [(i, i + by) for i in range(count) if 0 <= i + by < count]
    return lax.ppermute(array, axis, pairs)


def exchange(outgoing, axis):
    count = lax.axis_size(axis)
    me = lax.axis_index(axis)
    pieces = [lax.dynamic_index_in_dim(outgoing, me, 0, keepdims=False)]
    for shift in range(1, count):
        piece = lax.dynamic_index_in_dim(outgoing, (me + shift) % count, 0, keepdims=False)
        pairs = [(i, (i + shift) % count) for i in range(count)]
        pieces.append(lax.ppermute(piece, axis, pairs))
    return jnp.stack(pieces)


def toeplitz(fir_taps):
    length = fir_taps.shape[0]
    reversed_taps = fir_taps[::-1]
    base_column = jnp.concatenate(
        [jnp.zeros((1,), fir_taps.dtype), reversed_taps, jnp.zeros((length,), fir_taps.dtype)]
    )
    flattened = jnp.tile(base_column, length)[: 2 * length * length]
    return flattened.reshape(length, 2 * length).T


def bandpass(recording, fir_taps, tail_rows):
    channels, length = recording.shape
    width = fir_taps.shape[0]
    current = recording.reshape(channels, length // width, width)
    previous = jnp.concatenate([tail_rows[:, None, :], current[:, :-1, :]], axis=1)
    extended = jnp.concatenate([previous, current], axis=2).reshape(
        channels * (length // width), 2 * width
    )
    product = jnp.dot(extended, toeplitz(fir_taps), preferred_element_type=jnp.float32)
    return product.reshape(channels, length).astype(jnp.bfloat16)


def dft_table(length, bins, lowest):
    samples = np.arange(length, dtype=np.int64)
    indices = lowest + np.arange(bins, dtype=np.int64)
    phase = (samples[:, None] * indices[None, :] % length).astype(np.float64) * (
        2.0 * math.pi / length
    )
    basis_table = np.stack([np.cos(phase), -np.sin(phase)], axis=2)
    return basis_table.reshape(length, 2 * bins).astype(ml_dtypes.bfloat16)


def front_kernel(cnt_ref, rec_ref, tail_ref, toep_ref, basis_ref, *rest):
    outs, (scr_ref, inv_ref) = rest[:-2], rest[-2:]
    tile, length = rec_ref.shape
    width = tail_ref.shape[1]
    bins2 = basis_ref.shape[1]
    windows = length // WIN
    toep = toep_ref[...]
    basis = basis_ref[...]
    count = cnt_ref[0]
    for w in range(windows):
        if w == 0:
            ext0 = jnp.concatenate([tail_ref[...], rec_ref[:, 0:width]], axis=1)
        else:
            ext0 = rec_ref[:, WIN * w - width : WIN * w + width]
        ext1 = rec_ref[:, WIN * w : WIN * w + 2 * width]
        f0 = jnp.dot(ext0, toep, preferred_element_type=jnp.float32).astype(jnp.bfloat16)
        f1 = jnp.dot(ext1, toep, preferred_element_type=jnp.float32).astype(jnp.bfloat16)
        spec = jnp.dot(
            jnp.concatenate([f0, f1], axis=1), basis, preferred_element_type=jnp.float32
        ).T
        for h in range(tile // CH_BLK):
            scr_ref[h, pl.ds(bins2 * w, bins2), :] = spec[:, CH_BLK * h : CH_BLK * (h + 1)]
        power = jnp.sum(spec * spec, axis=0, keepdims=True) * (1.0 / bins2)
        keep = jnp.where(count > w, 1.0, 0.0).astype(jnp.float32)
        inv_ref[pl.ds(w, 1), :] = lax.rsqrt(power + whiten_eps) * keep
    scales = inv_ref[...]

    start = 0
    for o_ref in outs:

        def one_row(k, carry, o_ref=o_ref, start=start):
            for h in range(tile // CH_BLK):
                rows = scr_ref[h, pl.ds(start + k, windows, stride=bins2), :]
                part = rows * scales[:, CH_BLK * h : CH_BLK * (h + 1)]
                o_ref[k, :, CH_BLK * h : CH_BLK * (h + 1)] = part.astype(o_ref.dtype)
            return carry

        lax.fori_loop(0, o_ref.shape[0], one_row, 0)
        start += o_ref.shape[0]


def whiten_front(recording, tail_rows, fir_taps, kept_count, chunks, tile=512):
    channels, length = recording.shape
    width = tail_rows.shape[1]
    windows = length // WIN
    toep = toeplitz(fir_taps)
    sections = lax.axis_size("tm")
    bins_dev = NF // sections
    basis = dft_table(WIN, NF, FLO).reshape(WIN, sections, bins_dev, 2)
    basis = np.concatenate(
        [basis[:, :, lo:hi].reshape(WIN, -1) for lo, hi in zip(chunks[:-1], chunks[1:])], axis=1
    )
    basis = jnp.asarray(basis)
    bins2 = basis.shape[1]
    rows = [sections * (hi - lo) * 2 for lo, hi in zip(chunks[:-1], chunks[1:])]
    grid_spec = pltpu.PrefetchScalarGridSpec(
        num_scalar_prefetch=1,
        grid=(channels // tile,),
        in_specs=[
            pl.BlockSpec((tile, length), lambda i, c: (i, 0)),
            pl.BlockSpec((tile, width), lambda i, c: (i, 0)),
            pl.BlockSpec(toep.shape, lambda i, c: (0, 0)),
            pl.BlockSpec(basis.shape, lambda i, c: (0, 0)),
        ],
        out_specs=[pl.BlockSpec((r, windows, tile), lambda i, c: (0, 0, i)) for r in rows],
        scratch_shapes=[
            pltpu.VMEM((tile // CH_BLK, windows * bins2, CH_BLK), jnp.float32),
            pltpu.VMEM((windows, tile), jnp.float32),
        ],
    )
    flops = 2 * channels * windows * 3 * (2 * width) * bins2 * 2
    return pl.pallas_call(
        front_kernel,
        grid_spec=grid_spec,
        out_shape=[jax.ShapeDtypeStruct((r, windows, channels), jnp.bfloat16) for r in rows],
        compiler_params=pltpu.CompilerParams(
            dimension_semantics=("arbitrary",), vmem_limit_bytes=48 * 1024 * 1024
        ),
        cost_estimate=pl.CostEstimate(
            flops=flops,
            bytes_accessed=channels * length * 2 + bins2 * windows * channels * 2,
            transcendentals=channels * windows,
        ),
    )(kept_count, recording, tail_rows, toep, basis)


def stack_kernel(pb_ref, kw_ref, q_ref, a_ref, b_ref, *rest):
    o_ref = rest[-1]
    sections = kw_ref.shape[0]
    total = kw_ref[0]
    for s in range(1, sections):
        total = total + kw_ref[s]
    scale = 1.0 / jnp.sqrt(jnp.full((1, 1), total, jnp.int32).astype(jnp.float32))
    segs, bins, _, wins, blk = a_ref.shape

    def one_bin(jl, carry):
        left = a_ref[:, jl].reshape(segs * 2 * wins, blk)
        right = b_ref[:, jl]
        swapped = jnp.concatenate([right[:, 1:2], -right[:, 0:1]], axis=1)
        rhs = jnp.concatenate(
            [right.reshape(segs * 2 * wins, blk), swapped.reshape(segs * 2 * wins, blk)], axis=1
        )
        out = lax.dot_general(
            left, rhs, (((0,), (0,)), ((), ())), preferred_element_type=jnp.float32
        )
        o_ref[0, jl, 0] = out[:, :blk] * scale
        o_ref[0, jl, 1] = out[:, blk:] * scale
        return carry

    lax.fori_loop(0, bins, one_bin, 0, unroll=True)


def stack_pairs(gathered, pair_blocks, kept_windows, half, chunk, all_bins, previous=None):
    halves, segs, bins, two, wins, chans = gathered.shape
    blocks_per_half = chans // CH_BLK
    npairs = pair_blocks.shape[0]

    def left_map(p, pb, kw, q):
        a = pb[p, 0]
        return ((a // blocks_per_half + q[0]) % halves, 0, 0, 0, 0, a % blocks_per_half)

    def right_map(p, pb, kw, q):
        b = pb[p, 1]
        return ((b // blocks_per_half + q[0]) % halves, 0, 0, 0, 0, b % blocks_per_half)

    block = (None, segs, bins, two, wins, CH_BLK)
    in_specs = [pl.BlockSpec(block, left_map), pl.BlockSpec(block, right_map)]
    operands = [pair_blocks, kept_windows, half, gathered, gathered]
    aliases = {}
    if previous is not None:
        in_specs.append(pl.BlockSpec(memory_space=pl.ANY))
        operands.append(previous)
        aliases = {5: 0}
    grid_spec = pltpu.PrefetchScalarGridSpec(
        num_scalar_prefetch=3,
        grid=(npairs,),
        in_specs=in_specs,
        out_specs=pl.BlockSpec(
            (1, bins, 2, CH_BLK, CH_BLK), lambda p, pb, kw, q: (p, chunk, 0, 0, 0)
        ),
    )
    flops = 2 * npairs * bins * CH_BLK * (2 * CH_BLK) * (segs * two * wins)
    out_bytes = npairs * bins * 2 * CH_BLK * CH_BLK * 4
    in_bytes = 2 * npairs * segs * bins * two * wins * CH_BLK * 2
    return pl.pallas_call(
        stack_kernel,
        grid_spec=grid_spec,
        out_shape=jax.ShapeDtypeStruct((npairs, all_bins, 2, CH_BLK, CH_BLK), jnp.float32),
        input_output_aliases=aliases,
        compiler_params=pltpu.CompilerParams(
            dimension_semantics=("arbitrary",), vmem_limit_bytes=48 * 1024 * 1024
        ),
        cost_estimate=pl.CostEstimate(
            flops=flops, bytes_accessed=out_bytes + in_bytes, transcendentals=0
        ),
    )(*operands)


def per_device(recording, fir_taps, kept_windows, pair_blocks):
    channels, length = recording.shape
    width = fir_taps.shape[0]
    sections = lax.axis_size("tm")
    tail_rows = from_behind(recording[:, length - width :], "tm", 1)
    windows_dev = length // WIN
    segment = lax.axis_index("tm")
    kept_count = lax.dynamic_slice_in_dim(kept_windows, segment, 1, 0)
    bins_dev = NF // sections
    small = max(bins_dev // 4, 1)
    chunks = [0, bins_dev - small, bins_dev] if bins_dev > 1 else [0, bins_dev]
    whitened = whiten_front(recording, tail_rows, fir_taps, kept_count, chunks)
    half = jnp.zeros((1,), jnp.int32)
    result = None
    for lo, hi, part in zip(chunks[:-1], chunks[1:], whitened):
        outgoing = part.reshape(sections, hi - lo, 2, windows_dev, channels)
        by_freq = lax.all_to_all(outgoing, "tm", split_axis=0, concat_axis=0, tiled=True)
        gathered = lax.all_gather(by_freq, "pair", axis=0, tiled=False)
        result = stack_pairs(
            gathered, pair_blocks, kept_windows, half, lo // (hi - lo), bins_dev, result
        )
    return result


def solution(mesh):
    placed = (P(("groups", "pair"), "tm"), P(), P("groups"), P(("groups", "pair"), None))
    return jax.shard_map(
        per_device,
        mesh=mesh,
        in_specs=placed,
        out_specs=P(("groups", "pair"), "tm", None, None, None),
        check_vma=False,
    )
```

```python
import functools
import math

import jax
import jax.numpy as jnp
import ml_dtypes
import numpy as np
from jax import lax
from jax.experimental import pallas as pl
from jax.experimental.pallas import tpu as pltpu
from jax.sharding import PartitionSpec as P

CH_BLK = 128
WIN = 512
NF = 128
FLO = 8


whiten_eps = 1e-06


def from_behind(array, axis, by):
    count = lax.axis_size(axis)
    pairs = [(i, i + by) for i in range(count) if 0 <= i + by < count]
    return lax.ppermute(array, axis, pairs)


def exchange(outgoing, axis):
    count = lax.axis_size(axis)
    me = lax.axis_index(axis)
    pieces = [lax.dynamic_index_in_dim(outgoing, me, 0, keepdims=False)]
    for shift in range(1, count):
        piece = lax.dynamic_index_in_dim(outgoing, (me + shift) % count, 0, keepdims=False)
        pairs = [(i, (i + shift) % count) for i in range(count)]
        pieces.append(lax.ppermute(piece, axis, pairs))
    return jnp.stack(pieces)


def toeplitz(fir_taps):
    length = fir_taps.shape[0]
    reversed_taps = fir_taps[::-1]
    base_column = jnp.concatenate(
        [jnp.zeros((1,), fir_taps.dtype), reversed_taps, jnp.zeros((length,), fir_taps.dtype)]
    )
    flattened = jnp.tile(base_column, length)[: 2 * length * length]
    return flattened.reshape(length, 2 * length).T


def bandpass(recording, fir_taps, tail_rows):
    channels, length = recording.shape
    width = fir_taps.shape[0]
    current = recording.reshape(channels, length // width, width)
    previous = jnp.concatenate([tail_rows[:, None, :], current[:, :-1, :]], axis=1)
    extended = jnp.concatenate([previous, current], axis=2).reshape(
        channels * (length // width), 2 * width
    )
    product = jnp.dot(extended, toeplitz(fir_taps), preferred_element_type=jnp.float32)
    return product.reshape(channels, length).astype(jnp.bfloat16)


def dft_table(length, bins, lowest):
    samples = np.arange(length, dtype=np.int64)
    indices = lowest + np.arange(bins, dtype=np.int64)
    phase = (samples[:, None] * indices[None, :] % length).astype(np.float64) * (
        2.0 * math.pi / length
    )
    basis_table = np.stack([np.cos(phase), -np.sin(phase)], axis=2)
    return basis_table.reshape(length, 2 * bins).astype(ml_dtypes.bfloat16)


def front_kernel(cnt_ref, rec_ref, tail_ref, g_ref, *rest):
    outs, (scr_ref, inv_ref) = rest[:-2], rest[-2:]
    tile, length = rec_ref.shape
    width = tail_ref.shape[1]
    bins2 = g_ref.shape[1]
    windows = length // WIN
    response = g_ref[...]
    count = cnt_ref[0]
    for w in range(windows):
        if w == 0:
            ext = jnp.concatenate([tail_ref[...], rec_ref[:, 0:WIN]], axis=1)
        else:
            ext = rec_ref[:, WIN * w - width : WIN * w + WIN]
        spec = jnp.dot(ext, response, preferred_element_type=jnp.float32).T
        for h in range(tile // CH_BLK):
            scr_ref[h, pl.ds(bins2 * w, bins2), :] = spec[:, CH_BLK * h : CH_BLK * (h + 1)]
        power = jnp.sum(spec * spec, axis=0, keepdims=True) * (1.0 / bins2)
        keep = jnp.where(count > w, 1.0, 0.0).astype(jnp.float32)
        inv_ref[pl.ds(w, 1), :] = lax.rsqrt(power + whiten_eps) * keep
    scales = inv_ref[...]

    start = 0
    for o_ref in outs:

        def one_row(k, carry, o_ref=o_ref, start=start):
            for h in range(tile // CH_BLK):
                rows = scr_ref[h, pl.ds(start + k, windows, stride=bins2), :]
                part = rows * scales[:, CH_BLK * h : CH_BLK * (h + 1)]
                o_ref[k, :, CH_BLK * h : CH_BLK * (h + 1)] = part.astype(o_ref.dtype)
            return carry

        lax.fori_loop(0, o_ref.shape[0], one_row, 0)
        start += o_ref.shape[0]


def whiten_front(recording, tail_rows, fir_taps, kept_count, chunks, tile=512):
    channels, length = recording.shape
    width = tail_rows.shape[1]
    windows = length // WIN
    toep = toeplitz(fir_taps)
    sections = lax.axis_size("tm")
    bins_dev = NF // sections
    basis = dft_table(WIN, NF, FLO).reshape(WIN, sections, bins_dev, 2)
    basis = np.concatenate(
        [basis[:, :, lo:hi].reshape(WIN, -1) for lo, hi in zip(chunks[:-1], chunks[1:])], axis=1
    )
    basis = jnp.asarray(basis)
    bins2 = basis.shape[1]
    blocks = [
        jnp.dot(toep, basis[i * width : (i + 1) * width], preferred_element_type=jnp.float32)
        for i in range(WIN // width)
    ]
    response = jnp.zeros((WIN + width, bins2), jnp.float32)
    for i, part in enumerate(blocks):
        response = response.at[i * width : i * width + 2 * width].add(part)
    response = response.astype(jnp.bfloat16)
    rows = [sections * (hi - lo) * 2 for lo, hi in zip(chunks[:-1], chunks[1:])]
    grid_spec = pltpu.PrefetchScalarGridSpec(
        num_scalar_prefetch=1,
        grid=(channels // tile,),
        in_specs=[
            pl.BlockSpec((tile, length), lambda i, c: (i, 0)),
            pl.BlockSpec((tile, width), lambda i, c: (i, 0)),
            pl.BlockSpec(response.shape, lambda i, c: (0, 0)),
        ],
        out_specs=[pl.BlockSpec((r, windows, tile), lambda i, c: (0, 0, i)) for r in rows],
        scratch_shapes=[
            pltpu.VMEM((tile // CH_BLK, windows * bins2, CH_BLK), jnp.float32),
            pltpu.VMEM((windows, tile), jnp.float32),
        ],
    )
    flops = 2 * channels * windows * (WIN + width) * bins2
    return pl.pallas_call(
        front_kernel,
        grid_spec=grid_spec,
        out_shape=[jax.ShapeDtypeStruct((r, windows, channels), jnp.bfloat16) for r in rows],
        compiler_params=pltpu.CompilerParams(
            dimension_semantics=("arbitrary",), vmem_limit_bytes=48 * 1024 * 1024
        ),
        cost_estimate=pl.CostEstimate(
            flops=flops,
            bytes_accessed=channels * length * 2 + bins2 * windows * channels * 2,
            transcendentals=channels * windows,
        ),
    )(kept_count, recording, tail_rows, response)


def stack_kernel(pb_ref, kw_ref, q_ref, a_ref, b_ref, *rest):
    o_ref = rest[-1]
    sections = kw_ref.shape[0]
    total = kw_ref[0]
    for s in range(1, sections):
        total = total + kw_ref[s]
    scale = 1.0 / jnp.sqrt(jnp.full((1, 1), total, jnp.int32).astype(jnp.float32))
    segs, bins, _, wins, blk = a_ref.shape

    def one_bin(jl, carry):
        left = a_ref[:, jl].reshape(segs * 2 * wins, blk)
        right = b_ref[:, jl]
        swapped = jnp.concatenate([right[:, 1:2], -right[:, 0:1]], axis=1)
        rhs = jnp.concatenate(
            [right.reshape(segs * 2 * wins, blk), swapped.reshape(segs * 2 * wins, blk)], axis=1
        )
        out = lax.dot_general(
            left, rhs, (((0,), (0,)), ((), ())), preferred_element_type=jnp.float32
        )
        o_ref[0, jl, 0] = out[:, :blk] * scale
        o_ref[0, jl, 1] = out[:, blk:] * scale
        return carry

    lax.fori_loop(0, bins, one_bin, 0, unroll=True)


def stack_pairs(gathered, pair_blocks, kept_windows, half, chunk, all_bins, previous=None):
    halves, segs, bins, two, wins, chans = gathered.shape
    blocks_per_half = chans // CH_BLK
    npairs = pair_blocks.shape[0]

    def left_map(p, pb, kw, q):
        a = pb[p, 0]
        return ((a // blocks_per_half + q[0]) % halves, 0, 0, 0, 0, a % blocks_per_half)

    def right_map(p, pb, kw, q):
        b = pb[p, 1]
        return ((b // blocks_per_half + q[0]) % halves, 0, 0, 0, 0, b % blocks_per_half)

    block = (None, segs, bins, two, wins, CH_BLK)
    in_specs = [pl.BlockSpec(block, left_map), pl.BlockSpec(block, right_map)]
    operands = [pair_blocks, kept_windows, half, gathered, gathered]
    aliases = {}
    if previous is not None:
        in_specs.append(pl.BlockSpec(memory_space=pl.ANY))
        operands.append(previous)
        aliases = {5: 0}
    grid_spec = pltpu.PrefetchScalarGridSpec(
        num_scalar_prefetch=3,
        grid=(npairs,),
        in_specs=in_specs,
        out_specs=pl.BlockSpec(
            (1, bins, 2, CH_BLK, CH_BLK), lambda p, pb, kw, q: (p, chunk, 0, 0, 0)
        ),
    )
    flops = 2 * npairs * bins * CH_BLK * (2 * CH_BLK) * (segs * two * wins)
    out_bytes = npairs * bins * 2 * CH_BLK * CH_BLK * 4
    in_bytes = 2 * npairs * segs * bins * two * wins * CH_BLK * 2
    return pl.pallas_call(
        stack_kernel,
        grid_spec=grid_spec,
        out_shape=jax.ShapeDtypeStruct((npairs, all_bins, 2, CH_BLK, CH_BLK), jnp.float32),
        input_output_aliases=aliases,
        compiler_params=pltpu.CompilerParams(
            dimension_semantics=("arbitrary",), vmem_limit_bytes=48 * 1024 * 1024
        ),
        cost_estimate=pl.CostEstimate(
            flops=flops, bytes_accessed=out_bytes + in_bytes, transcendentals=0
        ),
    )(*operands)


def per_device(recording, fir_taps, kept_windows, pair_blocks):
    channels, length = recording.shape
    width = fir_taps.shape[0]
    sections = lax.axis_size("tm")
    tail_rows = from_behind(recording[:, length - width :], "tm", 1)
    windows_dev = length // WIN
    segment = lax.axis_index("tm")
    kept_count = lax.dynamic_slice_in_dim(kept_windows, segment, 1, 0)
    bins_dev = NF // sections
    small = max(bins_dev // 4, 1)
    chunks = [0, bins_dev - small, bins_dev] if bins_dev > 1 else [0, bins_dev]
    whitened = whiten_front(recording, tail_rows, fir_taps, kept_count, chunks)
    half = jnp.zeros((1,), jnp.int32)
    result = None
    for lo, hi, part in zip(chunks[:-1], chunks[1:], whitened):
        outgoing = part.reshape(sections, hi - lo, 2, windows_dev, channels)
        by_freq = lax.all_to_all(outgoing, "tm", split_axis=0, concat_axis=0, tiled=True)
        gathered = lax.all_gather(by_freq, "pair", axis=0, tiled=False)
        result = stack_pairs(
            gathered, pair_blocks, kept_windows, half, lo // (hi - lo), bins_dev, result
        )
    return result


def solution(mesh):
    placed = (P(("groups", "pair"), "tm"), P(), P("groups"), P(("groups", "pair"), None))
    return jax.shard_map(
        per_device,
        mesh=mesh,
        in_specs=placed,
        out_specs=P(("groups", "pair"), "tm", None, None, None),
        check_vma=False,
    )
```

```python
import functools
import math

import jax
import jax.numpy as jnp
import ml_dtypes
import numpy as np
from jax import lax
from jax.experimental import pallas as pl
from jax.experimental.pallas import tpu as pltpu
from jax.sharding import PartitionSpec as P

CH_BLK = 128
WIN = 512
NF = 128
FLO = 8


whiten_eps = 1e-06


def from_behind(array, axis, by):
    count = lax.axis_size(axis)
    pairs = [(i, i + by) for i in range(count) if 0 <= i + by < count]
    return lax.ppermute(array, axis, pairs)


def exchange(outgoing, axis):
    count = lax.axis_size(axis)
    me = lax.axis_index(axis)
    pieces = [lax.dynamic_index_in_dim(outgoing, me, 0, keepdims=False)]
    for shift in range(1, count):
        piece = lax.dynamic_index_in_dim(outgoing, (me + shift) % count, 0, keepdims=False)
        pairs = [(i, (i + shift) % count) for i in range(count)]
        pieces.append(lax.ppermute(piece, axis, pairs))
    return jnp.stack(pieces)


def toeplitz(fir_taps):
    length = fir_taps.shape[0]
    reversed_taps = fir_taps[::-1]
    base_column = jnp.concatenate(
        [jnp.zeros((1,), fir_taps.dtype), reversed_taps, jnp.zeros((length,), fir_taps.dtype)]
    )
    flattened = jnp.tile(base_column, length)[: 2 * length * length]
    return flattened.reshape(length, 2 * length).T


def bandpass(recording, fir_taps, tail_rows):
    channels, length = recording.shape
    width = fir_taps.shape[0]
    current = recording.reshape(channels, length // width, width)
    previous = jnp.concatenate([tail_rows[:, None, :], current[:, :-1, :]], axis=1)
    extended = jnp.concatenate([previous, current], axis=2).reshape(
        channels * (length // width), 2 * width
    )
    product = jnp.dot(extended, toeplitz(fir_taps), preferred_element_type=jnp.float32)
    return product.reshape(channels, length).astype(jnp.bfloat16)


def dft_table(length, bins, lowest):
    samples = np.arange(length, dtype=np.int64)
    indices = lowest + np.arange(bins, dtype=np.int64)
    phase = (samples[:, None] * indices[None, :] % length).astype(np.float64) * (
        2.0 * math.pi / length
    )
    basis_table = np.stack([np.cos(phase), -np.sin(phase)], axis=2)
    return basis_table.reshape(length, 2 * bins).astype(ml_dtypes.bfloat16)


def front_kernel(cnt_ref, rec_ref, tail_ref, toep_ref, basis_ref, *rest):
    outs, (scr_ref, inv_ref) = rest[:-2], rest[-2:]
    tile, length = rec_ref.shape
    width = tail_ref.shape[1]
    bins2 = basis_ref.shape[1]
    windows = length // WIN
    toep = toep_ref[...]
    basis = basis_ref[...]
    count = cnt_ref[0]
    for w in range(windows):
        if w == 0:
            ext0 = jnp.concatenate([tail_ref[...], rec_ref[:, 0:width]], axis=1)
        else:
            ext0 = rec_ref[:, WIN * w - width : WIN * w + width]
        ext1 = rec_ref[:, WIN * w : WIN * w + 2 * width]
        f0 = jnp.dot(ext0, toep, preferred_element_type=jnp.float32).astype(jnp.bfloat16)
        f1 = jnp.dot(ext1, toep, preferred_element_type=jnp.float32).astype(jnp.bfloat16)
        spec = jnp.dot(
            jnp.concatenate([f0, f1], axis=1), basis, preferred_element_type=jnp.float32
        ).T
        for h in range(tile // CH_BLK):
            scr_ref[h, pl.ds(bins2 * w, bins2), :] = spec[:, CH_BLK * h : CH_BLK * (h + 1)]
        power = jnp.sum(spec * spec, axis=0, keepdims=True) * (1.0 / bins2)
        keep = jnp.where(count > w, 1.0, 0.0).astype(jnp.float32)
        inv_ref[pl.ds(w, 1), :] = lax.rsqrt(power + whiten_eps) * keep
    scales = inv_ref[...]

    start = 0
    for o_ref in outs:

        def one_row(k, carry, o_ref=o_ref, start=start):
            for h in range(tile // CH_BLK):
                rows = scr_ref[h, pl.ds(start + k, windows, stride=bins2), :]
                part = rows * scales[:, CH_BLK * h : CH_BLK * (h + 1)]
                o_ref[k, :, CH_BLK * h : CH_BLK * (h + 1)] = part.astype(o_ref.dtype)
            return carry

        lax.fori_loop(0, o_ref.shape[0], one_row, 0, unroll=8)
        start += o_ref.shape[0]


def whiten_front(recording, tail_rows, fir_taps, kept_count, chunks, tile=512):
    channels, length = recording.shape
    width = tail_rows.shape[1]
    windows = length // WIN
    toep = toeplitz(fir_taps)
    sections = lax.axis_size("tm")
    bins_dev = NF // sections
    basis = dft_table(WIN, NF, FLO).reshape(WIN, sections, bins_dev, 2)
    basis = np.concatenate(
        [basis[:, :, lo:hi].reshape(WIN, -1) for lo, hi in zip(chunks[:-1], chunks[1:])], axis=1
    )
    basis = jnp.asarray(basis)
    bins2 = basis.shape[1]
    rows = [sections * (hi - lo) * 2 for lo, hi in zip(chunks[:-1], chunks[1:])]
    grid_spec = pltpu.PrefetchScalarGridSpec(
        num_scalar_prefetch=1,
        grid=(channels // tile,),
        in_specs=[
            pl.BlockSpec((tile, length), lambda i, c: (i, 0)),
            pl.BlockSpec((tile, width), lambda i, c: (i, 0)),
            pl.BlockSpec(toep.shape, lambda i, c: (0, 0)),
            pl.BlockSpec(basis.shape, lambda i, c: (0, 0)),
        ],
        out_specs=[pl.BlockSpec((r, windows, tile), lambda i, c: (0, 0, i)) for r in rows],
        scratch_shapes=[
            pltpu.VMEM((tile // CH_BLK, windows * bins2, CH_BLK), jnp.float32),
            pltpu.VMEM((windows, tile), jnp.float32),
        ],
    )
    flops = 2 * channels * windows * 3 * (2 * width) * bins2 * 2
    return pl.pallas_call(
        front_kernel,
        grid_spec=grid_spec,
        out_shape=[jax.ShapeDtypeStruct((r, windows, channels), jnp.bfloat16) for r in rows],
        compiler_params=pltpu.CompilerParams(
            dimension_semantics=("arbitrary",), vmem_limit_bytes=48 * 1024 * 1024
        ),
        cost_estimate=pl.CostEstimate(
            flops=flops,
            bytes_accessed=channels * length * 2 + bins2 * windows * channels * 2,
            transcendentals=channels * windows,
        ),
    )(kept_count, recording, tail_rows, toep, basis)


def stack_kernel(pb_ref, kw_ref, q_ref, a_ref, b_ref, *rest):
    o_ref = rest[-1]
    sections = kw_ref.shape[0]
    total = kw_ref[0]
    for s in range(1, sections):
        total = total + kw_ref[s]
    scale = 1.0 / jnp.sqrt(jnp.full((1, 1), total, jnp.int32).astype(jnp.float32))
    segs, bins, _, wins, blk = a_ref.shape

    def one_bin(jl, carry):
        left = a_ref[:, jl].reshape(segs * 2 * wins, blk)
        right = b_ref[:, jl]
        swapped = jnp.concatenate([right[:, 1:2], -right[:, 0:1]], axis=1)
        rhs = jnp.concatenate(
            [right.reshape(segs * 2 * wins, blk), swapped.reshape(segs * 2 * wins, blk)], axis=1
        )
        out = lax.dot_general(
            left, rhs, (((0,), (0,)), ((), ())), preferred_element_type=jnp.float32
        )
        o_ref[0, jl, 0] = out[:, :blk] * scale
        o_ref[0, jl, 1] = out[:, blk:] * scale
        return carry

    lax.fori_loop(0, bins, one_bin, 0, unroll=True)


def stack_pairs(gathered, pair_blocks, kept_windows, half, chunk, all_bins, previous=None):
    halves, segs, bins, two, wins, chans = gathered.shape
    blocks_per_half = chans // CH_BLK
    npairs = pair_blocks.shape[0]

    def left_map(p, pb, kw, q):
        a = pb[p, 0]
        return ((a // blocks_per_half + q[0]) % halves, 0, 0, 0, 0, a % blocks_per_half)

    def right_map(p, pb, kw, q):
        b = pb[p, 1]
        return ((b // blocks_per_half + q[0]) % halves, 0, 0, 0, 0, b % blocks_per_half)

    block = (None, segs, bins, two, wins, CH_BLK)
    in_specs = [pl.BlockSpec(block, left_map), pl.BlockSpec(block, right_map)]
    operands = [pair_blocks, kept_windows, half, gathered, gathered]
    aliases = {}
    if previous is not None:
        in_specs.append(pl.BlockSpec(memory_space=pl.ANY))
        operands.append(previous)
        aliases = {5: 0}
    grid_spec = pltpu.PrefetchScalarGridSpec(
        num_scalar_prefetch=3,
        grid=(npairs,),
        in_specs=in_specs,
        out_specs=pl.BlockSpec(
            (1, bins, 2, CH_BLK, CH_BLK), lambda p, pb, kw, q: (p, chunk, 0, 0, 0)
        ),
    )
    flops = 2 * npairs * bins * CH_BLK * (2 * CH_BLK) * (segs * two * wins)
    out_bytes = npairs * bins * 2 * CH_BLK * CH_BLK * 4
    in_bytes = 2 * npairs * segs * bins * two * wins * CH_BLK * 2
    return pl.pallas_call(
        stack_kernel,
        grid_spec=grid_spec,
        out_shape=jax.ShapeDtypeStruct((npairs, all_bins, 2, CH_BLK, CH_BLK), jnp.float32),
        input_output_aliases=aliases,
        compiler_params=pltpu.CompilerParams(
            dimension_semantics=("arbitrary",), vmem_limit_bytes=48 * 1024 * 1024
        ),
        cost_estimate=pl.CostEstimate(
            flops=flops, bytes_accessed=out_bytes + in_bytes, transcendentals=0
        ),
    )(*operands)


def per_device(recording, fir_taps, kept_windows, pair_blocks):
    channels, length = recording.shape
    width = fir_taps.shape[0]
    sections = lax.axis_size("tm")
    tail_rows = from_behind(recording[:, length - width :], "tm", 1)
    windows_dev = length // WIN
    segment = lax.axis_index("tm")
    kept_count = lax.dynamic_slice_in_dim(kept_windows, segment, 1, 0)
    bins_dev = NF // sections
    small = max(bins_dev // 4, 1)
    chunks = [0, bins_dev - small, bins_dev] if bins_dev > 1 else [0, bins_dev]
    whitened = whiten_front(recording, tail_rows, fir_taps, kept_count, chunks)
    half = jnp.zeros((1,), jnp.int32)
    result = None
    for lo, hi, part in zip(chunks[:-1], chunks[1:], whitened):
        outgoing = part.reshape(sections, hi - lo, 2, windows_dev, channels)
        by_freq = lax.all_to_all(outgoing, "tm", split_axis=0, concat_axis=0, tiled=True)
        gathered = lax.all_gather(by_freq, "pair", axis=0, tiled=False)
        result = stack_pairs(
            gathered, pair_blocks, kept_windows, half, lo // (hi - lo), bins_dev, result
        )
    return result


def solution(mesh):
    placed = (P(("groups", "pair"), "tm"), P(), P("groups"), P(("groups", "pair"), None))
    return jax.shard_map(
        per_device,
        mesh=mesh,
        in_specs=placed,
        out_specs=P(("groups", "pair"), "tm", None, None, None),
        check_vma=False,
    )
```

```python
import functools
import math

import jax
import jax.numpy as jnp
import ml_dtypes
import numpy as np
from jax import lax
from jax.experimental import pallas as pl
from jax.experimental.pallas import tpu as pltpu
from jax.sharding import PartitionSpec as P

CH_BLK = 128
WIN = 512
NF = 128
FLO = 8


whiten_eps = 1e-06


def from_behind(array, axis, by):
    count = lax.axis_size(axis)
    pairs = [(i, i + by) for i in range(count) if 0 <= i + by < count]
    return lax.ppermute(array, axis, pairs)


def exchange(outgoing, axis):
    count = lax.axis_size(axis)
    me = lax.axis_index(axis)
    pieces = [lax.dynamic_index_in_dim(outgoing, me, 0, keepdims=False)]
    for shift in range(1, count):
        piece = lax.dynamic_index_in_dim(outgoing, (me + shift) % count, 0, keepdims=False)
        pairs = [(i, (i + shift) % count) for i in range(count)]
        pieces.append(lax.ppermute(piece, axis, pairs))
    return jnp.stack(pieces)


def toeplitz(fir_taps):
    length = fir_taps.shape[0]
    reversed_taps = fir_taps[::-1]
    base_column = jnp.concatenate(
        [jnp.zeros((1,), fir_taps.dtype), reversed_taps, jnp.zeros((length,), fir_taps.dtype)]
    )
    flattened = jnp.tile(base_column, length)[: 2 * length * length]
    return flattened.reshape(length, 2 * length).T


def bandpass(recording, fir_taps, tail_rows):
    channels, length = recording.shape
    width = fir_taps.shape[0]
    current = recording.reshape(channels, length // width, width)
    previous = jnp.concatenate([tail_rows[:, None, :], current[:, :-1, :]], axis=1)
    extended = jnp.concatenate([previous, current], axis=2).reshape(
        channels * (length // width), 2 * width
    )
    product = jnp.dot(extended, toeplitz(fir_taps), preferred_element_type=jnp.float32)
    return product.reshape(channels, length).astype(jnp.bfloat16)


def dft_table(length, bins, lowest):
    samples = np.arange(length, dtype=np.int64)
    indices = lowest + np.arange(bins, dtype=np.int64)
    phase = (samples[:, None] * indices[None, :] % length).astype(np.float64) * (
        2.0 * math.pi / length
    )
    basis_table = np.stack([np.cos(phase), -np.sin(phase)], axis=2)
    return basis_table.reshape(length, 2 * bins).astype(ml_dtypes.bfloat16)


def front_kernel(cnt_ref, rec_ref, tail_ref, toep_ref, basis_ref, *rest):
    outs, (scr_ref, inv_ref) = rest[:-2], rest[-2:]
    tile, length = rec_ref.shape
    width = tail_ref.shape[1]
    bins2 = basis_ref.shape[1]
    windows = length // WIN
    toep = toep_ref[...]
    basis = basis_ref[...]
    count = cnt_ref[lax.axis_index("tm")]
    for w in range(windows):
        if w == 0:
            ext0 = jnp.concatenate([tail_ref[...], rec_ref[:, 0:width]], axis=1)
        else:
            ext0 = rec_ref[:, WIN * w - width : WIN * w + width]
        ext1 = rec_ref[:, WIN * w : WIN * w + 2 * width]
        f0 = jnp.dot(ext0, toep, preferred_element_type=jnp.float32).astype(jnp.bfloat16)
        f1 = jnp.dot(ext1, toep, preferred_element_type=jnp.float32).astype(jnp.bfloat16)
        spec = jnp.dot(
            jnp.concatenate([f0, f1], axis=1), basis, preferred_element_type=jnp.float32
        ).T
        for h in range(tile // CH_BLK):
            scr_ref[h, pl.ds(bins2 * w, bins2), :] = spec[:, CH_BLK * h : CH_BLK * (h + 1)]
        power = jnp.sum(spec * spec, axis=0, keepdims=True) * (1.0 / bins2)
        keep = jnp.where(count > w, 1.0, 0.0).astype(jnp.float32)
        inv_ref[pl.ds(w, 1), :] = lax.rsqrt(power + whiten_eps) * keep
    scales = inv_ref[...]

    start = 0
    for o_ref in outs:

        def one_row(k, carry, o_ref=o_ref, start=start):
            for h in range(tile // CH_BLK):
                rows = scr_ref[h, pl.ds(start + k, windows, stride=bins2), :]
                part = rows * scales[:, CH_BLK * h : CH_BLK * (h + 1)]
                o_ref[k, :, CH_BLK * h : CH_BLK * (h + 1)] = part.astype(o_ref.dtype)
            return carry

        lax.fori_loop(0, o_ref.shape[0], one_row, 0, unroll=16)
        start += o_ref.shape[0]


def whiten_front(recording, tail_rows, fir_taps, kept_count, chunks, tile=512):
    channels, length = recording.shape
    width = tail_rows.shape[1]
    windows = length // WIN
    toep = toeplitz(fir_taps)
    sections = lax.axis_size("tm")
    bins_dev = NF // sections
    basis = dft_table(WIN, NF, FLO).reshape(WIN, sections, bins_dev, 2)
    basis = np.concatenate(
        [basis[:, :, lo:hi].reshape(WIN, -1) for lo, hi in zip(chunks[:-1], chunks[1:])], axis=1
    )
    basis = jnp.asarray(basis)
    bins2 = basis.shape[1]
    rows = [sections * (hi - lo) * 2 for lo, hi in zip(chunks[:-1], chunks[1:])]
    grid_spec = pltpu.PrefetchScalarGridSpec(
        num_scalar_prefetch=1,
        grid=(channels // tile,),
        in_specs=[
            pl.BlockSpec((tile, length), lambda i, c: (i, 0)),
            pl.BlockSpec((tile, width), lambda i, c: (i, 0)),
            pl.BlockSpec(toep.shape, lambda i, c: (0, 0)),
            pl.BlockSpec(basis.shape, lambda i, c: (0, 0)),
        ],
        out_specs=[pl.BlockSpec((r, windows, tile), lambda i, c: (0, 0, i)) for r in rows],
        scratch_shapes=[
            pltpu.VMEM((tile // CH_BLK, windows * bins2, CH_BLK), jnp.float32),
            pltpu.VMEM((windows, tile), jnp.float32),
        ],
    )
    flops = 2 * channels * windows * 3 * (2 * width) * bins2 * 2
    return pl.pallas_call(
        front_kernel,
        grid_spec=grid_spec,
        out_shape=[jax.ShapeDtypeStruct((r, windows, channels), jnp.bfloat16) for r in rows],
        compiler_params=pltpu.CompilerParams(
            dimension_semantics=("arbitrary",), vmem_limit_bytes=48 * 1024 * 1024
        ),
        cost_estimate=pl.CostEstimate(
            flops=flops,
            bytes_accessed=channels * length * 2 + bins2 * windows * channels * 2,
            transcendentals=channels * windows,
        ),
    )(kept_count, recording, tail_rows, toep, basis)


def stack_kernel(pb_ref, kw_ref, q_ref, a_ref, b_ref, *rest):
    o_ref = rest[-1]
    sections = kw_ref.shape[0]
    total = kw_ref[0]
    for s in range(1, sections):
        total = total + kw_ref[s]
    scale = 1.0 / jnp.sqrt(jnp.full((1, 1), total, jnp.int32).astype(jnp.float32))
    segs, bins, _, wins, blk = a_ref.shape

    def one_bin(jl, carry):
        left = a_ref[:, jl].reshape(segs * 2 * wins, blk)
        right = b_ref[:, jl]
        swapped = jnp.concatenate([right[:, 1:2], -right[:, 0:1]], axis=1)
        rhs = jnp.concatenate(
            [right.reshape(segs * 2 * wins, blk), swapped.reshape(segs * 2 * wins, blk)], axis=1
        )
        out = lax.dot_general(
            left, rhs, (((0,), (0,)), ((), ())), preferred_element_type=jnp.float32
        )
        o_ref[0, jl, 0] = out[:, :blk] * scale
        o_ref[0, jl, 1] = out[:, blk:] * scale
        return carry

    lax.fori_loop(0, bins, one_bin, 0, unroll=True)


def stack_pairs(gathered, pair_blocks, kept_windows, half, chunk, all_bins, previous=None):
    halves, segs, bins, two, wins, chans = gathered.shape
    blocks_per_half = chans // CH_BLK
    npairs = pair_blocks.shape[0]

    def left_map(p, pb, kw, q):
        a = pb[p, 0]
        return ((a // blocks_per_half + q[0]) % halves, 0, 0, 0, 0, a % blocks_per_half)

    def right_map(p, pb, kw, q):
        b = pb[p, 1]
        return ((b // blocks_per_half + q[0]) % halves, 0, 0, 0, 0, b % blocks_per_half)

    block = (None, segs, bins, two, wins, CH_BLK)
    in_specs = [pl.BlockSpec(block, left_map), pl.BlockSpec(block, right_map)]
    operands = [pair_blocks, kept_windows, half, gathered, gathered]
    aliases = {}
    if previous is not None:
        in_specs.append(pl.BlockSpec(memory_space=pl.ANY))
        operands.append(previous)
        aliases = {5: 0}
    grid_spec = pltpu.PrefetchScalarGridSpec(
        num_scalar_prefetch=3,
        grid=(npairs,),
        in_specs=in_specs,
        out_specs=pl.BlockSpec(
            (1, bins, 2, CH_BLK, CH_BLK), lambda p, pb, kw, q: (p, chunk, 0, 0, 0)
        ),
    )
    flops = 2 * npairs * bins * CH_BLK * (2 * CH_BLK) * (segs * two * wins)
    out_bytes = npairs * bins * 2 * CH_BLK * CH_BLK * 4
    in_bytes = 2 * npairs * segs * bins * two * wins * CH_BLK * 2
    return pl.pallas_call(
        stack_kernel,
        grid_spec=grid_spec,
        out_shape=jax.ShapeDtypeStruct((npairs, all_bins, 2, CH_BLK, CH_BLK), jnp.float32),
        input_output_aliases=aliases,
        compiler_params=pltpu.CompilerParams(
            dimension_semantics=("arbitrary",), vmem_limit_bytes=48 * 1024 * 1024
        ),
        cost_estimate=pl.CostEstimate(
            flops=flops, bytes_accessed=out_bytes + in_bytes, transcendentals=0
        ),
    )(*operands)


def per_device(recording, fir_taps, kept_windows, pair_blocks):
    channels, length = recording.shape
    width = fir_taps.shape[0]
    sections = lax.axis_size("tm")
    tail_rows = from_behind(recording[:, length - width :], "tm", 1)
    windows_dev = length // WIN
    bins_dev = NF // sections
    small = max(bins_dev // 4, 1)
    chunks = [0, bins_dev - small, bins_dev] if bins_dev > 1 else [0, bins_dev]
    whitened = whiten_front(recording, tail_rows, fir_taps, kept_windows, chunks)
    half = jnp.zeros((1,), jnp.int32)
    result = None
    for lo, hi, part in zip(chunks[:-1], chunks[1:], whitened):
        outgoing = part.reshape(sections, hi - lo, 2, windows_dev, channels)
        by_freq = lax.all_to_all(outgoing, "tm", split_axis=0, concat_axis=0, tiled=True)
        gathered = lax.all_gather(by_freq, "pair", axis=0, tiled=False)
        result = stack_pairs(
            gathered, pair_blocks, kept_windows, half, lo // (hi - lo), bins_dev, result
        )
    return result


def solution(mesh):
    placed = (P(("groups", "pair"), "tm"), P(), P("groups"), P(("groups", "pair"), None))
    return jax.shard_map(
        per_device,
        mesh=mesh,
        in_specs=placed,
        out_specs=P(("groups", "pair"), "tm", None, None, None),
        check_vma=False,
    )
```

```python
import functools
import math

import jax
import jax.numpy as jnp
import ml_dtypes
import numpy as np
from jax import lax
from jax.experimental import pallas as pl
from jax.experimental.pallas import tpu as pltpu
from jax.sharding import PartitionSpec as P

CH_BLK = 128
WIN = 512
NF = 128
FLO = 8


whiten_eps = 1e-06


def from_behind(array, axis, by):
    count = lax.axis_size(axis)
    pairs = [(i, i + by) for i in range(count) if 0 <= i + by < count]
    return lax.ppermute(array, axis, pairs)


def exchange(outgoing, axis):
    count = lax.axis_size(axis)
    me = lax.axis_index(axis)
    pieces = [lax.dynamic_index_in_dim(outgoing, me, 0, keepdims=False)]
    for shift in range(1, count):
        piece = lax.dynamic_index_in_dim(outgoing, (me + shift) % count, 0, keepdims=False)
        pairs = [(i, (i + shift) % count) for i in range(count)]
        pieces.append(lax.ppermute(piece, axis, pairs))
    return jnp.stack(pieces)


def toeplitz(fir_taps):
    length = fir_taps.shape[0]
    reversed_taps = fir_taps[::-1]
    base_column = jnp.concatenate(
        [jnp.zeros((1,), fir_taps.dtype), reversed_taps, jnp.zeros((length,), fir_taps.dtype)]
    )
    flattened = jnp.tile(base_column, length)[: 2 * length * length]
    return flattened.reshape(length, 2 * length).T


def bandpass(recording, fir_taps, tail_rows):
    channels, length = recording.shape
    width = fir_taps.shape[0]
    current = recording.reshape(channels, length // width, width)
    previous = jnp.concatenate([tail_rows[:, None, :], current[:, :-1, :]], axis=1)
    extended = jnp.concatenate([previous, current], axis=2).reshape(
        channels * (length // width), 2 * width
    )
    product = jnp.dot(extended, toeplitz(fir_taps), preferred_element_type=jnp.float32)
    return product.reshape(channels, length).astype(jnp.bfloat16)


def dft_table(length, bins, lowest):
    samples = np.arange(length, dtype=np.int64)
    indices = lowest + np.arange(bins, dtype=np.int64)
    phase = (samples[:, None] * indices[None, :] % length).astype(np.float64) * (
        2.0 * math.pi / length
    )
    basis_table = np.stack([np.cos(phase), -np.sin(phase)], axis=2)
    return basis_table.reshape(length, 2 * bins).astype(ml_dtypes.bfloat16)


def front_kernel(cnt_ref, rec_ref, tail_ref, toep_ref, basis_ref, *rest):
    outs, (scr_ref, inv_ref) = rest[:-2], rest[-2:]
    tile, length = rec_ref.shape
    width = tail_ref.shape[1]
    bins2 = basis_ref.shape[1]
    windows = length // WIN
    toep = toep_ref[...]
    basis = basis_ref[...]
    count = cnt_ref[lax.axis_index("tm")]
    for w in range(windows):
        if w == 0:
            ext0 = jnp.concatenate([tail_ref[...], rec_ref[:, 0:width]], axis=1)
        else:
            ext0 = rec_ref[:, WIN * w - width : WIN * w + width]
        ext1 = rec_ref[:, WIN * w : WIN * w + 2 * width]
        f0 = jnp.dot(ext0, toep, preferred_element_type=jnp.float32).astype(jnp.bfloat16)
        f1 = jnp.dot(ext1, toep, preferred_element_type=jnp.float32).astype(jnp.bfloat16)
        spec = jnp.dot(
            jnp.concatenate([f0, f1], axis=1), basis, preferred_element_type=jnp.float32
        ).T
        for h in range(tile // CH_BLK):
            scr_ref[h, pl.ds(bins2 * w, bins2), :] = spec[:, CH_BLK * h : CH_BLK * (h + 1)]
        power = jnp.sum(spec * spec, axis=0, keepdims=True) * (1.0 / bins2)
        keep = jnp.where(count > w, 1.0, 0.0).astype(jnp.float32)
        inv_ref[pl.ds(w, 1), :] = lax.rsqrt(power + whiten_eps) * keep
    scales = inv_ref[...]

    start = 0
    for o_ref in outs:

        def one_row(k, carry, o_ref=o_ref, start=start):
            for h in range(tile // CH_BLK):
                rows = scr_ref[h, pl.ds(start + k, windows, stride=bins2), :]
                part = rows * scales[:, CH_BLK * h : CH_BLK * (h + 1)]
                o_ref[k, :, CH_BLK * h : CH_BLK * (h + 1)] = part.astype(o_ref.dtype)
            return carry

        lax.fori_loop(0, o_ref.shape[0], one_row, 0, unroll=16)
        start += o_ref.shape[0]


def whiten_front(recording, tail_rows, fir_taps, kept_count, chunks, tile=512):
    channels, length = recording.shape
    width = tail_rows.shape[1]
    windows = length // WIN
    toep = toeplitz(fir_taps)
    sections = lax.axis_size("tm")
    bins_dev = NF // sections
    basis = dft_table(WIN, NF, FLO).reshape(WIN, sections, bins_dev, 2)
    basis = np.concatenate(
        [basis[:, :, lo:hi].reshape(WIN, -1) for lo, hi in zip(chunks[:-1], chunks[1:])], axis=1
    )
    basis = jnp.asarray(basis)
    bins2 = basis.shape[1]
    rows = [sections * (hi - lo) * 2 for lo, hi in zip(chunks[:-1], chunks[1:])]
    grid_spec = pltpu.PrefetchScalarGridSpec(
        num_scalar_prefetch=1,
        grid=(channels // tile,),
        in_specs=[
            pl.BlockSpec((tile, length), lambda i, c: (i, 0)),
            pl.BlockSpec((tile, width), lambda i, c: (i, 0)),
            pl.BlockSpec(toep.shape, lambda i, c: (0, 0)),
            pl.BlockSpec(basis.shape, lambda i, c: (0, 0)),
        ],
        out_specs=[pl.BlockSpec((r, windows, tile), lambda i, c: (0, 0, i)) for r in rows],
        scratch_shapes=[
            pltpu.VMEM((tile // CH_BLK, windows * bins2, CH_BLK), jnp.float32),
            pltpu.VMEM((windows, tile), jnp.float32),
        ],
    )
    flops = 2 * channels * windows * 3 * (2 * width) * bins2 * 2
    return pl.pallas_call(
        front_kernel,
        grid_spec=grid_spec,
        out_shape=[jax.ShapeDtypeStruct((r, windows, channels), jnp.bfloat16) for r in rows],
        compiler_params=pltpu.CompilerParams(
            dimension_semantics=("arbitrary",), vmem_limit_bytes=48 * 1024 * 1024
        ),
        cost_estimate=pl.CostEstimate(
            flops=flops,
            bytes_accessed=channels * length * 2 + bins2 * windows * channels * 2,
            transcendentals=channels * windows,
        ),
    )(kept_count, recording, tail_rows, toep, basis)


def stack_kernel_for(half_blocks, pb_ref, kw_ref, am_ref, ap_ref, bm_ref, bp_ref, *rest):
    o_ref = rest[-1]
    sections = kw_ref.shape[0]
    total = kw_ref[0]
    for s in range(1, sections):
        total = total + kw_ref[s]
    scale = 1.0 / jnp.sqrt(jnp.full((1, 1), total, jnp.int32).astype(jnp.float32))
    segs, bins, _, wins, blk = am_ref.shape
    p = pl.program_id(0)
    mine = lax.axis_index("pair")
    left_mine = pb_ref[p, 0] // half_blocks == mine
    right_mine = pb_ref[p, 1] // half_blocks == mine

    def one_bin(jl, carry):
        left = jnp.where(left_mine, am_ref[:, jl], ap_ref[:, jl]).reshape(segs * 2 * wins, blk)
        right = jnp.where(right_mine, bm_ref[:, jl], bp_ref[:, jl])
        swapped = jnp.concatenate([right[:, 1:2], -right[:, 0:1]], axis=1)
        rhs = jnp.concatenate(
            [right.reshape(segs * 2 * wins, blk), swapped.reshape(segs * 2 * wins, blk)], axis=1
        )
        out = lax.dot_general(
            left, rhs, (((0,), (0,)), ((), ())), preferred_element_type=jnp.float32
        )
        o_ref[0, jl, 0] = out[:, :blk] * scale
        o_ref[0, jl, 1] = out[:, blk:] * scale
        return carry

    lax.fori_loop(0, bins, one_bin, 0, unroll=True)


def stack_pairs(local, partner, pair_blocks, kept_windows, chunk, all_bins, previous=None):
    segs, bins, two, wins, chans = local.shape
    blocks_per_half = chans // CH_BLK
    npairs = pair_blocks.shape[0]

    def left_map(p, pb, kw):
        return (0, 0, 0, 0, pb[p, 0] % blocks_per_half)

    def right_map(p, pb, kw):
        return (0, 0, 0, 0, pb[p, 1] % blocks_per_half)

    block = (segs, bins, two, wins, CH_BLK)
    in_specs = [pl.BlockSpec(block, left_map)] * 2 + [pl.BlockSpec(block, right_map)] * 2
    operands = [pair_blocks, kept_windows, local, partner, local, partner]
    aliases = {}
    if previous is not None:
        in_specs.append(pl.BlockSpec(memory_space=pl.ANY))
        operands.append(previous)
        aliases = {6: 0}
    grid_spec = pltpu.PrefetchScalarGridSpec(
        num_scalar_prefetch=2,
        grid=(npairs,),
        in_specs=in_specs,
        out_specs=pl.BlockSpec(
            (1, bins, 2, CH_BLK, CH_BLK), lambda p, pb, kw: (p, chunk, 0, 0, 0)
        ),
    )
    flops = 2 * npairs * bins * CH_BLK * (2 * CH_BLK) * (segs * two * wins)
    out_bytes = npairs * bins * 2 * CH_BLK * CH_BLK * 4
    in_bytes = 4 * npairs * segs * bins * two * wins * CH_BLK * 2
    return pl.pallas_call(
        functools.partial(stack_kernel_for, blocks_per_half),
        grid_spec=grid_spec,
        out_shape=jax.ShapeDtypeStruct((npairs, all_bins, 2, CH_BLK, CH_BLK), jnp.float32),
        input_output_aliases=aliases,
        compiler_params=pltpu.CompilerParams(
            dimension_semantics=("arbitrary",), vmem_limit_bytes=48 * 1024 * 1024
        ),
        cost_estimate=pl.CostEstimate(
            flops=flops, bytes_accessed=out_bytes + in_bytes, transcendentals=0
        ),
    )(*operands)


def per_device(recording, fir_taps, kept_windows, pair_blocks):
    channels, length = recording.shape
    width = fir_taps.shape[0]
    sections = lax.axis_size("tm")
    tail_rows = from_behind(recording[:, length - width :], "tm", 1)
    windows_dev = length // WIN
    bins_dev = NF // sections
    small = max(bins_dev // 4, 1)
    chunks = [0, bins_dev - small, bins_dev] if bins_dev > 1 else [0, bins_dev]
    whitened = whiten_front(recording, tail_rows, fir_taps, kept_windows, chunks)
    result = None
    for lo, hi, part in zip(chunks[:-1], chunks[1:], whitened):
        outgoing = part.reshape(sections, hi - lo, 2, windows_dev, channels)
        by_freq = lax.all_to_all(outgoing, "tm", split_axis=0, concat_axis=0, tiled=True)
        partner = lax.ppermute(by_freq, "pair", [(0, 1), (1, 0)])
        result = stack_pairs(
            by_freq, partner, pair_blocks, kept_windows, lo // (hi - lo), bins_dev, result
        )
    return result


def solution(mesh):
    placed = (P(("groups", "pair"), "tm"), P(), P("groups"), P(("groups", "pair"), None))
    return jax.shard_map(
        per_device,
        mesh=mesh,
        in_specs=placed,
        out_specs=P(("groups", "pair"), "tm", None, None, None),
        check_vma=False,
    )
```

```python
import functools
import math

import jax
import jax.numpy as jnp
import ml_dtypes
import numpy as np
from jax import lax
from jax.experimental import pallas as pl
from jax.experimental.pallas import tpu as pltpu
from jax.sharding import PartitionSpec as P

CH_BLK = 128
WIN = 512
NF = 128
FLO = 8


whiten_eps = 1e-06


def from_behind(array, axis, by):
    count = lax.axis_size(axis)
    pairs = [(i, i + by) for i in range(count) if 0 <= i + by < count]
    return lax.ppermute(array, axis, pairs)


def exchange(outgoing, axis):
    count = lax.axis_size(axis)
    me = lax.axis_index(axis)
    pieces = [lax.dynamic_index_in_dim(outgoing, me, 0, keepdims=False)]
    for shift in range(1, count):
        piece = lax.dynamic_index_in_dim(outgoing, (me + shift) % count, 0, keepdims=False)
        pairs = [(i, (i + shift) % count) for i in range(count)]
        pieces.append(lax.ppermute(piece, axis, pairs))
    return jnp.stack(pieces)


def toeplitz(fir_taps):
    length = fir_taps.shape[0]
    reversed_taps = fir_taps[::-1]
    base_column = jnp.concatenate(
        [jnp.zeros((1,), fir_taps.dtype), reversed_taps, jnp.zeros((length,), fir_taps.dtype)]
    )
    flattened = jnp.tile(base_column, length)[: 2 * length * length]
    return flattened.reshape(length, 2 * length).T


def bandpass(recording, fir_taps, tail_rows):
    channels, length = recording.shape
    width = fir_taps.shape[0]
    current = recording.reshape(channels, length // width, width)
    previous = jnp.concatenate([tail_rows[:, None, :], current[:, :-1, :]], axis=1)
    extended = jnp.concatenate([previous, current], axis=2).reshape(
        channels * (length // width), 2 * width
    )
    product = jnp.dot(extended, toeplitz(fir_taps), preferred_element_type=jnp.float32)
    return product.reshape(channels, length).astype(jnp.bfloat16)


def dft_table(length, bins, lowest):
    samples = np.arange(length, dtype=np.int64)
    indices = lowest + np.arange(bins, dtype=np.int64)
    phase = (samples[:, None] * indices[None, :] % length).astype(np.float64) * (
        2.0 * math.pi / length
    )
    basis_table = np.stack([np.cos(phase), -np.sin(phase)], axis=2)
    return basis_table.reshape(length, 2 * bins).astype(ml_dtypes.bfloat16)


def front_kernel(cnt_ref, rec_ref, tail_ref, toep_ref, basis_ref, *rest):
    outs, (scr_ref, inv_ref) = rest[:-2], rest[-2:]
    tile, length = rec_ref.shape
    width = tail_ref.shape[1]
    bins2 = basis_ref.shape[1]
    windows = length // WIN
    toep = toep_ref[...]
    basis = basis_ref[...]
    count = cnt_ref[lax.axis_index("tm")]
    for w in range(windows):
        if w == 0:
            ext0 = jnp.concatenate([tail_ref[...], rec_ref[:, 0:width]], axis=1)
        else:
            ext0 = rec_ref[:, WIN * w - width : WIN * w + width]
        ext1 = rec_ref[:, WIN * w : WIN * w + 2 * width]
        f0 = jnp.dot(ext0, toep, preferred_element_type=jnp.float32).astype(jnp.bfloat16)
        f1 = jnp.dot(ext1, toep, preferred_element_type=jnp.float32).astype(jnp.bfloat16)
        spec = jnp.dot(
            jnp.concatenate([f0, f1], axis=1), basis, preferred_element_type=jnp.float32
        ).T
        for h in range(tile // CH_BLK):
            scr_ref[h, pl.ds(bins2 * w, bins2), :] = spec[:, CH_BLK * h : CH_BLK * (h + 1)]
        power = jnp.sum(spec * spec, axis=0, keepdims=True) * (1.0 / bins2)
        keep = jnp.where(count > w, 1.0, 0.0).astype(jnp.float32)
        inv_ref[pl.ds(w, 1), :] = lax.rsqrt(power + whiten_eps) * keep
    scales = inv_ref[...]

    start = 0
    for o_ref in outs:

        def one_row(k, carry, o_ref=o_ref, start=start):
            for h in range(tile // CH_BLK):
                rows = scr_ref[h, pl.ds(start + k, windows, stride=bins2), :]
                part = rows * scales[:, CH_BLK * h : CH_BLK * (h + 1)]
                o_ref[k, :, CH_BLK * h : CH_BLK * (h + 1)] = part.astype(o_ref.dtype)
            return carry

        lax.fori_loop(0, o_ref.shape[0], one_row, 0, unroll=16)
        start += o_ref.shape[0]


def whiten_front(recording, tail_rows, fir_taps, kept_count, chunks, tile=512):
    channels, length = recording.shape
    width = tail_rows.shape[1]
    windows = length // WIN
    toep = toeplitz(fir_taps)
    sections = lax.axis_size("tm")
    bins_dev = NF // sections
    basis = dft_table(WIN, NF, FLO).reshape(WIN, sections, bins_dev, 2)
    basis = np.concatenate(
        [basis[:, :, lo:hi].reshape(WIN, -1) for lo, hi in zip(chunks[:-1], chunks[1:])], axis=1
    )
    basis = jnp.asarray(basis)
    bins2 = basis.shape[1]
    rows = [sections * (hi - lo) * 2 for lo, hi in zip(chunks[:-1], chunks[1:])]
    grid_spec = pltpu.PrefetchScalarGridSpec(
        num_scalar_prefetch=1,
        grid=(channels // tile,),
        in_specs=[
            pl.BlockSpec((tile, length), lambda i, c: (i, 0)),
            pl.BlockSpec((tile, width), lambda i, c: (i, 0)),
            pl.BlockSpec(toep.shape, lambda i, c: (0, 0)),
            pl.BlockSpec(basis.shape, lambda i, c: (0, 0)),
        ],
        out_specs=[pl.BlockSpec((r, windows, tile), lambda i, c: (0, 0, i)) for r in rows],
        scratch_shapes=[
            pltpu.VMEM((tile // CH_BLK, windows * bins2, CH_BLK), jnp.float32),
            pltpu.VMEM((windows, tile), jnp.float32),
        ],
    )
    flops = 2 * channels * windows * 3 * (2 * width) * bins2 * 2
    return pl.pallas_call(
        front_kernel,
        grid_spec=grid_spec,
        out_shape=[jax.ShapeDtypeStruct((r, windows, channels), jnp.bfloat16) for r in rows],
        compiler_params=pltpu.CompilerParams(
            dimension_semantics=("arbitrary",), vmem_limit_bytes=48 * 1024 * 1024
        ),
        cost_estimate=pl.CostEstimate(
            flops=flops,
            bytes_accessed=channels * length * 2 + bins2 * windows * channels * 2,
            transcendentals=channels * windows,
        ),
    )(kept_count, recording, tail_rows, toep, basis)


def stack_kernel_for(half_blocks, pb_ref, kw_ref, q_ref, am_ref, ap_ref, bm_ref, bp_ref, *rest):
    o_ref = rest[-1]
    sections = kw_ref.shape[0]
    total = kw_ref[0]
    for s in range(1, sections):
        total = total + kw_ref[s]
    scale = 1.0 / jnp.sqrt(jnp.full((1, 1), total, jnp.int32).astype(jnp.float32))
    segs, bins, _, wins, blk = am_ref.shape
    p = pl.program_id(0)
    mine = q_ref[0]
    left_mine = pb_ref[p, 0] // half_blocks == mine
    right_mine = pb_ref[p, 1] // half_blocks == mine

    def one_bin(jl, carry):
        left = jnp.where(left_mine, am_ref[:, jl], ap_ref[:, jl]).reshape(segs * 2 * wins, blk)
        right = jnp.where(right_mine, bm_ref[:, jl], bp_ref[:, jl])
        swapped = jnp.concatenate([right[:, 1:2], -right[:, 0:1]], axis=1)
        rhs = jnp.concatenate(
            [right.reshape(segs * 2 * wins, blk), swapped.reshape(segs * 2 * wins, blk)], axis=1
        )
        out = lax.dot_general(
            left, rhs, (((0,), (0,)), ((), ())), preferred_element_type=jnp.float32
        )
        o_ref[0, jl, 0] = out[:, :blk] * scale
        o_ref[0, jl, 1] = out[:, blk:] * scale
        return carry

    lax.fori_loop(0, bins, one_bin, 0, unroll=True)


def stack_pairs(local, partner, pair_blocks, kept_windows, half, chunk, all_bins, previous=None):
    segs, bins, two, wins, chans = local.shape
    blocks_per_half = chans // CH_BLK
    npairs = pair_blocks.shape[0]

    def held_map(side, wanted):
        def index_map(p, pb, kw, q):
            def block_of(i):
                return pb[i, side] % blocks_per_half

            def used_at(i):
                return (pb[i, side] // blocks_per_half == q[0]) == wanted

            held = block_of(npairs - 1)
            for i in reversed(range(npairs)):
                held = jnp.where(used_at(i), block_of(i), held)
            for i in range(npairs):
                held = jnp.where(jnp.logical_and(i <= p, used_at(i)), block_of(i), held)
            return (0, 0, 0, 0, held)

        return index_map

    block = (segs, bins, two, wins, CH_BLK)
    in_specs = [
        pl.BlockSpec(block, held_map(side, wanted)) for side in (0, 1) for wanted in (True, False)
    ]
    operands = [pair_blocks, kept_windows, half, local, partner, local, partner]
    aliases = {}
    if previous is not None:
        in_specs.append(pl.BlockSpec(memory_space=pl.ANY))
        operands.append(previous)
        aliases = {7: 0}
    grid_spec = pltpu.PrefetchScalarGridSpec(
        num_scalar_prefetch=3,
        grid=(npairs,),
        in_specs=in_specs,
        out_specs=pl.BlockSpec(
            (1, bins, 2, CH_BLK, CH_BLK), lambda p, pb, kw, q: (p, chunk, 0, 0, 0)
        ),
    )
    flops = 2 * npairs * bins * CH_BLK * (2 * CH_BLK) * (segs * two * wins)
    out_bytes = npairs * bins * 2 * CH_BLK * CH_BLK * 4
    in_bytes = 2 * npairs * segs * bins * two * wins * CH_BLK * 2
    return pl.pallas_call(
        functools.partial(stack_kernel_for, blocks_per_half),
        grid_spec=grid_spec,
        out_shape=jax.ShapeDtypeStruct((npairs, all_bins, 2, CH_BLK, CH_BLK), jnp.float32),
        input_output_aliases=aliases,
        compiler_params=pltpu.CompilerParams(
            dimension_semantics=("arbitrary",), vmem_limit_bytes=48 * 1024 * 1024
        ),
        cost_estimate=pl.CostEstimate(
            flops=flops, bytes_accessed=out_bytes + in_bytes, transcendentals=0
        ),
    )(*operands)


def per_device(recording, fir_taps, kept_windows, pair_blocks):
    channels, length = recording.shape
    width = fir_taps.shape[0]
    sections = lax.axis_size("tm")
    tail_rows = from_behind(recording[:, length - width :], "tm", 1)
    windows_dev = length // WIN
    bins_dev = NF // sections
    small = max(bins_dev // 4, 1)
    chunks = [0, bins_dev - small, bins_dev] if bins_dev > 1 else [0, bins_dev]
    whitened = whiten_front(recording, tail_rows, fir_taps, kept_windows, chunks)
    half = lax.axis_index("pair").reshape(1).astype(jnp.int32)
    result = None
    for lo, hi, part in zip(chunks[:-1], chunks[1:], whitened):
        outgoing = part.reshape(sections, hi - lo, 2, windows_dev, channels)
        by_freq = lax.all_to_all(outgoing, "tm", split_axis=0, concat_axis=0, tiled=True)
        partner = lax.ppermute(by_freq, "pair", [(0, 1), (1, 0)])
        result = stack_pairs(
            by_freq, partner, pair_blocks, kept_windows, half, lo // (hi - lo), bins_dev, result
        )
    return result


def solution(mesh):
    placed = (P(("groups", "pair"), "tm"), P(), P("groups"), P(("groups", "pair"), None))
    return jax.shard_map(
        per_device,
        mesh=mesh,
        in_specs=placed,
        out_specs=P(("groups", "pair"), "tm", None, None, None),
        check_vma=False,
    )
```

```python
import functools
import math

import jax
import jax.numpy as jnp
import ml_dtypes
import numpy as np
from jax import lax
from jax.experimental import pallas as pl
from jax.experimental.pallas import tpu as pltpu
from jax.sharding import PartitionSpec as P

CH_BLK = 128
WIN = 512
NF = 128
FLO = 8


whiten_eps = 1e-06


def from_behind(array, axis, by):
    count = lax.axis_size(axis)
    pairs = [(i, i + by) for i in range(count) if 0 <= i + by < count]
    return lax.ppermute(array, axis, pairs)


def exchange(outgoing, axis):
    count = lax.axis_size(axis)
    me = lax.axis_index(axis)
    pieces = [lax.dynamic_index_in_dim(outgoing, me, 0, keepdims=False)]
    for shift in range(1, count):
        piece = lax.dynamic_index_in_dim(outgoing, (me + shift) % count, 0, keepdims=False)
        pairs = [(i, (i + shift) % count) for i in range(count)]
        pieces.append(lax.ppermute(piece, axis, pairs))
    return jnp.stack(pieces)


def toeplitz(fir_taps):
    length = fir_taps.shape[0]
    reversed_taps = fir_taps[::-1]
    base_column = jnp.concatenate(
        [jnp.zeros((1,), fir_taps.dtype), reversed_taps, jnp.zeros((length,), fir_taps.dtype)]
    )
    flattened = jnp.tile(base_column, length)[: 2 * length * length]
    return flattened.reshape(length, 2 * length).T


def bandpass(recording, fir_taps, tail_rows):
    channels, length = recording.shape
    width = fir_taps.shape[0]
    current = recording.reshape(channels, length // width, width)
    previous = jnp.concatenate([tail_rows[:, None, :], current[:, :-1, :]], axis=1)
    extended = jnp.concatenate([previous, current], axis=2).reshape(
        channels * (length // width), 2 * width
    )
    product = jnp.dot(extended, toeplitz(fir_taps), preferred_element_type=jnp.float32)
    return product.reshape(channels, length).astype(jnp.bfloat16)


def dft_table(length, bins, lowest):
    samples = np.arange(length, dtype=np.int64)
    indices = lowest + np.arange(bins, dtype=np.int64)
    phase = (samples[:, None] * indices[None, :] % length).astype(np.float64) * (
        2.0 * math.pi / length
    )
    basis_table = np.stack([np.cos(phase), -np.sin(phase)], axis=2)
    return basis_table.reshape(length, 2 * bins).astype(ml_dtypes.bfloat16)


def front_kernel(cnt_ref, rec_ref, tail_ref, toep_ref, basis_ref, *rest):
    outs, (scr_ref, inv_ref) = rest[:-2], rest[-2:]
    tile, length = rec_ref.shape
    width = tail_ref.shape[1]
    bins2 = basis_ref.shape[1]
    windows = length // WIN
    toep = toep_ref[...]
    basis = basis_ref[...]
    count = cnt_ref[lax.axis_index("tm")]
    for w in range(windows):
        if w == 0:
            ext0 = jnp.concatenate([tail_ref[...], rec_ref[:, 0:width]], axis=1)
        else:
            ext0 = rec_ref[:, WIN * w - width : WIN * w + width]
        ext1 = rec_ref[:, WIN * w : WIN * w + 2 * width]
        f0 = jnp.dot(ext0, toep, preferred_element_type=jnp.float32).astype(jnp.bfloat16)
        f1 = jnp.dot(ext1, toep, preferred_element_type=jnp.float32).astype(jnp.bfloat16)
        spec = jnp.dot(
            jnp.concatenate([f0, f1], axis=1), basis, preferred_element_type=jnp.float32
        ).T
        for h in range(tile // CH_BLK):
            scr_ref[h, pl.ds(bins2 * w, bins2), :] = spec[:, CH_BLK * h : CH_BLK * (h + 1)]
        power = jnp.sum(spec * spec, axis=0, keepdims=True) * (1.0 / bins2)
        keep = jnp.where(count > w, 1.0, 0.0).astype(jnp.float32)
        inv_ref[pl.ds(w, 1), :] = lax.rsqrt(power + whiten_eps) * keep
    scales = inv_ref[...]

    start = 0
    for o_ref in outs:

        def one_row(k, carry, o_ref=o_ref, start=start):
            for h in range(tile // CH_BLK):
                rows = scr_ref[h, pl.ds(start + k, windows, stride=bins2), :]
                part = rows * scales[:, CH_BLK * h : CH_BLK * (h + 1)]
                o_ref[k, :, CH_BLK * h : CH_BLK * (h + 1)] = part.astype(o_ref.dtype)
            return carry

        lax.fori_loop(0, o_ref.shape[0], one_row, 0, unroll=16)
        start += o_ref.shape[0]


def whiten_front(recording, tail_rows, fir_taps, kept_count, chunks, tile=512):
    channels, length = recording.shape
    width = tail_rows.shape[1]
    windows = length // WIN
    toep = toeplitz(fir_taps)
    sections = lax.axis_size("tm")
    bins_dev = NF // sections
    basis = dft_table(WIN, NF, FLO).reshape(WIN, sections, bins_dev, 2)
    basis = np.concatenate(
        [basis[:, :, lo:hi].reshape(WIN, -1) for lo, hi in zip(chunks[:-1], chunks[1:])], axis=1
    )
    basis = jnp.asarray(basis)
    bins2 = basis.shape[1]
    rows = [sections * (hi - lo) * 2 for lo, hi in zip(chunks[:-1], chunks[1:])]
    grid_spec = pltpu.PrefetchScalarGridSpec(
        num_scalar_prefetch=1,
        grid=(channels // tile,),
        in_specs=[
            pl.BlockSpec((tile, length), lambda i, c: (i, 0)),
            pl.BlockSpec((tile, width), lambda i, c: (i, 0)),
            pl.BlockSpec(toep.shape, lambda i, c: (0, 0)),
            pl.BlockSpec(basis.shape, lambda i, c: (0, 0)),
        ],
        out_specs=[pl.BlockSpec((r, windows, tile), lambda i, c: (0, 0, i)) for r in rows],
        scratch_shapes=[
            pltpu.VMEM((tile // CH_BLK, windows * bins2, CH_BLK), jnp.float32),
            pltpu.VMEM((windows, tile), jnp.float32),
        ],
    )
    flops = 2 * channels * windows * 3 * (2 * width) * bins2 * 2
    return pl.pallas_call(
        front_kernel,
        grid_spec=grid_spec,
        out_shape=[jax.ShapeDtypeStruct((r, windows, channels), jnp.bfloat16) for r in rows],
        compiler_params=pltpu.CompilerParams(
            dimension_semantics=("arbitrary",), vmem_limit_bytes=48 * 1024 * 1024
        ),
        cost_estimate=pl.CostEstimate(
            flops=flops,
            bytes_accessed=channels * length * 2 + bins2 * windows * channels * 2,
            transcendentals=channels * windows,
        ),
    )(kept_count, recording, tail_rows, toep, basis)


def stack_kernel_for(half_blocks, pb_ref, kw_ref, am_ref, ap_ref, bm_ref, bp_ref, *rest):
    o_ref = rest[-1]
    sections = kw_ref.shape[0]
    total = kw_ref[0]
    for s in range(1, sections):
        total = total + kw_ref[s]
    scale = 1.0 / jnp.sqrt(jnp.full((1, 1), total, jnp.int32).astype(jnp.float32))
    segs, bins, _, wins, blk = am_ref.shape
    p = pl.program_id(0)
    mine = lax.axis_index("pair")
    left_mine = pb_ref[p, 0] // half_blocks == mine
    right_mine = pb_ref[p, 1] // half_blocks == mine

    def one_bin(jl, carry):
        left = jnp.where(left_mine, am_ref[:, jl], ap_ref[:, jl]).reshape(segs * 2 * wins, blk)
        right = jnp.where(right_mine, bm_ref[:, jl], bp_ref[:, jl])
        swapped = jnp.concatenate([right[:, 1:2], -right[:, 0:1]], axis=1)
        rhs = jnp.concatenate(
            [right.reshape(segs * 2 * wins, blk), swapped.reshape(segs * 2 * wins, blk)], axis=1
        )
        out = lax.dot_general(
            left, rhs, (((0,), (0,)), ((), ())), preferred_element_type=jnp.float32
        )
        o_ref[0, jl, 0] = out[:, :blk] * scale
        o_ref[0, jl, 1] = out[:, blk:] * scale
        return carry

    lax.fori_loop(0, bins, one_bin, 0, unroll=True)


def stack_pairs(local, partner, pair_blocks, kept_windows, chunk, all_bins, previous=None):
    segs, bins, two, wins, chans = local.shape
    blocks_per_half = chans // CH_BLK
    npairs = pair_blocks.shape[0]

    def left_map(p, pb, kw):
        return (0, 0, 0, 0, pb[p, 0] % blocks_per_half)

    def right_map(p, pb, kw):
        return (0, 0, 0, 0, pb[p, 1] % blocks_per_half)

    block = (segs, bins, two, wins, CH_BLK)
    in_specs = [pl.BlockSpec(block, left_map)] * 2 + [pl.BlockSpec(block, right_map)] * 2
    operands = [pair_blocks, kept_windows, local, partner, local, partner]
    aliases = {}
    if previous is not None:
        in_specs.append(pl.BlockSpec(memory_space=pl.ANY))
        operands.append(previous)
        aliases = {6: 0}
    grid_spec = pltpu.PrefetchScalarGridSpec(
        num_scalar_prefetch=2,
        grid=(npairs,),
        in_specs=in_specs,
        out_specs=pl.BlockSpec(
            (1, bins, 2, CH_BLK, CH_BLK), lambda p, pb, kw: (p, chunk, 0, 0, 0)
        ),
    )
    flops = 2 * npairs * bins * CH_BLK * (2 * CH_BLK) * (segs * two * wins)
    out_bytes = npairs * bins * 2 * CH_BLK * CH_BLK * 4
    in_bytes = 4 * npairs * segs * bins * two * wins * CH_BLK * 2
    return pl.pallas_call(
        functools.partial(stack_kernel_for, blocks_per_half),
        grid_spec=grid_spec,
        out_shape=jax.ShapeDtypeStruct((npairs, all_bins, 2, CH_BLK, CH_BLK), jnp.float32),
        input_output_aliases=aliases,
        compiler_params=pltpu.CompilerParams(
            dimension_semantics=("arbitrary",), vmem_limit_bytes=48 * 1024 * 1024
        ),
        cost_estimate=pl.CostEstimate(
            flops=flops, bytes_accessed=out_bytes + in_bytes, transcendentals=0
        ),
    )(*operands)


def per_device(recording, fir_taps, kept_windows, pair_blocks):
    channels, length = recording.shape
    width = fir_taps.shape[0]
    sections = lax.axis_size("tm")
    tail_rows = from_behind(recording[:, length - width :], "tm", 1)
    windows_dev = length // WIN
    bins_dev = NF // sections
    small = max(bins_dev // 2, 1)
    chunks = [0, bins_dev - small, bins_dev] if bins_dev > 1 else [0, bins_dev]
    whitened = whiten_front(recording, tail_rows, fir_taps, kept_windows, chunks)
    result = None
    for lo, hi, part in zip(chunks[:-1], chunks[1:], whitened):
        outgoing = part.reshape(sections, hi - lo, 2, windows_dev, channels)
        by_freq = lax.all_to_all(outgoing, "tm", split_axis=0, concat_axis=0, tiled=True)
        partner = lax.ppermute(by_freq, "pair", [(0, 1), (1, 0)])
        result = stack_pairs(
            by_freq, partner, pair_blocks, kept_windows, lo // (hi - lo), bins_dev, result
        )
    return result


def solution(mesh):
    placed = (P(("groups", "pair"), "tm"), P(), P("groups"), P(("groups", "pair"), None))
    return jax.shard_map(
        per_device,
        mesh=mesh,
        in_specs=placed,
        out_specs=P(("groups", "pair"), "tm", None, None, None),
        check_vma=False,
    )
```

```python
import functools
import math

import jax
import jax.numpy as jnp
import ml_dtypes
import numpy as np
from jax import lax
from jax.experimental import pallas as pl
from jax.experimental.pallas import tpu as pltpu
from jax.sharding import PartitionSpec as P

CH_BLK = 128
WIN = 512
NF = 128
FLO = 8


whiten_eps = 1e-06


def from_behind(array, axis, by):
    count = lax.axis_size(axis)
    pairs = [(i, i + by) for i in range(count) if 0 <= i + by < count]
    return lax.ppermute(array, axis, pairs)


def exchange(outgoing, axis):
    count = lax.axis_size(axis)
    me = lax.axis_index(axis)
    pieces = [lax.dynamic_index_in_dim(outgoing, me, 0, keepdims=False)]
    for shift in range(1, count):
        piece = lax.dynamic_index_in_dim(outgoing, (me + shift) % count, 0, keepdims=False)
        pairs = [(i, (i + shift) % count) for i in range(count)]
        pieces.append(lax.ppermute(piece, axis, pairs))
    return jnp.stack(pieces)


def toeplitz(fir_taps):
    length = fir_taps.shape[0]
    reversed_taps = fir_taps[::-1]
    base_column = jnp.concatenate(
        [jnp.zeros((1,), fir_taps.dtype), reversed_taps, jnp.zeros((length,), fir_taps.dtype)]
    )
    flattened = jnp.tile(base_column, length)[: 2 * length * length]
    return flattened.reshape(length, 2 * length).T


def bandpass(recording, fir_taps, tail_rows):
    channels, length = recording.shape
    width = fir_taps.shape[0]
    current = recording.reshape(channels, length // width, width)
    previous = jnp.concatenate([tail_rows[:, None, :], current[:, :-1, :]], axis=1)
    extended = jnp.concatenate([previous, current], axis=2).reshape(
        channels * (length // width), 2 * width
    )
    product = jnp.dot(extended, toeplitz(fir_taps), preferred_element_type=jnp.float32)
    return product.reshape(channels, length).astype(jnp.bfloat16)


def dft_table(length, bins, lowest):
    samples = np.arange(length, dtype=np.int64)
    indices = lowest + np.arange(bins, dtype=np.int64)
    phase = (samples[:, None] * indices[None, :] % length).astype(np.float64) * (
        2.0 * math.pi / length
    )
    basis_table = np.stack([np.cos(phase), -np.sin(phase)], axis=2)
    return basis_table.reshape(length, 2 * bins).astype(ml_dtypes.bfloat16)


def front_kernel(cnt_ref, rec_ref, tail_ref, toep_ref, basis_ref, *rest):
    outs, (scr_ref, inv_ref) = rest[:-2], rest[-2:]
    tile, length = rec_ref.shape
    width = tail_ref.shape[1]
    bins2 = basis_ref.shape[1]
    windows = length // WIN
    toep = toep_ref[...]
    basis = basis_ref[...]
    count = cnt_ref[lax.axis_index("tm")]
    for w in range(windows):
        if w == 0:
            ext0 = jnp.concatenate([tail_ref[...], rec_ref[:, 0:width]], axis=1)
        else:
            ext0 = rec_ref[:, WIN * w - width : WIN * w + width]
        ext1 = rec_ref[:, WIN * w : WIN * w + 2 * width]
        f0 = jnp.dot(ext0, toep, preferred_element_type=jnp.float32).astype(jnp.bfloat16)
        f1 = jnp.dot(ext1, toep, preferred_element_type=jnp.float32).astype(jnp.bfloat16)
        spec = jnp.dot(
            jnp.concatenate([f0, f1], axis=1), basis, preferred_element_type=jnp.float32
        ).T
        for h in range(tile // CH_BLK):
            scr_ref[h, pl.ds(bins2 * w, bins2), :] = spec[:, CH_BLK * h : CH_BLK * (h + 1)]
        power = jnp.sum(spec * spec, axis=0, keepdims=True) * (1.0 / bins2)
        keep = jnp.where(count > w, 1.0, 0.0).astype(jnp.float32)
        inv_ref[pl.ds(w, 1), :] = lax.rsqrt(power + whiten_eps) * keep
    scales = inv_ref[...]

    start = 0
    for o_ref in outs:

        def one_row(k, carry, o_ref=o_ref, start=start):
            for h in range(tile // CH_BLK):
                rows = scr_ref[h, pl.ds(start + k, windows, stride=bins2), :]
                part = rows * scales[:, CH_BLK * h : CH_BLK * (h + 1)]
                o_ref[k, :, CH_BLK * h : CH_BLK * (h + 1)] = part.astype(o_ref.dtype)
            return carry

        lax.fori_loop(0, o_ref.shape[0], one_row, 0, unroll=16)
        start += o_ref.shape[0]


def whiten_front(recording, tail_rows, fir_taps, kept_count, chunks, tile=512):
    channels, length = recording.shape
    width = tail_rows.shape[1]
    windows = length // WIN
    toep = toeplitz(fir_taps)
    sections = lax.axis_size("tm")
    bins_dev = NF // sections
    basis = dft_table(WIN, NF, FLO).reshape(WIN, sections, bins_dev, 2)
    basis = np.concatenate(
        [basis[:, :, lo:hi].reshape(WIN, -1) for lo, hi in zip(chunks[:-1], chunks[1:])], axis=1
    )
    basis = jnp.asarray(basis)
    bins2 = basis.shape[1]
    rows = [sections * (hi - lo) * 2 for lo, hi in zip(chunks[:-1], chunks[1:])]
    grid_spec = pltpu.PrefetchScalarGridSpec(
        num_scalar_prefetch=1,
        grid=(channels // tile,),
        in_specs=[
            pl.BlockSpec((tile, length), lambda i, c: (i, 0)),
            pl.BlockSpec((tile, width), lambda i, c: (i, 0)),
            pl.BlockSpec(toep.shape, lambda i, c: (0, 0)),
            pl.BlockSpec(basis.shape, lambda i, c: (0, 0)),
        ],
        out_specs=[pl.BlockSpec((r, windows, tile), lambda i, c: (0, 0, i)) for r in rows],
        scratch_shapes=[
            pltpu.VMEM((tile // CH_BLK, windows * bins2, CH_BLK), jnp.float32),
            pltpu.VMEM((windows, tile), jnp.float32),
        ],
    )
    flops = 2 * channels * windows * 3 * (2 * width) * bins2 * 2
    return pl.pallas_call(
        front_kernel,
        grid_spec=grid_spec,
        out_shape=[jax.ShapeDtypeStruct((r, windows, channels), jnp.bfloat16) for r in rows],
        compiler_params=pltpu.CompilerParams(
            dimension_semantics=("arbitrary",), vmem_limit_bytes=48 * 1024 * 1024
        ),
        cost_estimate=pl.CostEstimate(
            flops=flops,
            bytes_accessed=channels * length * 2 + bins2 * windows * channels * 2,
            transcendentals=channels * windows,
        ),
    )(kept_count, recording, tail_rows, toep, basis)


def stack_kernel_for(half_blocks, pb_ref, kw_ref, am_ref, ap_ref, bm_ref, bp_ref, *rest):
    o_ref = rest[-1]
    sections = kw_ref.shape[0]
    total = kw_ref[0]
    for s in range(1, sections):
        total = total + kw_ref[s]
    scale = 1.0 / jnp.sqrt(jnp.full((1, 1), total, jnp.int32).astype(jnp.float32))
    segs, bins, _, wins, blk = am_ref.shape
    p = pl.program_id(0)
    mine = lax.axis_index("pair")
    left_mine = pb_ref[p, 0] // half_blocks == mine
    right_mine = pb_ref[p, 1] // half_blocks == mine

    def stack_from(a_ref, b_ref):
        def one_bin(jl, carry):
            left = a_ref[:, jl].reshape(segs * 2 * wins, blk)
            right = b_ref[:, jl]
            swapped = jnp.concatenate([right[:, 1:2], -right[:, 0:1]], axis=1)
            rhs = jnp.concatenate(
                [right.reshape(segs * 2 * wins, blk), swapped.reshape(segs * 2 * wins, blk)],
                axis=1,
            )
            out = lax.dot_general(
                left, rhs, (((0,), (0,)), ((), ())), preferred_element_type=jnp.float32
            )
            o_ref[0, jl, 0] = out[:, :blk] * scale
            o_ref[0, jl, 1] = out[:, blk:] * scale
            return carry

        lax.fori_loop(0, bins, one_bin, 0, unroll=True)

    for left_here in (True, False):
        for right_here in (True, False):
            chosen = jnp.logical_and(left_mine == left_here, right_mine == right_here)
            pl.when(chosen)(
                functools.partial(
                    stack_from,
                    am_ref if left_here else ap_ref,
                    bm_ref if right_here else bp_ref,
                )
            )


def stack_pairs(local, partner, pair_blocks, kept_windows, chunk, all_bins, previous=None):
    segs, bins, two, wins, chans = local.shape
    blocks_per_half = chans // CH_BLK
    npairs = pair_blocks.shape[0]

    def left_map(p, pb, kw):
        return (0, 0, 0, 0, pb[p, 0] % blocks_per_half)

    def right_map(p, pb, kw):
        return (0, 0, 0, 0, pb[p, 1] % blocks_per_half)

    block = (segs, bins, two, wins, CH_BLK)
    in_specs = [pl.BlockSpec(block, left_map)] * 2 + [pl.BlockSpec(block, right_map)] * 2
    operands = [pair_blocks, kept_windows, local, partner, local, partner]
    aliases = {}
    if previous is not None:
        in_specs.append(pl.BlockSpec(memory_space=pl.ANY))
        operands.append(previous)
        aliases = {6: 0}
    grid_spec = pltpu.PrefetchScalarGridSpec(
        num_scalar_prefetch=2,
        grid=(npairs,),
        in_specs=in_specs,
        out_specs=pl.BlockSpec(
            (1, bins, 2, CH_BLK, CH_BLK), lambda p, pb, kw: (p, chunk, 0, 0, 0)
        ),
    )
    flops = 2 * npairs * bins * CH_BLK * (2 * CH_BLK) * (segs * two * wins)
    out_bytes = npairs * bins * 2 * CH_BLK * CH_BLK * 4
    in_bytes = 4 * npairs * segs * bins * two * wins * CH_BLK * 2
    return pl.pallas_call(
        functools.partial(stack_kernel_for, blocks_per_half),
        grid_spec=grid_spec,
        out_shape=jax.ShapeDtypeStruct((npairs, all_bins, 2, CH_BLK, CH_BLK), jnp.float32),
        input_output_aliases=aliases,
        compiler_params=pltpu.CompilerParams(
            dimension_semantics=("arbitrary",), vmem_limit_bytes=48 * 1024 * 1024
        ),
        cost_estimate=pl.CostEstimate(
            flops=flops, bytes_accessed=out_bytes + in_bytes, transcendentals=0
        ),
    )(*operands)


def per_device(recording, fir_taps, kept_windows, pair_blocks):
    channels, length = recording.shape
    width = fir_taps.shape[0]
    sections = lax.axis_size("tm")
    tail_rows = from_behind(recording[:, length - width :], "tm", 1)
    windows_dev = length // WIN
    bins_dev = NF // sections
    small = max(bins_dev // 2, 1)
    chunks = [0, bins_dev - small, bins_dev] if bins_dev > 1 else [0, bins_dev]
    whitened = whiten_front(recording, tail_rows, fir_taps, kept_windows, chunks)
    result = None
    for lo, hi, part in zip(chunks[:-1], chunks[1:], whitened):
        outgoing = part.reshape(sections, hi - lo, 2, windows_dev, channels)
        by_freq = lax.all_to_all(outgoing, "tm", split_axis=0, concat_axis=0, tiled=True)
        partner = lax.ppermute(by_freq, "pair", [(0, 1), (1, 0)])
        result = stack_pairs(
            by_freq, partner, pair_blocks, kept_windows, lo // (hi - lo), bins_dev, result
        )
    return result


def solution(mesh):
    placed = (P(("groups", "pair"), "tm"), P(), P("groups"), P(("groups", "pair"), None))
    return jax.shard_map(
        per_device,
        mesh=mesh,
        in_specs=placed,
        out_specs=P(("groups", "pair"), "tm", None, None, None),
        check_vma=False,
    )
```

```python
import functools
import math

import jax
import jax.numpy as jnp
import ml_dtypes
import numpy as np
from jax import lax
from jax.experimental import pallas as pl
from jax.experimental.pallas import tpu as pltpu
from jax.sharding import PartitionSpec as P

CH_BLK = 128
WIN = 512
NF = 128
FLO = 8


whiten_eps = 1e-06


def from_behind(array, axis, by):
    count = lax.axis_size(axis)
    pairs = [(i, i + by) for i in range(count) if 0 <= i + by < count]
    return lax.ppermute(array, axis, pairs)


def exchange(outgoing, axis):
    count = lax.axis_size(axis)
    me = lax.axis_index(axis)
    pieces = [lax.dynamic_index_in_dim(outgoing, me, 0, keepdims=False)]
    for shift in range(1, count):
        piece = lax.dynamic_index_in_dim(outgoing, (me + shift) % count, 0, keepdims=False)
        pairs = [(i, (i + shift) % count) for i in range(count)]
        pieces.append(lax.ppermute(piece, axis, pairs))
    return jnp.stack(pieces)


def toeplitz(fir_taps):
    length = fir_taps.shape[0]
    reversed_taps = fir_taps[::-1]
    base_column = jnp.concatenate(
        [jnp.zeros((1,), fir_taps.dtype), reversed_taps, jnp.zeros((length,), fir_taps.dtype)]
    )
    flattened = jnp.tile(base_column, length)[: 2 * length * length]
    return flattened.reshape(length, 2 * length).T


def bandpass(recording, fir_taps, tail_rows):
    channels, length = recording.shape
    width = fir_taps.shape[0]
    current = recording.reshape(channels, length // width, width)
    previous = jnp.concatenate([tail_rows[:, None, :], current[:, :-1, :]], axis=1)
    extended = jnp.concatenate([previous, current], axis=2).reshape(
        channels * (length // width), 2 * width
    )
    product = jnp.dot(extended, toeplitz(fir_taps), preferred_element_type=jnp.float32)
    return product.reshape(channels, length).astype(jnp.bfloat16)


def dft_table(length, bins, lowest):
    samples = np.arange(length, dtype=np.int64)
    indices = lowest + np.arange(bins, dtype=np.int64)
    phase = (samples[:, None] * indices[None, :] % length).astype(np.float64) * (
        2.0 * math.pi / length
    )
    basis_table = np.stack([np.cos(phase), -np.sin(phase)], axis=2)
    return basis_table.reshape(length, 2 * bins).astype(ml_dtypes.bfloat16)


def front_kernel(cnt_ref, rec_ref, tail_ref, toep_ref, basis_ref, *rest):
    outs, (scr_ref, inv_ref) = rest[:-2], rest[-2:]
    tile, length = rec_ref.shape
    width = tail_ref.shape[1]
    bins2 = basis_ref.shape[1]
    windows = length // WIN
    toep = toep_ref[...]
    basis = basis_ref[...]
    count = cnt_ref[lax.axis_index("tm")]
    for w in range(windows):
        if w == 0:
            ext0 = jnp.concatenate([tail_ref[...], rec_ref[:, 0:width]], axis=1)
        else:
            ext0 = rec_ref[:, WIN * w - width : WIN * w + width]
        ext1 = rec_ref[:, WIN * w : WIN * w + 2 * width]
        f0 = jnp.dot(ext0, toep, preferred_element_type=jnp.float32).astype(jnp.bfloat16)
        f1 = jnp.dot(ext1, toep, preferred_element_type=jnp.float32).astype(jnp.bfloat16)
        spec = jnp.dot(
            jnp.concatenate([f0, f1], axis=1), basis, preferred_element_type=jnp.float32
        ).T
        for h in range(tile // CH_BLK):
            scr_ref[h, pl.ds(bins2 * w, bins2), :] = spec[:, CH_BLK * h : CH_BLK * (h + 1)]
        power = jnp.sum(spec * spec, axis=0, keepdims=True) * (1.0 / bins2)
        keep = jnp.where(count > w, 1.0, 0.0).astype(jnp.float32)
        inv_ref[pl.ds(w, 1), :] = lax.rsqrt(power + whiten_eps) * keep
    scales = inv_ref[...]

    start = 0
    for o_ref in outs:

        def one_row(k, carry, o_ref=o_ref, start=start):
            for h in range(tile // CH_BLK):
                rows = scr_ref[h, pl.ds(start + k, windows, stride=bins2), :]
                part = rows * scales[:, CH_BLK * h : CH_BLK * (h + 1)]
                o_ref[k, :, CH_BLK * h : CH_BLK * (h + 1)] = part.astype(o_ref.dtype)
            return carry

        lax.fori_loop(0, o_ref.shape[0], one_row, 0, unroll=16)
        start += o_ref.shape[0]


def whiten_front(recording, tail_rows, fir_taps, kept_count, chunks, tile=256):
    channels, length = recording.shape
    width = tail_rows.shape[1]
    windows = length // WIN
    toep = toeplitz(fir_taps)
    sections = lax.axis_size("tm")
    bins_dev = NF // sections
    basis = dft_table(WIN, NF, FLO).reshape(WIN, sections, bins_dev, 2)
    basis = np.concatenate(
        [basis[:, :, lo:hi].reshape(WIN, -1) for lo, hi in zip(chunks[:-1], chunks[1:])], axis=1
    )
    basis = jnp.asarray(basis)
    bins2 = basis.shape[1]
    rows = [sections * (hi - lo) * 2 for lo, hi in zip(chunks[:-1], chunks[1:])]
    grid_spec = pltpu.PrefetchScalarGridSpec(
        num_scalar_prefetch=1,
        grid=(channels // tile,),
        in_specs=[
            pl.BlockSpec((tile, length), lambda i, c: (i, 0)),
            pl.BlockSpec((tile, width), lambda i, c: (i, 0)),
            pl.BlockSpec(toep.shape, lambda i, c: (0, 0)),
            pl.BlockSpec(basis.shape, lambda i, c: (0, 0)),
        ],
        out_specs=[pl.BlockSpec((r, windows, tile), lambda i, c: (0, 0, i)) for r in rows],
        scratch_shapes=[
            pltpu.VMEM((tile // CH_BLK, windows * bins2, CH_BLK), jnp.float32),
            pltpu.VMEM((windows, tile), jnp.float32),
        ],
    )
    flops = 2 * channels * windows * 3 * (2 * width) * bins2 * 2
    return pl.pallas_call(
        front_kernel,
        grid_spec=grid_spec,
        out_shape=[jax.ShapeDtypeStruct((r, windows, channels), jnp.bfloat16) for r in rows],
        compiler_params=pltpu.CompilerParams(
            dimension_semantics=("arbitrary",), vmem_limit_bytes=48 * 1024 * 1024
        ),
        cost_estimate=pl.CostEstimate(
            flops=flops,
            bytes_accessed=channels * length * 2 + bins2 * windows * channels * 2,
            transcendentals=channels * windows,
        ),
    )(kept_count, recording, tail_rows, toep, basis)


def stack_kernel_for(half_blocks, pb_ref, kw_ref, am_ref, ap_ref, bm_ref, bp_ref, *rest):
    o_ref = rest[-1]
    sections = kw_ref.shape[0]
    total = kw_ref[0]
    for s in range(1, sections):
        total = total + kw_ref[s]
    scale = 1.0 / jnp.sqrt(jnp.full((1, 1), total, jnp.int32).astype(jnp.float32))
    segs, bins, _, wins, blk = am_ref.shape
    p = pl.program_id(0)
    mine = lax.axis_index("pair")
    left_mine = pb_ref[p, 0] // half_blocks == mine
    right_mine = pb_ref[p, 1] // half_blocks == mine

    def one_bin(jl, carry):
        left = jnp.where(left_mine, am_ref[:, jl], ap_ref[:, jl]).reshape(segs * 2 * wins, blk)
        right = jnp.where(right_mine, bm_ref[:, jl], bp_ref[:, jl])
        swapped = jnp.concatenate([right[:, 1:2], -right[:, 0:1]], axis=1)
        rhs = jnp.concatenate(
            [right.reshape(segs * 2 * wins, blk), swapped.reshape(segs * 2 * wins, blk)], axis=1
        )
        out = lax.dot_general(
            left, rhs, (((0,), (0,)), ((), ())), preferred_element_type=jnp.float32
        )
        o_ref[0, jl, 0] = out[:, :blk] * scale
        o_ref[0, jl, 1] = out[:, blk:] * scale
        return carry

    lax.fori_loop(0, bins, one_bin, 0, unroll=True)


def stack_pairs(local, partner, pair_blocks, kept_windows, chunk, all_bins, previous=None):
    segs, bins, two, wins, chans = local.shape
    blocks_per_half = chans // CH_BLK
    npairs = pair_blocks.shape[0]

    def left_map(p, pb, kw):
        return (0, 0, 0, 0, pb[p, 0] % blocks_per_half)

    def right_map(p, pb, kw):
        return (0, 0, 0, 0, pb[p, 1] % blocks_per_half)

    block = (segs, bins, two, wins, CH_BLK)
    in_specs = [pl.BlockSpec(block, left_map)] * 2 + [pl.BlockSpec(block, right_map)] * 2
    operands = [pair_blocks, kept_windows, local, partner, local, partner]
    aliases = {}
    if previous is not None:
        in_specs.append(pl.BlockSpec(memory_space=pl.ANY))
        operands.append(previous)
        aliases = {6: 0}
    grid_spec = pltpu.PrefetchScalarGridSpec(
        num_scalar_prefetch=2,
        grid=(npairs,),
        in_specs=in_specs,
        out_specs=pl.BlockSpec(
            (1, bins, 2, CH_BLK, CH_BLK), lambda p, pb, kw: (p, chunk, 0, 0, 0)
        ),
    )
    flops = 2 * npairs * bins * CH_BLK * (2 * CH_BLK) * (segs * two * wins)
    out_bytes = npairs * bins * 2 * CH_BLK * CH_BLK * 4
    in_bytes = 4 * npairs * segs * bins * two * wins * CH_BLK * 2
    return pl.pallas_call(
        functools.partial(stack_kernel_for, blocks_per_half),
        grid_spec=grid_spec,
        out_shape=jax.ShapeDtypeStruct((npairs, all_bins, 2, CH_BLK, CH_BLK), jnp.float32),
        input_output_aliases=aliases,
        compiler_params=pltpu.CompilerParams(
            dimension_semantics=("arbitrary",), vmem_limit_bytes=48 * 1024 * 1024
        ),
        cost_estimate=pl.CostEstimate(
            flops=flops, bytes_accessed=out_bytes + in_bytes, transcendentals=0
        ),
    )(*operands)


def per_device(recording, fir_taps, kept_windows, pair_blocks):
    channels, length = recording.shape
    width = fir_taps.shape[0]
    sections = lax.axis_size("tm")
    tail_rows = from_behind(recording[:, length - width :], "tm", 1)
    windows_dev = length // WIN
    bins_dev = NF // sections
    small = max(bins_dev // 2, 1)
    chunks = [0, bins_dev - small, bins_dev] if bins_dev > 1 else [0, bins_dev]
    whitened = whiten_front(recording, tail_rows, fir_taps, kept_windows, chunks)
    result = None
    for lo, hi, part in zip(chunks[:-1], chunks[1:], whitened):
        outgoing = part.reshape(sections, hi - lo, 2, windows_dev, channels)
        by_freq = lax.all_to_all(outgoing, "tm", split_axis=0, concat_axis=0, tiled=True)
        partner = lax.ppermute(by_freq, "pair", [(0, 1), (1, 0)])
        result = stack_pairs(
            by_freq, partner, pair_blocks, kept_windows, lo // (hi - lo), bins_dev, result
        )
    return result


def solution(mesh):
    placed = (P(("groups", "pair"), "tm"), P(), P("groups"), P(("groups", "pair"), None))
    return jax.shard_map(
        per_device,
        mesh=mesh,
        in_specs=placed,
        out_specs=P(("groups", "pair"), "tm", None, None, None),
        check_vma=False,
    )
```

```python
import functools
import math

import jax
import jax.numpy as jnp
import ml_dtypes
import numpy as np
from jax import lax
from jax.experimental import pallas as pl
from jax.experimental.pallas import tpu as pltpu
from jax.sharding import PartitionSpec as P

CH_BLK = 128
WIN = 512
NF = 128
FLO = 8


whiten_eps = 1e-06


def from_behind(array, axis, by):
    count = lax.axis_size(axis)
    pairs = [(i, i + by) for i in range(count) if 0 <= i + by < count]
    return lax.ppermute(array, axis, pairs)


def exchange(outgoing, axis):
    count = lax.axis_size(axis)
    me = lax.axis_index(axis)
    pieces = [lax.dynamic_index_in_dim(outgoing, me, 0, keepdims=False)]
    for shift in range(1, count):
        piece = lax.dynamic_index_in_dim(outgoing, (me + shift) % count, 0, keepdims=False)
        pairs = [(i, (i + shift) % count) for i in range(count)]
        pieces.append(lax.ppermute(piece, axis, pairs))
    return jnp.stack(pieces)


def toeplitz(fir_taps):
    length = fir_taps.shape[0]
    reversed_taps = fir_taps[::-1]
    base_column = jnp.concatenate(
        [jnp.zeros((1,), fir_taps.dtype), reversed_taps, jnp.zeros((length,), fir_taps.dtype)]
    )
    flattened = jnp.tile(base_column, length)[: 2 * length * length]
    return flattened.reshape(length, 2 * length).T


def bandpass(recording, fir_taps, tail_rows):
    channels, length = recording.shape
    width = fir_taps.shape[0]
    current = recording.reshape(channels, length // width, width)
    previous = jnp.concatenate([tail_rows[:, None, :], current[:, :-1, :]], axis=1)
    extended = jnp.concatenate([previous, current], axis=2).reshape(
        channels * (length // width), 2 * width
    )
    product = jnp.dot(extended, toeplitz(fir_taps), preferred_element_type=jnp.float32)
    return product.reshape(channels, length).astype(jnp.bfloat16)


def dft_table(length, bins, lowest):
    samples = np.arange(length, dtype=np.int64)
    indices = lowest + np.arange(bins, dtype=np.int64)
    phase = (samples[:, None] * indices[None, :] % length).astype(np.float64) * (
        2.0 * math.pi / length
    )
    basis_table = np.stack([np.cos(phase), -np.sin(phase)], axis=2)
    return basis_table.reshape(length, 2 * bins).astype(ml_dtypes.bfloat16)


def front_kernel(cnt_ref, rec_ref, toep_ref, basis_ref, *rest):
    outs, f1_ref, (scr_ref, inv_ref) = rest[:-3], rest[-3], rest[-2:]
    tile, length = rec_ref.shape
    width = toep_ref.shape[1]
    bins2 = basis_ref.shape[1]
    windows = length // WIN
    toep = toep_ref[...]
    basis = basis_ref[...]
    count = cnt_ref[lax.axis_index("tm")]
    f1_ref[...] = jnp.dot(
        rec_ref[:, 0 : 2 * width], toep, preferred_element_type=jnp.float32
    ).astype(jnp.bfloat16)
    for h in range(tile // CH_BLK):
        scr_ref[h, pl.ds(0, bins2), :] = jnp.zeros((bins2, CH_BLK), jnp.float32)
    inv_ref[pl.ds(0, 1), :] = jnp.zeros((1, tile), jnp.float32)
    for w in range(1, windows):
        ext0 = rec_ref[:, WIN * w - width : WIN * w + width]
        ext1 = rec_ref[:, WIN * w : WIN * w + 2 * width]
        f0 = jnp.dot(ext0, toep, preferred_element_type=jnp.float32).astype(jnp.bfloat16)
        f1 = jnp.dot(ext1, toep, preferred_element_type=jnp.float32).astype(jnp.bfloat16)
        spec = jnp.dot(
            jnp.concatenate([f0, f1], axis=1), basis, preferred_element_type=jnp.float32
        ).T
        for h in range(tile // CH_BLK):
            scr_ref[h, pl.ds(bins2 * w, bins2), :] = spec[:, CH_BLK * h : CH_BLK * (h + 1)]
        power = jnp.sum(spec * spec, axis=0, keepdims=True) * (1.0 / bins2)
        keep = jnp.where(count > w, 1.0, 0.0).astype(jnp.float32)
        inv_ref[pl.ds(w, 1), :] = lax.rsqrt(power + whiten_eps) * keep
    scales = inv_ref[...]

    start = 0
    for o_ref in outs:

        def one_row(k, carry, o_ref=o_ref, start=start):
            for h in range(tile // CH_BLK):
                rows = scr_ref[h, pl.ds(start + k, windows, stride=bins2), :]
                part = rows * scales[:, CH_BLK * h : CH_BLK * (h + 1)]
                o_ref[k, :, CH_BLK * h : CH_BLK * (h + 1)] = part.astype(o_ref.dtype)
            return carry

        lax.fori_loop(0, o_ref.shape[0], one_row, 0, unroll=16)
        start += o_ref.shape[0]


def first_window_kernel(count_parts, cnt_ref, tail_ref, rec_ref, f1_ref, toep_ref, basis_ref, *rest):
    ins, outs, w0_ref = rest[:count_parts], rest[count_parts : 2 * count_parts], rest[-1]
    bins2 = basis_ref.shape[1]
    count = cnt_ref[lax.axis_index("tm")]
    ext0 = jnp.concatenate([tail_ref[...], rec_ref[...]], axis=1)
    f0 = jnp.dot(ext0, toep_ref[...], preferred_element_type=jnp.float32).astype(jnp.bfloat16)
    spec = jnp.dot(
        jnp.concatenate([f0, f1_ref[...]], axis=1), basis_ref[...], preferred_element_type=jnp.float32
    ).T
    power = jnp.sum(spec * spec, axis=0, keepdims=True) * (1.0 / bins2)
    keep = jnp.where(count > 0, 1.0, 0.0).astype(jnp.float32)
    w0_ref[...] = spec * (lax.rsqrt(power + whiten_eps) * keep)
    start = 0
    for i_ref, o_ref in zip(ins, outs):

        def one_row(k, carry, i_ref=i_ref, o_ref=o_ref, start=start):
            held = i_ref[k]
            first = w0_ref[pl.ds(start + k, 1), :].astype(held.dtype)
            rowid = lax.broadcasted_iota(jnp.int32, held.shape, 0)
            o_ref[k] = jnp.where(rowid == 0, first, held)
            return carry

        lax.fori_loop(0, o_ref.shape[0], one_row, 0, unroll=8)
        start += o_ref.shape[0]


def fill_first_window(parts, recording, tail_rows, f1, toep, basis, kept_count):
    channels, width = tail_rows.shape
    bins2 = basis.shape[1]
    count_parts = len(parts)
    full = lambda shape: pl.BlockSpec(shape, lambda i, c: (0,) * len(shape))
    grid_spec = pltpu.PrefetchScalarGridSpec(
        num_scalar_prefetch=1,
        grid=(1,),
        in_specs=[
            full(tail_rows.shape),
            pl.BlockSpec((channels, width), lambda i, c: (0, 0)),
            full(f1.shape),
            full(toep.shape),
            full(basis.shape),
        ]
        + [full(p.shape) for p in parts],
        out_specs=[full(p.shape) for p in parts],
        scratch_shapes=[pltpu.VMEM((bins2, channels), jnp.float32)],
    )
    return pl.pallas_call(
        functools.partial(first_window_kernel, count_parts),
        grid_spec=grid_spec,
        out_shape=[jax.ShapeDtypeStruct(p.shape, p.dtype) for p in parts],
        input_output_aliases={6 + i: i for i in range(count_parts)},
        compiler_params=pltpu.CompilerParams(
            dimension_semantics=("arbitrary",), vmem_limit_bytes=48 * 1024 * 1024
        ),
        cost_estimate=pl.CostEstimate(
            flops=2 * channels * 3 * (2 * width) * bins2,
            bytes_accessed=4 * sum(p.size for p in parts),
            transcendentals=channels,
        ),
    )(kept_count, tail_rows, recording, f1, toep, basis, *parts)


def whiten_front(recording, tail_rows, fir_taps, kept_count, chunks, tile=512):
    channels, length = recording.shape
    width = tail_rows.shape[1]
    windows = length // WIN
    toep = toeplitz(fir_taps)
    sections = lax.axis_size("tm")
    bins_dev = NF // sections
    basis = dft_table(WIN, NF, FLO).reshape(WIN, sections, bins_dev, 2)
    basis = np.concatenate(
        [basis[:, :, lo:hi].reshape(WIN, -1) for lo, hi in zip(chunks[:-1], chunks[1:])], axis=1
    )
    basis = jnp.asarray(basis)
    bins2 = basis.shape[1]
    rows = [sections * (hi - lo) * 2 for lo, hi in zip(chunks[:-1], chunks[1:])]
    grid_spec = pltpu.PrefetchScalarGridSpec(
        num_scalar_prefetch=1,
        grid=(channels // tile,),
        in_specs=[
            pl.BlockSpec((tile, length), lambda i, c: (i, 0)),
            pl.BlockSpec(toep.shape, lambda i, c: (0, 0)),
            pl.BlockSpec(basis.shape, lambda i, c: (0, 0)),
        ],
        out_specs=[pl.BlockSpec((r, windows, tile), lambda i, c: (0, 0, i)) for r in rows]
        + [pl.BlockSpec((tile, width), lambda i, c: (i, 0))],
        scratch_shapes=[
            pltpu.VMEM((tile // CH_BLK, windows * bins2, CH_BLK), jnp.float32),
            pltpu.VMEM((windows, tile), jnp.float32),
        ],
    )
    flops = 2 * channels * windows * 3 * (2 * width) * bins2 * 2
    *parts, f1 = pl.pallas_call(
        front_kernel,
        grid_spec=grid_spec,
        out_shape=[jax.ShapeDtypeStruct((r, windows, channels), jnp.bfloat16) for r in rows]
        + [jax.ShapeDtypeStruct((channels, width), jnp.bfloat16)],
        compiler_params=pltpu.CompilerParams(
            dimension_semantics=("arbitrary",), vmem_limit_bytes=48 * 1024 * 1024
        ),
        cost_estimate=pl.CostEstimate(
            flops=flops,
            bytes_accessed=channels * length * 2 + bins2 * windows * channels * 2,
            transcendentals=channels * windows,
        ),
    )(kept_count, recording, toep, basis)
    return fill_first_window(parts, recording, tail_rows, f1, toep, basis, kept_count)


def stack_kernel_for(half_blocks, pb_ref, kw_ref, am_ref, ap_ref, bm_ref, bp_ref, *rest):
    o_ref = rest[-1]
    sections = kw_ref.shape[0]
    total = kw_ref[0]
    for s in range(1, sections):
        total = total + kw_ref[s]
    scale = 1.0 / jnp.sqrt(jnp.full((1, 1), total, jnp.int32).astype(jnp.float32))
    segs, bins, _, wins, blk = am_ref.shape
    p = pl.program_id(0)
    mine = lax.axis_index("pair")
    left_mine = pb_ref[p, 0] // half_blocks == mine
    right_mine = pb_ref[p, 1] // half_blocks == mine

    def one_bin(jl, carry):
        left = jnp.where(left_mine, am_ref[:, jl], ap_ref[:, jl]).reshape(segs * 2 * wins, blk)
        right = jnp.where(right_mine, bm_ref[:, jl], bp_ref[:, jl])
        swapped = jnp.concatenate([right[:, 1:2], -right[:, 0:1]], axis=1)
        rhs = jnp.concatenate(
            [right.reshape(segs * 2 * wins, blk), swapped.reshape(segs * 2 * wins, blk)], axis=1
        )
        out = lax.dot_general(
            left, rhs, (((0,), (0,)), ((), ())), preferred_element_type=jnp.float32
        )
        o_ref[0, jl, 0] = out[:, :blk] * scale
        o_ref[0, jl, 1] = out[:, blk:] * scale
        return carry

    lax.fori_loop(0, bins, one_bin, 0, unroll=True)


def stack_pairs(local, partner, pair_blocks, kept_windows, chunk, all_bins, previous=None):
    segs, bins, two, wins, chans = local.shape
    blocks_per_half = chans // CH_BLK
    npairs = pair_blocks.shape[0]

    def left_map(p, pb, kw):
        return (0, 0, 0, 0, pb[p, 0] % blocks_per_half)

    def right_map(p, pb, kw):
        return (0, 0, 0, 0, pb[p, 1] % blocks_per_half)

    block = (segs, bins, two, wins, CH_BLK)
    in_specs = [pl.BlockSpec(block, left_map)] * 2 + [pl.BlockSpec(block, right_map)] * 2
    operands = [pair_blocks, kept_windows, local, partner, local, partner]
    aliases = {}
    if previous is not None:
        in_specs.append(pl.BlockSpec(memory_space=pl.ANY))
        operands.append(previous)
        aliases = {6: 0}
    grid_spec = pltpu.PrefetchScalarGridSpec(
        num_scalar_prefetch=2,
        grid=(npairs,),
        in_specs=in_specs,
        out_specs=pl.BlockSpec(
            (1, bins, 2, CH_BLK, CH_BLK), lambda p, pb, kw: (p, chunk, 0, 0, 0)
        ),
    )
    flops = 2 * npairs * bins * CH_BLK * (2 * CH_BLK) * (segs * two * wins)
    out_bytes = npairs * bins * 2 * CH_BLK * CH_BLK * 4
    in_bytes = 4 * npairs * segs * bins * two * wins * CH_BLK * 2
    return pl.pallas_call(
        functools.partial(stack_kernel_for, blocks_per_half),
        grid_spec=grid_spec,
        out_shape=jax.ShapeDtypeStruct((npairs, all_bins, 2, CH_BLK, CH_BLK), jnp.float32),
        input_output_aliases=aliases,
        compiler_params=pltpu.CompilerParams(
            dimension_semantics=("arbitrary",), vmem_limit_bytes=48 * 1024 * 1024
        ),
        cost_estimate=pl.CostEstimate(
            flops=flops, bytes_accessed=out_bytes + in_bytes, transcendentals=0
        ),
    )(*operands)


def per_device(recording, fir_taps, kept_windows, pair_blocks):
    channels, length = recording.shape
    width = fir_taps.shape[0]
    sections = lax.axis_size("tm")
    tail_rows = from_behind(recording[:, length - width :], "tm", 1)
    windows_dev = length // WIN
    bins_dev = NF // sections
    small = max(bins_dev // 2, 1)
    chunks = [0, bins_dev - small, bins_dev] if bins_dev > 1 else [0, bins_dev]
    whitened = whiten_front(recording, tail_rows, fir_taps, kept_windows, chunks)
    result = None
    for lo, hi, part in zip(chunks[:-1], chunks[1:], whitened):
        outgoing = part.reshape(sections, hi - lo, 2, windows_dev, channels)
        by_freq = lax.all_to_all(outgoing, "tm", split_axis=0, concat_axis=0, tiled=True)
        partner = lax.ppermute(by_freq, "pair", [(0, 1), (1, 0)])
        result = stack_pairs(
            by_freq, partner, pair_blocks, kept_windows, lo // (hi - lo), bins_dev, result
        )
    return result


def solution(mesh):
    placed = (P(("groups", "pair"), "tm"), P(), P("groups"), P(("groups", "pair"), None))
    return jax.shard_map(
        per_device,
        mesh=mesh,
        in_specs=placed,
        out_specs=P(("groups", "pair"), "tm", None, None, None),
        check_vma=False,
    )
```

```python
import functools
import math

import jax
import jax.numpy as jnp
import ml_dtypes
import numpy as np
from jax import lax
from jax.experimental import pallas as pl
from jax.experimental.pallas import tpu as pltpu
from jax.sharding import PartitionSpec as P

CH_BLK = 128
WIN = 512
NF = 128
FLO = 8


whiten_eps = 1e-06


def from_behind(array, axis, by):
    count = lax.axis_size(axis)
    pairs = [(i, i + by) for i in range(count) if 0 <= i + by < count]
    return lax.ppermute(array, axis, pairs)


def exchange(outgoing, axis):
    count = lax.axis_size(axis)
    me = lax.axis_index(axis)
    pieces = [lax.dynamic_index_in_dim(outgoing, me, 0, keepdims=False)]
    for shift in range(1, count):
        piece = lax.dynamic_index_in_dim(outgoing, (me + shift) % count, 0, keepdims=False)
        pairs = [(i, (i + shift) % count) for i in range(count)]
        pieces.append(lax.ppermute(piece, axis, pairs))
    return jnp.stack(pieces)


def toeplitz(fir_taps):
    length = fir_taps.shape[0]
    reversed_taps = fir_taps[::-1]
    base_column = jnp.concatenate(
        [jnp.zeros((1,), fir_taps.dtype), reversed_taps, jnp.zeros((length,), fir_taps.dtype)]
    )
    flattened = jnp.tile(base_column, length)[: 2 * length * length]
    return flattened.reshape(length, 2 * length).T


def bandpass(recording, fir_taps, tail_rows):
    channels, length = recording.shape
    width = fir_taps.shape[0]
    current = recording.reshape(channels, length // width, width)
    previous = jnp.concatenate([tail_rows[:, None, :], current[:, :-1, :]], axis=1)
    extended = jnp.concatenate([previous, current], axis=2).reshape(
        channels * (length // width), 2 * width
    )
    product = jnp.dot(extended, toeplitz(fir_taps), preferred_element_type=jnp.float32)
    return product.reshape(channels, length).astype(jnp.bfloat16)


def dft_table(length, bins, lowest):
    samples = np.arange(length, dtype=np.int64)
    indices = lowest + np.arange(bins, dtype=np.int64)
    phase = (samples[:, None] * indices[None, :] % length).astype(np.float64) * (
        2.0 * math.pi / length
    )
    basis_table = np.stack([np.cos(phase), -np.sin(phase)], axis=2)
    return basis_table.reshape(length, 2 * bins).astype(ml_dtypes.bfloat16)


def front_kernel(cnt_ref, rec_ref, toep_ref, basis_ref, *rest):
    outs, f1_ref, (scr_ref, inv_ref) = rest[:-3], rest[-3], rest[-2:]
    tile, length = rec_ref.shape
    width = toep_ref.shape[1]
    bins2 = basis_ref.shape[1]
    windows = length // WIN
    toep = toep_ref[...]
    basis = basis_ref[...]
    count = cnt_ref[lax.axis_index("tm")]
    f1_ref[...] = jnp.dot(
        rec_ref[:, 0 : 2 * width], toep, preferred_element_type=jnp.float32
    ).astype(jnp.bfloat16)
    for h in range(tile // CH_BLK):
        scr_ref[h, pl.ds(0, bins2), :] = jnp.zeros((bins2, CH_BLK), jnp.float32)
    inv_ref[pl.ds(0, 1), :] = jnp.zeros((1, tile), jnp.float32)
    for w in range(1, windows):
        ext0 = rec_ref[:, WIN * w - width : WIN * w + width]
        ext1 = rec_ref[:, WIN * w : WIN * w + 2 * width]
        f0 = jnp.dot(ext0, toep, preferred_element_type=jnp.float32).astype(jnp.bfloat16)
        f1 = jnp.dot(ext1, toep, preferred_element_type=jnp.float32).astype(jnp.bfloat16)
        spec = jnp.dot(
            jnp.concatenate([f0, f1], axis=1), basis, preferred_element_type=jnp.float32
        ).T
        for h in range(tile // CH_BLK):
            scr_ref[h, pl.ds(bins2 * w, bins2), :] = spec[:, CH_BLK * h : CH_BLK * (h + 1)]
        power = jnp.sum(spec * spec, axis=0, keepdims=True) * (1.0 / bins2)
        keep = jnp.where(count > w, 1.0, 0.0).astype(jnp.float32)
        inv_ref[pl.ds(w, 1), :] = lax.rsqrt(power + whiten_eps) * keep
    scales = inv_ref[...]

    start = 0
    for o_ref in outs:

        def one_row(k, carry, o_ref=o_ref, start=start):
            for h in range(tile // CH_BLK):
                rows = scr_ref[h, pl.ds(start + k, windows, stride=bins2), :]
                part = rows * scales[:, CH_BLK * h : CH_BLK * (h + 1)]
                o_ref[k, :, CH_BLK * h : CH_BLK * (h + 1)] = part.astype(o_ref.dtype)
            return carry

        lax.fori_loop(0, o_ref.shape[0], one_row, 0, unroll=16)
        start += o_ref.shape[0]


def first_window_kernel(count_parts, part_rows, cnt_ref, tail_ref, rec_ref, f1_ref, toep_ref, basis_ref, *rest):
    ins, outs, w0_ref = rest[:count_parts], rest[count_parts : 2 * count_parts], rest[-1]
    bins2 = basis_ref.shape[1]
    step = pl.program_id(0)

    @pl.when(step == 0)
    def _():
        count = cnt_ref[lax.axis_index("tm")]
        ext0 = jnp.concatenate([tail_ref[...], rec_ref[...]], axis=1)
        f0 = jnp.dot(ext0, toep_ref[...], preferred_element_type=jnp.float32).astype(jnp.bfloat16)
        spec = jnp.dot(
            jnp.concatenate([f0, f1_ref[...]], axis=1),
            basis_ref[...],
            preferred_element_type=jnp.float32,
        ).T
        power = jnp.sum(spec * spec, axis=0, keepdims=True) * (1.0 / bins2)
        keep = jnp.where(count > 0, 1.0, 0.0).astype(jnp.float32)
        w0_ref[...] = spec * (lax.rsqrt(power + whiten_eps) * keep)

    start = 0
    for i_ref, o_ref, total in zip(ins, outs, part_rows):
        base = start + step * o_ref.shape[0]

        def one_row(k, carry, i_ref=i_ref, o_ref=o_ref, base=base):
            held = i_ref[k]
            first = w0_ref[pl.ds(base + k, 1), :].astype(held.dtype)
            rowid = lax.broadcasted_iota(jnp.int32, held.shape, 0)
            o_ref[k] = jnp.where(rowid == 0, first, held)
            return carry

        lax.fori_loop(0, o_ref.shape[0], one_row, 0, unroll=8)
        start += total


def fill_first_window(parts, recording, tail_rows, f1, toep, basis, kept_count):
    channels, width = tail_rows.shape
    bins2 = basis.shape[1]
    count_parts = len(parts)
    part_rows = tuple(p.shape[0] for p in parts)
    steps = 4
    for r in part_rows:
        steps = math.gcd(steps, r)
    full = lambda shape: pl.BlockSpec(shape, lambda i, c: (0,) * len(shape))
    piece = lambda p: pl.BlockSpec((p.shape[0] // steps,) + p.shape[1:], lambda i, c: (i, 0, 0))
    grid_spec = pltpu.PrefetchScalarGridSpec(
        num_scalar_prefetch=1,
        grid=(steps,),
        in_specs=[
            full(tail_rows.shape),
            pl.BlockSpec((channels, width), lambda i, c: (0, 0)),
            full(f1.shape),
            full(toep.shape),
            full(basis.shape),
        ]
        + [piece(p) for p in parts],
        out_specs=[piece(p) for p in parts],
        scratch_shapes=[pltpu.VMEM((bins2, channels), jnp.float32)],
    )
    return pl.pallas_call(
        functools.partial(first_window_kernel, count_parts, part_rows),
        grid_spec=grid_spec,
        out_shape=[jax.ShapeDtypeStruct(p.shape, p.dtype) for p in parts],
        input_output_aliases={6 + i: i for i in range(count_parts)},
        compiler_params=pltpu.CompilerParams(
            dimension_semantics=("arbitrary",), vmem_limit_bytes=48 * 1024 * 1024
        ),
        cost_estimate=pl.CostEstimate(
            flops=2 * channels * 3 * (2 * width) * bins2,
            bytes_accessed=4 * sum(p.size for p in parts),
            transcendentals=channels,
        ),
    )(kept_count, tail_rows, recording, f1, toep, basis, *parts)


def whiten_front(recording, tail_rows, fir_taps, kept_count, chunks, tile=512):
    channels, length = recording.shape
    width = tail_rows.shape[1]
    windows = length // WIN
    toep = toeplitz(fir_taps)
    sections = lax.axis_size("tm")
    bins_dev = NF // sections
    basis = dft_table(WIN, NF, FLO).reshape(WIN, sections, bins_dev, 2)
    basis = np.concatenate(
        [basis[:, :, lo:hi].reshape(WIN, -1) for lo, hi in zip(chunks[:-1], chunks[1:])], axis=1
    )
    basis = jnp.asarray(basis)
    bins2 = basis.shape[1]
    rows = [sections * (hi - lo) * 2 for lo, hi in zip(chunks[:-1], chunks[1:])]
    grid_spec = pltpu.PrefetchScalarGridSpec(
        num_scalar_prefetch=1,
        grid=(channels // tile,),
        in_specs=[
            pl.BlockSpec((tile, length), lambda i, c: (i, 0)),
            pl.BlockSpec(toep.shape, lambda i, c: (0, 0)),
            pl.BlockSpec(basis.shape, lambda i, c: (0, 0)),
        ],
        out_specs=[pl.BlockSpec((r, windows, tile), lambda i, c: (0, 0, i)) for r in rows]
        + [pl.BlockSpec((tile, width), lambda i, c: (i, 0))],
        scratch_shapes=[
            pltpu.VMEM((tile // CH_BLK, windows * bins2, CH_BLK), jnp.float32),
            pltpu.VMEM((windows, tile), jnp.float32),
        ],
    )
    flops = 2 * channels * windows * 3 * (2 * width) * bins2 * 2
    *parts, f1 = pl.pallas_call(
        front_kernel,
        grid_spec=grid_spec,
        out_shape=[jax.ShapeDtypeStruct((r, windows, channels), jnp.bfloat16) for r in rows]
        + [jax.ShapeDtypeStruct((channels, width), jnp.bfloat16)],
        compiler_params=pltpu.CompilerParams(
            dimension_semantics=("arbitrary",), vmem_limit_bytes=48 * 1024 * 1024
        ),
        cost_estimate=pl.CostEstimate(
            flops=flops,
            bytes_accessed=channels * length * 2 + bins2 * windows * channels * 2,
            transcendentals=channels * windows,
        ),
    )(kept_count, recording, toep, basis)
    return fill_first_window(parts, recording, tail_rows, f1, toep, basis, kept_count)


def stack_kernel_for(half_blocks, pb_ref, kw_ref, am_ref, ap_ref, bm_ref, bp_ref, *rest):
    o_ref = rest[-1]
    sections = kw_ref.shape[0]
    total = kw_ref[0]
    for s in range(1, sections):
        total = total + kw_ref[s]
    scale = 1.0 / jnp.sqrt(jnp.full((1, 1), total, jnp.int32).astype(jnp.float32))
    segs, bins, _, wins, blk = am_ref.shape
    p = pl.program_id(0)
    mine = lax.axis_index("pair")
    left_mine = pb_ref[p, 0] // half_blocks == mine
    right_mine = pb_ref[p, 1] // half_blocks == mine

    def one_bin(jl, carry):
        left = jnp.where(left_mine, am_ref[:, jl], ap_ref[:, jl]).reshape(segs * 2 * wins, blk)
        right = jnp.where(right_mine, bm_ref[:, jl], bp_ref[:, jl])
        swapped = jnp.concatenate([right[:, 1:2], -right[:, 0:1]], axis=1)
        rhs = jnp.concatenate(
            [right.reshape(segs * 2 * wins, blk), swapped.reshape(segs * 2 * wins, blk)], axis=1
        )
        out = lax.dot_general(
            left, rhs, (((0,), (0,)), ((), ())), preferred_element_type=jnp.float32
        )
        o_ref[0, jl, 0] = out[:, :blk] * scale
        o_ref[0, jl, 1] = out[:, blk:] * scale
        return carry

    lax.fori_loop(0, bins, one_bin, 0, unroll=True)


def stack_pairs(local, partner, pair_blocks, kept_windows, chunk, all_bins, previous=None):
    segs, bins, two, wins, chans = local.shape
    blocks_per_half = chans // CH_BLK
    npairs = pair_blocks.shape[0]

    def left_map(p, pb, kw):
        return (0, 0, 0, 0, pb[p, 0] % blocks_per_half)

    def right_map(p, pb, kw):
        return (0, 0, 0, 0, pb[p, 1] % blocks_per_half)

    block = (segs, bins, two, wins, CH_BLK)
    in_specs = [pl.BlockSpec(block, left_map)] * 2 + [pl.BlockSpec(block, right_map)] * 2
    operands = [pair_blocks, kept_windows, local, partner, local, partner]
    aliases = {}
    if previous is not None:
        in_specs.append(pl.BlockSpec(memory_space=pl.ANY))
        operands.append(previous)
        aliases = {6: 0}
    grid_spec = pltpu.PrefetchScalarGridSpec(
        num_scalar_prefetch=2,
        grid=(npairs,),
        in_specs=in_specs,
        out_specs=pl.BlockSpec(
            (1, bins, 2, CH_BLK, CH_BLK), lambda p, pb, kw: (p, chunk, 0, 0, 0)
        ),
    )
    flops = 2 * npairs * bins * CH_BLK * (2 * CH_BLK) * (segs * two * wins)
    out_bytes = npairs * bins * 2 * CH_BLK * CH_BLK * 4
    in_bytes = 4 * npairs * segs * bins * two * wins * CH_BLK * 2
    return pl.pallas_call(
        functools.partial(stack_kernel_for, blocks_per_half),
        grid_spec=grid_spec,
        out_shape=jax.ShapeDtypeStruct((npairs, all_bins, 2, CH_BLK, CH_BLK), jnp.float32),
        input_output_aliases=aliases,
        compiler_params=pltpu.CompilerParams(
            dimension_semantics=("arbitrary",), vmem_limit_bytes=48 * 1024 * 1024
        ),
        cost_estimate=pl.CostEstimate(
            flops=flops, bytes_accessed=out_bytes + in_bytes, transcendentals=0
        ),
    )(*operands)


def per_device(recording, fir_taps, kept_windows, pair_blocks):
    channels, length = recording.shape
    width = fir_taps.shape[0]
    sections = lax.axis_size("tm")
    tail_rows = from_behind(recording[:, length - width :], "tm", 1)
    windows_dev = length // WIN
    bins_dev = NF // sections
    small = max(bins_dev // 2, 1)
    chunks = [0, bins_dev - small, bins_dev] if bins_dev > 1 else [0, bins_dev]
    whitened = whiten_front(recording, tail_rows, fir_taps, kept_windows, chunks)
    result = None
    for lo, hi, part in zip(chunks[:-1], chunks[1:], whitened):
        outgoing = part.reshape(sections, hi - lo, 2, windows_dev, channels)
        by_freq = lax.all_to_all(outgoing, "tm", split_axis=0, concat_axis=0, tiled=True)
        partner = lax.ppermute(by_freq, "pair", [(0, 1), (1, 0)])
        result = stack_pairs(
            by_freq, partner, pair_blocks, kept_windows, lo // (hi - lo), bins_dev, result
        )
    return result


def solution(mesh):
    placed = (P(("groups", "pair"), "tm"), P(), P("groups"), P(("groups", "pair"), None))
    return jax.shard_map(
        per_device,
        mesh=mesh,
        in_specs=placed,
        out_specs=P(("groups", "pair"), "tm", None, None, None),
        check_vma=False,
    )
```

```python
import functools
import math

import jax
import jax.numpy as jnp
import ml_dtypes
import numpy as np
from jax import lax
from jax.experimental import pallas as pl
from jax.experimental.pallas import tpu as pltpu
from jax.sharding import PartitionSpec as P

CH_BLK = 128
WIN = 512
NF = 128
FLO = 8


whiten_eps = 1e-06


def from_behind(array, axis, by):
    count = lax.axis_size(axis)
    pairs = [(i, i + by) for i in range(count) if 0 <= i + by < count]
    return lax.ppermute(array, axis, pairs)


def exchange(outgoing, axis):
    count = lax.axis_size(axis)
    me = lax.axis_index(axis)
    pieces = [lax.dynamic_index_in_dim(outgoing, me, 0, keepdims=False)]
    for shift in range(1, count):
        piece = lax.dynamic_index_in_dim(outgoing, (me + shift) % count, 0, keepdims=False)
        pairs = [(i, (i + shift) % count) for i in range(count)]
        pieces.append(lax.ppermute(piece, axis, pairs))
    return jnp.stack(pieces)


def toeplitz(fir_taps):
    length = fir_taps.shape[0]
    reversed_taps = fir_taps[::-1]
    base_column = jnp.concatenate(
        [jnp.zeros((1,), fir_taps.dtype), reversed_taps, jnp.zeros((length,), fir_taps.dtype)]
    )
    flattened = jnp.tile(base_column, length)[: 2 * length * length]
    return flattened.reshape(length, 2 * length).T


def bandpass(recording, fir_taps, tail_rows):
    channels, length = recording.shape
    width = fir_taps.shape[0]
    current = recording.reshape(channels, length // width, width)
    previous = jnp.concatenate([tail_rows[:, None, :], current[:, :-1, :]], axis=1)
    extended = jnp.concatenate([previous, current], axis=2).reshape(
        channels * (length // width), 2 * width
    )
    product = jnp.dot(extended, toeplitz(fir_taps), preferred_element_type=jnp.float32)
    return product.reshape(channels, length).astype(jnp.bfloat16)


def dft_table(length, bins, lowest):
    samples = np.arange(length, dtype=np.int64)
    indices = lowest + np.arange(bins, dtype=np.int64)
    phase = (samples[:, None] * indices[None, :] % length).astype(np.float64) * (
        2.0 * math.pi / length
    )
    basis_table = np.stack([np.cos(phase), -np.sin(phase)], axis=2)
    return basis_table.reshape(length, 2 * bins).astype(ml_dtypes.bfloat16)


def front_kernel(cnt_ref, rec_ref, toep_ref, basis_ref, *rest):
    outs, f1_ref, (scr_ref, inv_ref) = rest[:-3], rest[-3], rest[-2:]
    tile, length = rec_ref.shape
    width = toep_ref.shape[1]
    bins2 = basis_ref.shape[1]
    windows = length // WIN
    toep = toep_ref[...]
    basis = basis_ref[...]
    count = cnt_ref[lax.axis_index("tm")]
    f1_ref[...] = jnp.dot(
        rec_ref[:, 0 : 2 * width], toep, preferred_element_type=jnp.float32
    ).astype(jnp.bfloat16)
    for h in range(tile // CH_BLK):
        scr_ref[h, pl.ds(0, bins2), :] = jnp.zeros((bins2, CH_BLK), jnp.float32)
    inv_ref[pl.ds(0, 1), :] = jnp.zeros((1, tile), jnp.float32)
    for w in range(1, windows):
        ext0 = rec_ref[:, WIN * w - width : WIN * w + width]
        ext1 = rec_ref[:, WIN * w : WIN * w + 2 * width]
        f0 = jnp.dot(ext0, toep, preferred_element_type=jnp.float32).astype(jnp.bfloat16)
        f1 = jnp.dot(ext1, toep, preferred_element_type=jnp.float32).astype(jnp.bfloat16)
        spec = jnp.dot(
            jnp.concatenate([f0, f1], axis=1), basis, preferred_element_type=jnp.float32
        ).T
        for h in range(tile // CH_BLK):
            scr_ref[h, pl.ds(bins2 * w, bins2), :] = spec[:, CH_BLK * h : CH_BLK * (h + 1)]
        power = jnp.sum(spec * spec, axis=0, keepdims=True) * (1.0 / bins2)
        keep = jnp.where(count > w, 1.0, 0.0).astype(jnp.float32)
        inv_ref[pl.ds(w, 1), :] = lax.rsqrt(power + whiten_eps) * keep
    scales = inv_ref[...]

    start = 0
    for o_ref in outs:

        def one_row(k, carry, o_ref=o_ref, start=start):
            for h in range(tile // CH_BLK):
                rows = scr_ref[h, pl.ds(start + k, windows, stride=bins2), :]
                part = rows * scales[:, CH_BLK * h : CH_BLK * (h + 1)]
                o_ref[k, :, CH_BLK * h : CH_BLK * (h + 1)] = part.astype(o_ref.dtype)
            return carry

        lax.fori_loop(0, o_ref.shape[0], one_row, 0, unroll=16)
        start += o_ref.shape[0]


def first_window_kernel(count_parts, cnt_ref, tail_ref, rec_ref, f1_ref, toep_ref, basis_ref, *rest):
    ins, outs, w0_ref = rest[:count_parts], rest[count_parts : 2 * count_parts], rest[-1]
    bins2 = basis_ref.shape[1]
    count = cnt_ref[lax.axis_index("tm")]
    ext0 = jnp.concatenate([tail_ref[...], rec_ref[...]], axis=1)
    f0 = jnp.dot(ext0, toep_ref[...], preferred_element_type=jnp.float32).astype(jnp.bfloat16)
    spec = jnp.dot(
        jnp.concatenate([f0, f1_ref[...]], axis=1), basis_ref[...], preferred_element_type=jnp.float32
    ).T
    power = jnp.sum(spec * spec, axis=0, keepdims=True) * (1.0 / bins2)
    keep = jnp.where(count > 0, 1.0, 0.0).astype(jnp.float32)
    w0_ref[...] = spec * (lax.rsqrt(power + whiten_eps) * keep)
    start = 0
    for i_ref, o_ref in zip(ins, outs):

        def one_row(k, carry, i_ref=i_ref, o_ref=o_ref, start=start):
            held = i_ref[k]
            first = w0_ref[pl.ds(start + k, 1), :].astype(held.dtype)
            rowid = lax.broadcasted_iota(jnp.int32, held.shape, 0)
            o_ref[k] = jnp.where(rowid == 0, first, held)
            return carry

        lax.fori_loop(0, o_ref.shape[0], one_row, 0, unroll=8)
        start += o_ref.shape[0]


def fill_first_window(parts, recording, tail_rows, f1, toep, basis, kept_count):
    channels, width = tail_rows.shape
    bins2 = basis.shape[1]
    count_parts = len(parts)
    full = lambda shape: pl.BlockSpec(shape, lambda i, c: (0,) * len(shape))
    grid_spec = pltpu.PrefetchScalarGridSpec(
        num_scalar_prefetch=1,
        grid=(1,),
        in_specs=[
            full(tail_rows.shape),
            pl.BlockSpec((channels, width), lambda i, c: (0, 0)),
            full(f1.shape),
            full(toep.shape),
            full(basis.shape),
        ]
        + [full(p.shape) for p in parts],
        out_specs=[full(p.shape) for p in parts],
        scratch_shapes=[pltpu.VMEM((bins2, channels), jnp.float32)],
    )
    return pl.pallas_call(
        functools.partial(first_window_kernel, count_parts),
        grid_spec=grid_spec,
        out_shape=[jax.ShapeDtypeStruct(p.shape, p.dtype) for p in parts],
        input_output_aliases={6 + i: i for i in range(count_parts)},
        compiler_params=pltpu.CompilerParams(
            dimension_semantics=("arbitrary",), vmem_limit_bytes=48 * 1024 * 1024
        ),
        cost_estimate=pl.CostEstimate(
            flops=2 * channels * 3 * (2 * width) * bins2,
            bytes_accessed=4 * sum(p.size for p in parts),
            transcendentals=channels,
        ),
    )(kept_count, tail_rows, recording, f1, toep, basis, *parts)


def whiten_front(recording, fir_taps, kept_count, chunks, tile=512):
    channels, length = recording.shape
    width = fir_taps.shape[0]
    windows = length // WIN
    toep = toeplitz(fir_taps)
    sections = lax.axis_size("tm")
    bins_dev = NF // sections
    basis = dft_table(WIN, NF, FLO).reshape(WIN, sections, bins_dev, 2)
    basis = np.concatenate(
        [basis[:, :, lo:hi].reshape(WIN, -1) for lo, hi in zip(chunks[:-1], chunks[1:])], axis=1
    )
    basis = jnp.asarray(basis)
    bins2 = basis.shape[1]
    rows = [sections * (hi - lo) * 2 for lo, hi in zip(chunks[:-1], chunks[1:])]
    grid_spec = pltpu.PrefetchScalarGridSpec(
        num_scalar_prefetch=1,
        grid=(channels // tile,),
        in_specs=[
            pl.BlockSpec((tile, length), lambda i, c: (i, 0)),
            pl.BlockSpec(toep.shape, lambda i, c: (0, 0)),
            pl.BlockSpec(basis.shape, lambda i, c: (0, 0)),
        ],
        out_specs=[pl.BlockSpec((r, windows, tile), lambda i, c: (0, 0, i)) for r in rows]
        + [pl.BlockSpec((tile, width), lambda i, c: (i, 0))],
        scratch_shapes=[
            pltpu.VMEM((tile // CH_BLK, windows * bins2, CH_BLK), jnp.float32),
            pltpu.VMEM((windows, tile), jnp.float32),
        ],
    )
    flops = 2 * channels * windows * 3 * (2 * width) * bins2 * 2
    *parts, f1 = pl.pallas_call(
        front_kernel,
        grid_spec=grid_spec,
        out_shape=[jax.ShapeDtypeStruct((r, windows, channels), jnp.bfloat16) for r in rows]
        + [jax.ShapeDtypeStruct((channels, width), jnp.bfloat16)],
        compiler_params=pltpu.CompilerParams(
            dimension_semantics=("arbitrary",), vmem_limit_bytes=48 * 1024 * 1024
        ),
        cost_estimate=pl.CostEstimate(
            flops=flops,
            bytes_accessed=channels * length * 2 + bins2 * windows * channels * 2,
            transcendentals=channels * windows,
        ),
    )(kept_count, recording, toep, basis)
    tail_source, f1 = lax.optimization_barrier((recording[:, length - width :], f1))
    tail_rows = from_behind(tail_source, "tm", 1)
    return fill_first_window(parts, recording, tail_rows, f1, toep, basis, kept_count)


def stack_kernel_for(half_blocks, pb_ref, kw_ref, am_ref, ap_ref, bm_ref, bp_ref, *rest):
    o_ref = rest[-1]
    sections = kw_ref.shape[0]
    total = kw_ref[0]
    for s in range(1, sections):
        total = total + kw_ref[s]
    scale = 1.0 / jnp.sqrt(jnp.full((1, 1), total, jnp.int32).astype(jnp.float32))
    segs, bins, _, wins, blk = am_ref.shape
    p = pl.program_id(0)
    mine = lax.axis_index("pair")
    left_mine = pb_ref[p, 0] // half_blocks == mine
    right_mine = pb_ref[p, 1] // half_blocks == mine

    def one_bin(jl, carry):
        left = jnp.where(left_mine, am_ref[:, jl], ap_ref[:, jl]).reshape(segs * 2 * wins, blk)
        right = jnp.where(right_mine, bm_ref[:, jl], bp_ref[:, jl])
        swapped = jnp.concatenate([right[:, 1:2], -right[:, 0:1]], axis=1)
        rhs = jnp.concatenate(
            [right.reshape(segs * 2 * wins, blk), swapped.reshape(segs * 2 * wins, blk)], axis=1
        )
        out = lax.dot_general(
            left, rhs, (((0,), (0,)), ((), ())), preferred_element_type=jnp.float32
        )
        o_ref[0, jl, 0] = out[:, :blk] * scale
        o_ref[0, jl, 1] = out[:, blk:] * scale
        return carry

    lax.fori_loop(0, bins, one_bin, 0, unroll=True)


def stack_pairs(local, partner, pair_blocks, kept_windows, chunk, all_bins, previous=None):
    segs, bins, two, wins, chans = local.shape
    blocks_per_half = chans // CH_BLK
    npairs = pair_blocks.shape[0]

    def left_map(p, pb, kw):
        return (0, 0, 0, 0, pb[p, 0] % blocks_per_half)

    def right_map(p, pb, kw):
        return (0, 0, 0, 0, pb[p, 1] % blocks_per_half)

    block = (segs, bins, two, wins, CH_BLK)
    in_specs = [pl.BlockSpec(block, left_map)] * 2 + [pl.BlockSpec(block, right_map)] * 2
    operands = [pair_blocks, kept_windows, local, partner, local, partner]
    aliases = {}
    if previous is not None:
        in_specs.append(pl.BlockSpec(memory_space=pl.ANY))
        operands.append(previous)
        aliases = {6: 0}
    grid_spec = pltpu.PrefetchScalarGridSpec(
        num_scalar_prefetch=2,
        grid=(npairs,),
        in_specs=in_specs,
        out_specs=pl.BlockSpec(
            (1, bins, 2, CH_BLK, CH_BLK), lambda p, pb, kw: (p, chunk, 0, 0, 0)
        ),
    )
    flops = 2 * npairs * bins * CH_BLK * (2 * CH_BLK) * (segs * two * wins)
    out_bytes = npairs * bins * 2 * CH_BLK * CH_BLK * 4
    in_bytes = 4 * npairs * segs * bins * two * wins * CH_BLK * 2
    return pl.pallas_call(
        functools.partial(stack_kernel_for, blocks_per_half),
        grid_spec=grid_spec,
        out_shape=jax.ShapeDtypeStruct((npairs, all_bins, 2, CH_BLK, CH_BLK), jnp.float32),
        input_output_aliases=aliases,
        compiler_params=pltpu.CompilerParams(
            dimension_semantics=("arbitrary",), vmem_limit_bytes=48 * 1024 * 1024
        ),
        cost_estimate=pl.CostEstimate(
            flops=flops, bytes_accessed=out_bytes + in_bytes, transcendentals=0
        ),
    )(*operands)


def per_device(recording, fir_taps, kept_windows, pair_blocks):
    channels, length = recording.shape
    width = fir_taps.shape[0]
    sections = lax.axis_size("tm")
    windows_dev = length // WIN
    bins_dev = NF // sections
    small = max(bins_dev // 2, 1)
    chunks = [0, bins_dev - small, bins_dev] if bins_dev > 1 else [0, bins_dev]
    whitened = whiten_front(recording, fir_taps, kept_windows, chunks)
    result = None
    for lo, hi, part in zip(chunks[:-1], chunks[1:], whitened):
        outgoing = part.reshape(sections, hi - lo, 2, windows_dev, channels)
        by_freq = lax.all_to_all(outgoing, "tm", split_axis=0, concat_axis=0, tiled=True)
        partner = lax.ppermute(by_freq, "pair", [(0, 1), (1, 0)])
        result = stack_pairs(
            by_freq, partner, pair_blocks, kept_windows, lo // (hi - lo), bins_dev, result
        )
    return result


def solution(mesh):
    placed = (P(("groups", "pair"), "tm"), P(), P("groups"), P(("groups", "pair"), None))
    return jax.shard_map(
        per_device,
        mesh=mesh,
        in_specs=placed,
        out_specs=P(("groups", "pair"), "tm", None, None, None),
        check_vma=False,
    )
```

```python
import functools
import math

import jax
import jax.numpy as jnp
import ml_dtypes
import numpy as np
from jax import lax
from jax.experimental import pallas as pl
from jax.experimental.pallas import tpu as pltpu
from jax.sharding import PartitionSpec as P

CH_BLK = 128
WIN = 512
NF = 128
FLO = 8


whiten_eps = 1e-06


def from_behind(array, axis, by):
    count = lax.axis_size(axis)
    pairs = [(i, i + by) for i in range(count) if 0 <= i + by < count]
    return lax.ppermute(array, axis, pairs)


def exchange(outgoing, axis):
    count = lax.axis_size(axis)
    me = lax.axis_index(axis)
    pieces = [lax.dynamic_index_in_dim(outgoing, me, 0, keepdims=False)]
    for shift in range(1, count):
        piece = lax.dynamic_index_in_dim(outgoing, (me + shift) % count, 0, keepdims=False)
        pairs = [(i, (i + shift) % count) for i in range(count)]
        pieces.append(lax.ppermute(piece, axis, pairs))
    return jnp.stack(pieces)


def toeplitz(fir_taps):
    length = fir_taps.shape[0]
    reversed_taps = fir_taps[::-1]
    base_column = jnp.concatenate(
        [jnp.zeros((1,), fir_taps.dtype), reversed_taps, jnp.zeros((length,), fir_taps.dtype)]
    )
    flattened = jnp.tile(base_column, length)[: 2 * length * length]
    return flattened.reshape(length, 2 * length).T


def bandpass(recording, fir_taps, tail_rows):
    channels, length = recording.shape
    width = fir_taps.shape[0]
    current = recording.reshape(channels, length // width, width)
    previous = jnp.concatenate([tail_rows[:, None, :], current[:, :-1, :]], axis=1)
    extended = jnp.concatenate([previous, current], axis=2).reshape(
        channels * (length // width), 2 * width
    )
    product = jnp.dot(extended, toeplitz(fir_taps), preferred_element_type=jnp.float32)
    return product.reshape(channels, length).astype(jnp.bfloat16)


def dft_table(length, bins, lowest):
    samples = np.arange(length, dtype=np.int64)
    indices = lowest + np.arange(bins, dtype=np.int64)
    phase = (samples[:, None] * indices[None, :] % length).astype(np.float64) * (
        2.0 * math.pi / length
    )
    basis_table = np.stack([np.cos(phase), -np.sin(phase)], axis=2)
    return basis_table.reshape(length, 2 * bins).astype(ml_dtypes.bfloat16)


def build_toeplitz(taps_ref):
    width = taps_ref.shape[1]
    row = jnp.concatenate(
        [taps_ref[...].astype(jnp.float32), jnp.zeros((1, width), jnp.float32)], axis=1
    )
    grid = jnp.broadcast_to(row, (2 * width, 2 * width))
    rolled = pltpu.roll(grid, width, 1, stride=1, stride_axis=0)
    return rolled[:, :width].astype(jnp.bfloat16)


def front_kernel(cnt_ref, rec_ref, toep_ref, basis_ref, *rest):
    outs, f1_ref, (scr_ref, inv_ref) = rest[:-3], rest[-3], rest[-2:]
    tile, length = rec_ref.shape
    width = toep_ref.shape[1]
    bins2 = basis_ref.shape[1]
    windows = length // WIN
    toep = build_toeplitz(toep_ref)
    basis = basis_ref[...]
    count = cnt_ref[lax.axis_index("tm")]
    f1_ref[...] = jnp.dot(
        rec_ref[:, 0 : 2 * width], toep, preferred_element_type=jnp.float32
    ).astype(jnp.bfloat16)
    for h in range(tile // CH_BLK):
        scr_ref[h, pl.ds(0, bins2), :] = jnp.zeros((bins2, CH_BLK), jnp.float32)
    inv_ref[pl.ds(0, 1), :] = jnp.zeros((1, tile), jnp.float32)
    for w in range(1, windows):
        ext0 = rec_ref[:, WIN * w - width : WIN * w + width]
        ext1 = rec_ref[:, WIN * w : WIN * w + 2 * width]
        f0 = jnp.dot(ext0, toep, preferred_element_type=jnp.float32).astype(jnp.bfloat16)
        f1 = jnp.dot(ext1, toep, preferred_element_type=jnp.float32).astype(jnp.bfloat16)
        spec = jnp.dot(
            jnp.concatenate([f0, f1], axis=1), basis, preferred_element_type=jnp.float32
        ).T
        for h in range(tile // CH_BLK):
            scr_ref[h, pl.ds(bins2 * w, bins2), :] = spec[:, CH_BLK * h : CH_BLK * (h + 1)]
        power = jnp.sum(spec * spec, axis=0, keepdims=True) * (1.0 / bins2)
        keep = jnp.where(count > w, 1.0, 0.0).astype(jnp.float32)
        inv_ref[pl.ds(w, 1), :] = lax.rsqrt(power + whiten_eps) * keep
    scales = inv_ref[...]

    start = 0
    for o_ref in outs:

        def one_row(k, carry, o_ref=o_ref, start=start):
            for h in range(tile // CH_BLK):
                rows = scr_ref[h, pl.ds(start + k, windows, stride=bins2), :]
                part = rows * scales[:, CH_BLK * h : CH_BLK * (h + 1)]
                o_ref[k, :, CH_BLK * h : CH_BLK * (h + 1)] = part.astype(o_ref.dtype)
            return carry

        lax.fori_loop(0, o_ref.shape[0], one_row, 0, unroll=16)
        start += o_ref.shape[0]


def first_window_kernel(count_parts, cnt_ref, tail_ref, rec_ref, f1_ref, toep_ref, basis_ref, *rest):
    ins, outs, w0_ref = rest[:count_parts], rest[count_parts : 2 * count_parts], rest[-1]
    bins2 = basis_ref.shape[1]
    count = cnt_ref[lax.axis_index("tm")]
    ext0 = jnp.concatenate([tail_ref[...], rec_ref[...]], axis=1)
    f0 = jnp.dot(ext0, build_toeplitz(toep_ref), preferred_element_type=jnp.float32).astype(
        jnp.bfloat16
    )
    spec = jnp.dot(
        jnp.concatenate([f0, f1_ref[...]], axis=1), basis_ref[...], preferred_element_type=jnp.float32
    ).T
    power = jnp.sum(spec * spec, axis=0, keepdims=True) * (1.0 / bins2)
    keep = jnp.where(count > 0, 1.0, 0.0).astype(jnp.float32)
    w0_ref[...] = spec * (lax.rsqrt(power + whiten_eps) * keep)
    start = 0
    for i_ref, o_ref in zip(ins, outs):

        def one_row(k, carry, i_ref=i_ref, o_ref=o_ref, start=start):
            held = i_ref[k]
            first = w0_ref[pl.ds(start + k, 1), :].astype(held.dtype)
            rowid = lax.broadcasted_iota(jnp.int32, held.shape, 0)
            o_ref[k] = jnp.where(rowid == 0, first, held)
            return carry

        lax.fori_loop(0, o_ref.shape[0], one_row, 0, unroll=8)
        start += o_ref.shape[0]


def fill_first_window(parts, recording, tail_rows, f1, toep, basis, kept_count):
    channels, width = tail_rows.shape
    bins2 = basis.shape[1]
    count_parts = len(parts)
    full = lambda shape: pl.BlockSpec(shape, lambda i, c: (0,) * len(shape))
    grid_spec = pltpu.PrefetchScalarGridSpec(
        num_scalar_prefetch=1,
        grid=(1,),
        in_specs=[
            full(tail_rows.shape),
            pl.BlockSpec((channels, width), lambda i, c: (0, 0)),
            full(f1.shape),
            full(toep.shape),
            full(basis.shape),
        ]
        + [full(p.shape) for p in parts],
        out_specs=[full(p.shape) for p in parts],
        scratch_shapes=[pltpu.VMEM((bins2, channels), jnp.float32)],
    )
    return pl.pallas_call(
        functools.partial(first_window_kernel, count_parts),
        grid_spec=grid_spec,
        out_shape=[jax.ShapeDtypeStruct(p.shape, p.dtype) for p in parts],
        input_output_aliases={6 + i: i for i in range(count_parts)},
        compiler_params=pltpu.CompilerParams(
            dimension_semantics=("arbitrary",), vmem_limit_bytes=48 * 1024 * 1024
        ),
        cost_estimate=pl.CostEstimate(
            flops=2 * channels * 3 * (2 * width) * bins2,
            bytes_accessed=4 * sum(p.size for p in parts),
            transcendentals=channels,
        ),
    )(kept_count, tail_rows, recording, f1, toep, basis, *parts)


def whiten_front(recording, tail_rows, fir_taps, kept_count, chunks, tile=512):
    channels, length = recording.shape
    width = tail_rows.shape[1]
    windows = length // WIN
    toep = fir_taps.reshape(1, -1)
    sections = lax.axis_size("tm")
    bins_dev = NF // sections
    basis = dft_table(WIN, NF, FLO).reshape(WIN, sections, bins_dev, 2)
    basis = np.concatenate(
        [basis[:, :, lo:hi].reshape(WIN, -1) for lo, hi in zip(chunks[:-1], chunks[1:])], axis=1
    )
    basis = jnp.asarray(basis)
    bins2 = basis.shape[1]
    rows = [sections * (hi - lo) * 2 for lo, hi in zip(chunks[:-1], chunks[1:])]
    grid_spec = pltpu.PrefetchScalarGridSpec(
        num_scalar_prefetch=1,
        grid=(channels // tile,),
        in_specs=[
            pl.BlockSpec((tile, length), lambda i, c: (i, 0)),
            pl.BlockSpec(toep.shape, lambda i, c: (0, 0)),
            pl.BlockSpec(basis.shape, lambda i, c: (0, 0)),
        ],
        out_specs=[pl.BlockSpec((r, windows, tile), lambda i, c: (0, 0, i)) for r in rows]
        + [pl.BlockSpec((tile, width), lambda i, c: (i, 0))],
        scratch_shapes=[
            pltpu.VMEM((tile // CH_BLK, windows * bins2, CH_BLK), jnp.float32),
            pltpu.VMEM((windows, tile), jnp.float32),
        ],
    )
    flops = 2 * channels * windows * 3 * (2 * width) * bins2 * 2
    *parts, f1 = pl.pallas_call(
        front_kernel,
        grid_spec=grid_spec,
        out_shape=[jax.ShapeDtypeStruct((r, windows, channels), jnp.bfloat16) for r in rows]
        + [jax.ShapeDtypeStruct((channels, width), jnp.bfloat16)],
        compiler_params=pltpu.CompilerParams(
            dimension_semantics=("arbitrary",), vmem_limit_bytes=48 * 1024 * 1024
        ),
        cost_estimate=pl.CostEstimate(
            flops=flops,
            bytes_accessed=channels * length * 2 + bins2 * windows * channels * 2,
            transcendentals=channels * windows,
        ),
    )(kept_count, recording, toep, basis)
    return fill_first_window(parts, recording, tail_rows, f1, toep, basis, kept_count)


def stack_kernel_for(half_blocks, pb_ref, kw_ref, am_ref, ap_ref, bm_ref, bp_ref, *rest):
    o_ref = rest[-1]
    sections = kw_ref.shape[0]
    total = kw_ref[0]
    for s in range(1, sections):
        total = total + kw_ref[s]
    scale = 1.0 / jnp.sqrt(jnp.full((1, 1), total, jnp.int32).astype(jnp.float32))
    segs, bins, _, wins, blk = am_ref.shape
    p = pl.program_id(0)
    mine = lax.axis_index("pair")
    left_mine = pb_ref[p, 0] // half_blocks == mine
    right_mine = pb_ref[p, 1] // half_blocks == mine

    def one_bin(jl, carry):
        left = jnp.where(left_mine, am_ref[:, jl], ap_ref[:, jl]).reshape(segs * 2 * wins, blk)
        right = jnp.where(right_mine, bm_ref[:, jl], bp_ref[:, jl])
        swapped = jnp.concatenate([right[:, 1:2], -right[:, 0:1]], axis=1)
        rhs = jnp.concatenate(
            [right.reshape(segs * 2 * wins, blk), swapped.reshape(segs * 2 * wins, blk)], axis=1
        )
        out = lax.dot_general(
            left, rhs, (((0,), (0,)), ((), ())), preferred_element_type=jnp.float32
        )
        o_ref[0, jl, 0] = out[:, :blk] * scale
        o_ref[0, jl, 1] = out[:, blk:] * scale
        return carry

    lax.fori_loop(0, bins, one_bin, 0, unroll=True)


def stack_pairs(local, partner, pair_blocks, kept_windows, chunk, all_bins, previous=None):
    segs, bins, two, wins, chans = local.shape
    blocks_per_half = chans // CH_BLK
    npairs = pair_blocks.shape[0]

    def left_map(p, pb, kw):
        return (0, 0, 0, 0, pb[p, 0] % blocks_per_half)

    def right_map(p, pb, kw):
        return (0, 0, 0, 0, pb[p, 1] % blocks_per_half)

    block = (segs, bins, two, wins, CH_BLK)
    in_specs = [pl.BlockSpec(block, left_map)] * 2 + [pl.BlockSpec(block, right_map)] * 2
    operands = [pair_blocks, kept_windows, local, partner, local, partner]
    aliases = {}
    if previous is not None:
        in_specs.append(pl.BlockSpec(memory_space=pl.ANY))
        operands.append(previous)
        aliases = {6: 0}
    grid_spec = pltpu.PrefetchScalarGridSpec(
        num_scalar_prefetch=2,
        grid=(npairs,),
        in_specs=in_specs,
        out_specs=pl.BlockSpec(
            (1, bins, 2, CH_BLK, CH_BLK), lambda p, pb, kw: (p, chunk, 0, 0, 0)
        ),
    )
    flops = 2 * npairs * bins * CH_BLK * (2 * CH_BLK) * (segs * two * wins)
    out_bytes = npairs * bins * 2 * CH_BLK * CH_BLK * 4
    in_bytes = 4 * npairs * segs * bins * two * wins * CH_BLK * 2
    return pl.pallas_call(
        functools.partial(stack_kernel_for, blocks_per_half),
        grid_spec=grid_spec,
        out_shape=jax.ShapeDtypeStruct((npairs, all_bins, 2, CH_BLK, CH_BLK), jnp.float32),
        input_output_aliases=aliases,
        compiler_params=pltpu.CompilerParams(
            dimension_semantics=("arbitrary",), vmem_limit_bytes=48 * 1024 * 1024
        ),
        cost_estimate=pl.CostEstimate(
            flops=flops, bytes_accessed=out_bytes + in_bytes, transcendentals=0
        ),
    )(*operands)


def per_device(recording, fir_taps, kept_windows, pair_blocks):
    channels, length = recording.shape
    width = fir_taps.shape[0]
    sections = lax.axis_size("tm")
    tail_rows = from_behind(recording[:, length - width :], "tm", 1)
    windows_dev = length // WIN
    bins_dev = NF // sections
    small = max(bins_dev // 2, 1)
    chunks = [0, bins_dev - small, bins_dev] if bins_dev > 1 else [0, bins_dev]
    whitened = whiten_front(recording, tail_rows, fir_taps, kept_windows, chunks)
    result = None
    for lo, hi, part in zip(chunks[:-1], chunks[1:], whitened):
        outgoing = part.reshape(sections, hi - lo, 2, windows_dev, channels)
        by_freq = lax.all_to_all(outgoing, "tm", split_axis=0, concat_axis=0, tiled=True)
        partner = lax.ppermute(by_freq, "pair", [(0, 1), (1, 0)])
        result = stack_pairs(
            by_freq, partner, pair_blocks, kept_windows, lo // (hi - lo), bins_dev, result
        )
    return result


def solution(mesh):
    placed = (P(("groups", "pair"), "tm"), P(), P("groups"), P(("groups", "pair"), None))
    return jax.shard_map(
        per_device,
        mesh=mesh,
        in_specs=placed,
        out_specs=P(("groups", "pair"), "tm", None, None, None),
        check_vma=False,
    )
```

```python
import functools
import math

import jax
import jax.numpy as jnp
import ml_dtypes
import numpy as np
from jax import lax
from jax.experimental import pallas as pl
from jax.experimental.pallas import tpu as pltpu
from jax.sharding import PartitionSpec as P

CH_BLK = 128
WIN = 512
NF = 128
FLO = 8


whiten_eps = 1e-06


def from_behind(array, axis, by):
    count = lax.axis_size(axis)
    pairs = [(i, i + by) for i in range(count) if 0 <= i + by < count]
    return lax.ppermute(array, axis, pairs)


def exchange(outgoing, axis):
    count = lax.axis_size(axis)
    me = lax.axis_index(axis)
    pieces = [lax.dynamic_index_in_dim(outgoing, me, 0, keepdims=False)]
    for shift in range(1, count):
        piece = lax.dynamic_index_in_dim(outgoing, (me + shift) % count, 0, keepdims=False)
        pairs = [(i, (i + shift) % count) for i in range(count)]
        pieces.append(lax.ppermute(piece, axis, pairs))
    return jnp.stack(pieces)


def toeplitz(fir_taps):
    length = fir_taps.shape[0]
    reversed_taps = fir_taps[::-1]
    base_column = jnp.concatenate(
        [jnp.zeros((1,), fir_taps.dtype), reversed_taps, jnp.zeros((length,), fir_taps.dtype)]
    )
    flattened = jnp.tile(base_column, length)[: 2 * length * length]
    return flattened.reshape(length, 2 * length).T


def bandpass(recording, fir_taps, tail_rows):
    channels, length = recording.shape
    width = fir_taps.shape[0]
    current = recording.reshape(channels, length // width, width)
    previous = jnp.concatenate([tail_rows[:, None, :], current[:, :-1, :]], axis=1)
    extended = jnp.concatenate([previous, current], axis=2).reshape(
        channels * (length // width), 2 * width
    )
    product = jnp.dot(extended, toeplitz(fir_taps), preferred_element_type=jnp.float32)
    return product.reshape(channels, length).astype(jnp.bfloat16)


def dft_table(length, bins, lowest):
    samples = np.arange(length, dtype=np.int64)
    indices = lowest + np.arange(bins, dtype=np.int64)
    phase = (samples[:, None] * indices[None, :] % length).astype(np.float64) * (
        2.0 * math.pi / length
    )
    basis_table = np.stack([np.cos(phase), -np.sin(phase)], axis=2)
    return basis_table.reshape(length, 2 * bins).astype(ml_dtypes.bfloat16)


def front_kernel(cnt_ref, rec_ref, toep_ref, basis_ref, *rest):
    outs, f1_ref, (scr_ref, inv_ref) = rest[:-3], rest[-3], rest[-2:]
    tile, length = rec_ref.shape
    width = toep_ref.shape[1]
    bins2 = basis_ref.shape[1]
    windows = length // WIN
    toep = toep_ref[...]
    basis = basis_ref[...]
    count = cnt_ref[lax.axis_index("tm")]
    f1_ref[...] = jnp.dot(
        rec_ref[:, 0 : 2 * width], toep, preferred_element_type=jnp.float32
    ).astype(jnp.bfloat16)
    for h in range(tile // CH_BLK):
        scr_ref[h, pl.ds(0, bins2), :] = jnp.zeros((bins2, CH_BLK), jnp.float32)
    inv_ref[pl.ds(0, 1), :] = jnp.zeros((1, tile), jnp.float32)
    for w in range(1, windows):
        ext0 = rec_ref[:, WIN * w - width : WIN * w + width]
        ext1 = rec_ref[:, WIN * w : WIN * w + 2 * width]
        f0 = jnp.dot(ext0, toep, preferred_element_type=jnp.float32).astype(jnp.bfloat16)
        f1 = jnp.dot(ext1, toep, preferred_element_type=jnp.float32).astype(jnp.bfloat16)
        spec = jnp.dot(
            jnp.concatenate([f0, f1], axis=1), basis, preferred_element_type=jnp.float32
        ).T
        for h in range(tile // CH_BLK):
            scr_ref[h, pl.ds(bins2 * w, bins2), :] = spec[:, CH_BLK * h : CH_BLK * (h + 1)]
        power = jnp.sum(spec * spec, axis=0, keepdims=True) * (1.0 / bins2)
        keep = jnp.where(count > w, 1.0, 0.0).astype(jnp.float32)
        inv_ref[pl.ds(w, 1), :] = lax.rsqrt(power + whiten_eps) * keep
    scales = inv_ref[...]

    start = 0
    for o_ref in outs:

        def one_row(k, carry, o_ref=o_ref, start=start):
            for h in range(tile // CH_BLK):
                rows = scr_ref[h, pl.ds(start + k, windows, stride=bins2), :]
                part = rows * scales[:, CH_BLK * h : CH_BLK * (h + 1)]
                o_ref[k, :, CH_BLK * h : CH_BLK * (h + 1)] = part.astype(o_ref.dtype)
            return carry

        lax.fori_loop(0, o_ref.shape[0], one_row, 0, unroll=16)
        start += o_ref.shape[0]


def first_window_kernel(count_parts, cnt_ref, tail_ref, rec_ref, f1_ref, toep_ref, basis_ref, *rest):
    ins, outs, w0_ref = rest[:count_parts], rest[count_parts : 2 * count_parts], rest[-1]
    bins2 = basis_ref.shape[1]
    count = cnt_ref[lax.axis_index("tm")]
    ext0 = jnp.concatenate([tail_ref[...], rec_ref[...]], axis=1)
    f0 = jnp.dot(ext0, toep_ref[...], preferred_element_type=jnp.float32).astype(jnp.bfloat16)
    spec = jnp.dot(
        jnp.concatenate([f0, f1_ref[...]], axis=1), basis_ref[...], preferred_element_type=jnp.float32
    ).T
    power = jnp.sum(spec * spec, axis=0, keepdims=True) * (1.0 / bins2)
    keep = jnp.where(count > 0, 1.0, 0.0).astype(jnp.float32)
    w0_ref[...] = spec * (lax.rsqrt(power + whiten_eps) * keep)
    start = 0
    for i_ref, o_ref in zip(ins, outs):

        def one_row(k, carry, i_ref=i_ref, o_ref=o_ref, start=start):
            held = i_ref[k]
            first = w0_ref[pl.ds(start + k, 1), :].astype(held.dtype)
            rowid = lax.broadcasted_iota(jnp.int32, held.shape, 0)
            o_ref[k] = jnp.where(rowid == 0, first, held)
            return carry

        lax.fori_loop(0, o_ref.shape[0], one_row, 0, unroll=8)
        start += o_ref.shape[0]


def fill_first_window(parts, recording, tail_rows, f1, toep, basis, kept_count):
    channels, width = tail_rows.shape
    bins2 = basis.shape[1]
    count_parts = len(parts)
    full = lambda shape: pl.BlockSpec(shape, lambda i, c: (0,) * len(shape))
    grid_spec = pltpu.PrefetchScalarGridSpec(
        num_scalar_prefetch=1,
        grid=(1,),
        in_specs=[
            full(tail_rows.shape),
            pl.BlockSpec((channels, width), lambda i, c: (0, 0)),
            full(f1.shape),
            full(toep.shape),
            full(basis.shape),
        ]
        + [full(p.shape) for p in parts],
        out_specs=[full(p.shape) for p in parts],
        scratch_shapes=[pltpu.VMEM((bins2, channels), jnp.float32)],
    )
    return pl.pallas_call(
        functools.partial(first_window_kernel, count_parts),
        grid_spec=grid_spec,
        out_shape=[jax.ShapeDtypeStruct(p.shape, p.dtype) for p in parts],
        input_output_aliases={6 + i: i for i in range(count_parts)},
        compiler_params=pltpu.CompilerParams(
            dimension_semantics=("arbitrary",), vmem_limit_bytes=48 * 1024 * 1024
        ),
        cost_estimate=pl.CostEstimate(
            flops=2 * channels * 3 * (2 * width) * bins2,
            bytes_accessed=4 * sum(p.size for p in parts),
            transcendentals=channels,
        ),
    )(kept_count, tail_rows, recording, f1, toep, basis, *parts)


def whiten_front(recording, tail_rows, fir_taps, kept_count, chunks, tile=512):
    channels, length = recording.shape
    width = tail_rows.shape[1]
    windows = length // WIN
    toep = toeplitz(fir_taps)
    sections = lax.axis_size("tm")
    bins_dev = NF // sections
    basis = dft_table(WIN, NF, FLO).reshape(WIN, sections, bins_dev, 2)
    basis = np.concatenate(
        [basis[:, :, lo:hi].reshape(WIN, -1) for lo, hi in zip(chunks[:-1], chunks[1:])], axis=1
    )
    basis = jnp.asarray(basis)
    bins2 = basis.shape[1]
    rows = [sections * (hi - lo) * 2 for lo, hi in zip(chunks[:-1], chunks[1:])]
    grid_spec = pltpu.PrefetchScalarGridSpec(
        num_scalar_prefetch=1,
        grid=(channels // tile,),
        in_specs=[
            pl.BlockSpec((tile, length), lambda i, c: (i, 0)),
            pl.BlockSpec(toep.shape, lambda i, c: (0, 0)),
            pl.BlockSpec(basis.shape, lambda i, c: (0, 0)),
        ],
        out_specs=[pl.BlockSpec((r, windows, tile), lambda i, c: (0, 0, i)) for r in rows]
        + [pl.BlockSpec((tile, width), lambda i, c: (i, 0))],
        scratch_shapes=[
            pltpu.VMEM((tile // CH_BLK, windows * bins2, CH_BLK), jnp.float32),
            pltpu.VMEM((windows, tile), jnp.float32),
        ],
    )
    flops = 2 * channels * windows * 3 * (2 * width) * bins2 * 2
    *parts, f1 = pl.pallas_call(
        front_kernel,
        grid_spec=grid_spec,
        out_shape=[jax.ShapeDtypeStruct((r, windows, channels), jnp.bfloat16) for r in rows]
        + [jax.ShapeDtypeStruct((channels, width), jnp.bfloat16)],
        compiler_params=pltpu.CompilerParams(
            dimension_semantics=("arbitrary",), vmem_limit_bytes=48 * 1024 * 1024
        ),
        cost_estimate=pl.CostEstimate(
            flops=flops,
            bytes_accessed=channels * length * 2 + bins2 * windows * channels * 2,
            transcendentals=channels * windows,
        ),
    )(kept_count, recording, toep, basis)
    return fill_first_window(parts, recording, tail_rows, f1, toep, basis, kept_count)


def stack_kernel_for(half_blocks, pb_ref, kw_ref, am_ref, ap_ref, bm_ref, bp_ref, *rest):
    o_ref = rest[-1]
    sections = kw_ref.shape[0]
    total = kw_ref[0]
    for s in range(1, sections):
        total = total + kw_ref[s]
    scale = 1.0 / jnp.sqrt(jnp.full((1, 1), total, jnp.int32).astype(jnp.float32))
    segs, bins, _, wins, blk = am_ref.shape
    p = pl.program_id(0)
    mine = lax.axis_index("pair")
    left_mine = pb_ref[p, 0] // half_blocks == mine
    right_mine = pb_ref[p, 1] // half_blocks == mine

    def one_bin(jl, carry):
        left = jnp.where(left_mine, am_ref[:, jl], ap_ref[:, jl]).reshape(segs * 2 * wins, blk)
        right = jnp.where(right_mine, bm_ref[:, jl], bp_ref[:, jl])
        swapped = jnp.concatenate([right[:, 1:2], -right[:, 0:1]], axis=1)
        rhs = jnp.concatenate(
            [right.reshape(segs * 2 * wins, blk), swapped.reshape(segs * 2 * wins, blk)], axis=1
        )
        out = lax.dot_general(
            left, rhs, (((0,), (0,)), ((), ())), preferred_element_type=jnp.float32
        )
        o_ref[0, jl, 0] = out[:, :blk] * scale
        o_ref[0, jl, 1] = out[:, blk:] * scale
        return carry

    lax.fori_loop(0, bins, one_bin, 0, unroll=True)


def stack_pairs(local, partner, pair_blocks, kept_windows, chunk, all_bins, previous=None):
    segs, bins, two, wins, chans = local.shape
    blocks_per_half = chans // CH_BLK
    npairs = pair_blocks.shape[0]

    def left_map(p, pb, kw):
        return (0, 0, 0, 0, pb[p, 0] % blocks_per_half)

    def right_map(p, pb, kw):
        return (0, 0, 0, 0, pb[p, 1] % blocks_per_half)

    block = (segs, bins, two, wins, CH_BLK)
    in_specs = [pl.BlockSpec(block, left_map)] * 2 + [pl.BlockSpec(block, right_map)] * 2
    operands = [pair_blocks, kept_windows, local, partner, local, partner]
    aliases = {}
    if previous is not None:
        in_specs.append(pl.BlockSpec(memory_space=pl.ANY))
        operands.append(previous)
        aliases = {6: 0}
    grid_spec = pltpu.PrefetchScalarGridSpec(
        num_scalar_prefetch=2,
        grid=(npairs,),
        in_specs=in_specs,
        out_specs=pl.BlockSpec(
            (1, bins, 2, CH_BLK, CH_BLK), lambda p, pb, kw: (p, chunk, 0, 0, 0)
        ),
    )
    flops = 2 * npairs * bins * CH_BLK * (2 * CH_BLK) * (segs * two * wins)
    out_bytes = npairs * bins * 2 * CH_BLK * CH_BLK * 4
    in_bytes = 4 * npairs * segs * bins * two * wins * CH_BLK * 2
    return pl.pallas_call(
        functools.partial(stack_kernel_for, blocks_per_half),
        grid_spec=grid_spec,
        out_shape=jax.ShapeDtypeStruct((npairs, all_bins, 2, CH_BLK, CH_BLK), jnp.float32),
        input_output_aliases=aliases,
        compiler_params=pltpu.CompilerParams(
            dimension_semantics=("arbitrary",), vmem_limit_bytes=67043328
        ),
        cost_estimate=pl.CostEstimate(
            flops=flops, bytes_accessed=out_bytes + in_bytes, transcendentals=0
        ),
    )(*operands)


def per_device(recording, fir_taps, kept_windows, pair_blocks):
    channels, length = recording.shape
    width = fir_taps.shape[0]
    sections = lax.axis_size("tm")
    tail_rows = from_behind(recording[:, length - width :], "tm", 1)
    windows_dev = length // WIN
    bins_dev = NF // sections
    small = max(bins_dev // 2, 1)
    chunks = [0, bins_dev - small, bins_dev] if bins_dev > 1 else [0, bins_dev]
    whitened = whiten_front(recording, tail_rows, fir_taps, kept_windows, chunks)
    result = None
    for lo, hi, part in zip(chunks[:-1], chunks[1:], whitened):
        outgoing = part.reshape(sections, hi - lo, 2, windows_dev, channels)
        by_freq = lax.all_to_all(outgoing, "tm", split_axis=0, concat_axis=0, tiled=True)
        partner = lax.ppermute(by_freq, "pair", [(0, 1), (1, 0)])
        result = stack_pairs(
            by_freq, partner, pair_blocks, kept_windows, lo // (hi - lo), bins_dev, result
        )
    return result


def solution(mesh):
    placed = (P(("groups", "pair"), "tm"), P(), P("groups"), P(("groups", "pair"), None))
    return jax.shard_map(
        per_device,
        mesh=mesh,
        in_specs=placed,
        out_specs=P(("groups", "pair"), "tm", None, None, None),
        check_vma=False,
    )
```

```python
import functools
import math

import jax
import jax.numpy as jnp
import ml_dtypes
import numpy as np
from jax import lax
from jax.experimental import pallas as pl
from jax.experimental.pallas import tpu as pltpu
from jax.sharding import PartitionSpec as P

CH_BLK = 128
WIN = 512
NF = 128
FLO = 8


whiten_eps = 1e-06


def from_behind(array, axis, by):
    count = lax.axis_size(axis)
    pairs = [(i, i + by) for i in range(count) if 0 <= i + by < count]
    return lax.ppermute(array, axis, pairs)


def exchange(outgoing, axis):
    count = lax.axis_size(axis)
    me = lax.axis_index(axis)
    pieces = [lax.dynamic_index_in_dim(outgoing, me, 0, keepdims=False)]
    for shift in range(1, count):
        piece = lax.dynamic_index_in_dim(outgoing, (me + shift) % count, 0, keepdims=False)
        pairs = [(i, (i + shift) % count) for i in range(count)]
        pieces.append(lax.ppermute(piece, axis, pairs))
    return jnp.stack(pieces)


def toeplitz(fir_taps):
    length = fir_taps.shape[0]
    reversed_taps = fir_taps[::-1]
    base_column = jnp.concatenate(
        [jnp.zeros((1,), fir_taps.dtype), reversed_taps, jnp.zeros((length,), fir_taps.dtype)]
    )
    flattened = jnp.tile(base_column, length)[: 2 * length * length]
    return flattened.reshape(length, 2 * length).T


def bandpass(recording, fir_taps, tail_rows):
    channels, length = recording.shape
    width = fir_taps.shape[0]
    current = recording.reshape(channels, length // width, width)
    previous = jnp.concatenate([tail_rows[:, None, :], current[:, :-1, :]], axis=1)
    extended = jnp.concatenate([previous, current], axis=2).reshape(
        channels * (length // width), 2 * width
    )
    product = jnp.dot(extended, toeplitz(fir_taps), preferred_element_type=jnp.float32)
    return product.reshape(channels, length).astype(jnp.bfloat16)


def dft_table(length, bins, lowest):
    samples = np.arange(length, dtype=np.int64)
    indices = lowest + np.arange(bins, dtype=np.int64)
    phase = (samples[:, None] * indices[None, :] % length).astype(np.float64) * (
        2.0 * math.pi / length
    )
    basis_table = np.stack([np.cos(phase), -np.sin(phase)], axis=2)
    return basis_table.reshape(length, 2 * bins).astype(ml_dtypes.bfloat16)


def front_kernel(cnt_ref, rec_ref, toep_ref, basis_ref, *rest):
    outs, f1_ref, (scr_ref, inv_ref) = rest[:-3], rest[-3], rest[-2:]
    tile, length = rec_ref.shape
    width = toep_ref.shape[1]
    bins2 = basis_ref.shape[1]
    windows = length // WIN
    toep = toep_ref[...]
    basis = basis_ref[...]
    count = cnt_ref[lax.axis_index("tm")]
    f1_ref[...] = jnp.dot(
        rec_ref[:, 0 : 2 * width], toep, preferred_element_type=jnp.float32
    ).astype(jnp.bfloat16)
    for h in range(tile // CH_BLK):
        scr_ref[h, pl.ds(0, bins2), :] = jnp.zeros((bins2, CH_BLK), jnp.float32)
    inv_ref[pl.ds(0, 1), :] = jnp.zeros((1, tile), jnp.float32)
    for w in range(1, windows):
        ext0 = rec_ref[:, WIN * w - width : WIN * w + width]
        ext1 = rec_ref[:, WIN * w : WIN * w + 2 * width]
        f0 = jnp.dot(ext0, toep, preferred_element_type=jnp.float32).astype(jnp.bfloat16)
        f1 = jnp.dot(ext1, toep, preferred_element_type=jnp.float32).astype(jnp.bfloat16)
        spec = jnp.dot(
            jnp.concatenate([f0, f1], axis=1), basis, preferred_element_type=jnp.float32
        ).T
        for h in range(tile // CH_BLK):
            scr_ref[h, pl.ds(bins2 * w, bins2), :] = spec[:, CH_BLK * h : CH_BLK * (h + 1)]
        power = jnp.sum(spec * spec, axis=0, keepdims=True) * (1.0 / bins2)
        keep = jnp.where(count > w, 1.0, 0.0).astype(jnp.float32)
        inv_ref[pl.ds(w, 1), :] = lax.rsqrt(power + whiten_eps) * keep
    scales = inv_ref[...]

    start = 0
    for o_ref in outs:

        def one_row(k, carry, o_ref=o_ref, start=start):
            for h in range(tile // CH_BLK):
                rows = scr_ref[h, pl.ds(start + k, windows, stride=bins2), :]
                part = rows * scales[:, CH_BLK * h : CH_BLK * (h + 1)]
                o_ref[k, :, CH_BLK * h : CH_BLK * (h + 1)] = part.astype(o_ref.dtype)
            return carry

        lax.fori_loop(0, o_ref.shape[0], one_row, 0, unroll=32)
        start += o_ref.shape[0]


def first_window_kernel(count_parts, cnt_ref, tail_ref, rec_ref, f1_ref, toep_ref, basis_ref, *rest):
    ins, outs, w0_ref = rest[:count_parts], rest[count_parts : 2 * count_parts], rest[-1]
    bins2 = basis_ref.shape[1]
    count = cnt_ref[lax.axis_index("tm")]
    ext0 = jnp.concatenate([tail_ref[...], rec_ref[...]], axis=1)
    f0 = jnp.dot(ext0, toep_ref[...], preferred_element_type=jnp.float32).astype(jnp.bfloat16)
    spec = jnp.dot(
        jnp.concatenate([f0, f1_ref[...]], axis=1), basis_ref[...], preferred_element_type=jnp.float32
    ).T
    power = jnp.sum(spec * spec, axis=0, keepdims=True) * (1.0 / bins2)
    keep = jnp.where(count > 0, 1.0, 0.0).astype(jnp.float32)
    w0_ref[...] = spec * (lax.rsqrt(power + whiten_eps) * keep)
    start = 0
    for i_ref, o_ref in zip(ins, outs):

        def one_row(k, carry, i_ref=i_ref, o_ref=o_ref, start=start):
            held = i_ref[k]
            first = w0_ref[pl.ds(start + k, 1), :].astype(held.dtype)
            rowid = lax.broadcasted_iota(jnp.int32, held.shape, 0)
            o_ref[k] = jnp.where(rowid == 0, first, held)
            return carry

        lax.fori_loop(0, o_ref.shape[0], one_row, 0, unroll=8)
        start += o_ref.shape[0]


def fill_first_window(parts, recording, tail_rows, f1, toep, basis, kept_count):
    channels, width = tail_rows.shape
    bins2 = basis.shape[1]
    count_parts = len(parts)
    full = lambda shape: pl.BlockSpec(shape, lambda i, c: (0,) * len(shape))
    grid_spec = pltpu.PrefetchScalarGridSpec(
        num_scalar_prefetch=1,
        grid=(1,),
        in_specs=[
            full(tail_rows.shape),
            pl.BlockSpec((channels, width), lambda i, c: (0, 0)),
            full(f1.shape),
            full(toep.shape),
            full(basis.shape),
        ]
        + [full(p.shape) for p in parts],
        out_specs=[full(p.shape) for p in parts],
        scratch_shapes=[pltpu.VMEM((bins2, channels), jnp.float32)],
    )
    return pl.pallas_call(
        functools.partial(first_window_kernel, count_parts),
        grid_spec=grid_spec,
        out_shape=[jax.ShapeDtypeStruct(p.shape, p.dtype) for p in parts],
        input_output_aliases={6 + i: i for i in range(count_parts)},
        compiler_params=pltpu.CompilerParams(
            dimension_semantics=("arbitrary",), vmem_limit_bytes=48 * 1024 * 1024
        ),
        cost_estimate=pl.CostEstimate(
            flops=2 * channels * 3 * (2 * width) * bins2,
            bytes_accessed=4 * sum(p.size for p in parts),
            transcendentals=channels,
        ),
    )(kept_count, tail_rows, recording, f1, toep, basis, *parts)


def whiten_front(recording, tail_rows, fir_taps, kept_count, chunks, tile=512):
    channels, length = recording.shape
    width = tail_rows.shape[1]
    windows = length // WIN
    toep = toeplitz(fir_taps)
    sections = lax.axis_size("tm")
    bins_dev = NF // sections
    basis = dft_table(WIN, NF, FLO).reshape(WIN, sections, bins_dev, 2)
    basis = np.concatenate(
        [basis[:, :, lo:hi].reshape(WIN, -1) for lo, hi in zip(chunks[:-1], chunks[1:])], axis=1
    )
    basis = jnp.asarray(basis)
    bins2 = basis.shape[1]
    rows = [sections * (hi - lo) * 2 for lo, hi in zip(chunks[:-1], chunks[1:])]
    grid_spec = pltpu.PrefetchScalarGridSpec(
        num_scalar_prefetch=1,
        grid=(channels // tile,),
        in_specs=[
            pl.BlockSpec((tile, length), lambda i, c: (i, 0)),
            pl.BlockSpec(toep.shape, lambda i, c: (0, 0)),
            pl.BlockSpec(basis.shape, lambda i, c: (0, 0)),
        ],
        out_specs=[pl.BlockSpec((r, windows, tile), lambda i, c: (0, 0, i)) for r in rows]
        + [pl.BlockSpec((tile, width), lambda i, c: (i, 0))],
        scratch_shapes=[
            pltpu.VMEM((tile // CH_BLK, windows * bins2, CH_BLK), jnp.float32),
            pltpu.VMEM((windows, tile), jnp.float32),
        ],
    )
    flops = 2 * channels * windows * 3 * (2 * width) * bins2 * 2
    *parts, f1 = pl.pallas_call(
        front_kernel,
        grid_spec=grid_spec,
        out_shape=[jax.ShapeDtypeStruct((r, windows, channels), jnp.bfloat16) for r in rows]
        + [jax.ShapeDtypeStruct((channels, width), jnp.bfloat16)],
        compiler_params=pltpu.CompilerParams(
            dimension_semantics=("arbitrary",), vmem_limit_bytes=48 * 1024 * 1024
        ),
        cost_estimate=pl.CostEstimate(
            flops=flops,
            bytes_accessed=channels * length * 2 + bins2 * windows * channels * 2,
            transcendentals=channels * windows,
        ),
    )(kept_count, recording, toep, basis)
    return fill_first_window(parts, recording, tail_rows, f1, toep, basis, kept_count)


def stack_kernel_for(half_blocks, pb_ref, kw_ref, am_ref, ap_ref, bm_ref, bp_ref, *rest):
    o_ref = rest[-1]
    sections = kw_ref.shape[0]
    total = kw_ref[0]
    for s in range(1, sections):
        total = total + kw_ref[s]
    scale = 1.0 / jnp.sqrt(jnp.full((1, 1), total, jnp.int32).astype(jnp.float32))
    segs, bins, _, wins, blk = am_ref.shape
    p = pl.program_id(0)
    mine = lax.axis_index("pair")
    left_mine = pb_ref[p, 0] // half_blocks == mine
    right_mine = pb_ref[p, 1] // half_blocks == mine

    def one_bin(jl, carry):
        left = jnp.where(left_mine, am_ref[:, jl], ap_ref[:, jl]).reshape(segs * 2 * wins, blk)
        right = jnp.where(right_mine, bm_ref[:, jl], bp_ref[:, jl])
        swapped = jnp.concatenate([right[:, 1:2], -right[:, 0:1]], axis=1)
        rhs = jnp.concatenate(
            [right.reshape(segs * 2 * wins, blk), swapped.reshape(segs * 2 * wins, blk)], axis=1
        )
        out = lax.dot_general(
            left, rhs, (((0,), (0,)), ((), ())), preferred_element_type=jnp.float32
        )
        o_ref[0, jl, 0] = out[:, :blk] * scale
        o_ref[0, jl, 1] = out[:, blk:] * scale
        return carry

    lax.fori_loop(0, bins, one_bin, 0, unroll=True)


def stack_pairs(local, partner, pair_blocks, kept_windows, chunk, all_bins, previous=None):
    segs, bins, two, wins, chans = local.shape
    blocks_per_half = chans // CH_BLK
    npairs = pair_blocks.shape[0]

    def left_map(p, pb, kw):
        return (0, 0, 0, 0, pb[p, 0] % blocks_per_half)

    def right_map(p, pb, kw):
        return (0, 0, 0, 0, pb[p, 1] % blocks_per_half)

    block = (segs, bins, two, wins, CH_BLK)
    in_specs = [pl.BlockSpec(block, left_map)] * 2 + [pl.BlockSpec(block, right_map)] * 2
    operands = [pair_blocks, kept_windows, local, partner, local, partner]
    aliases = {}
    if previous is not None:
        in_specs.append(pl.BlockSpec(memory_space=pl.ANY))
        operands.append(previous)
        aliases = {6: 0}
    grid_spec = pltpu.PrefetchScalarGridSpec(
        num_scalar_prefetch=2,
        grid=(npairs,),
        in_specs=in_specs,
        out_specs=pl.BlockSpec(
            (1, bins, 2, CH_BLK, CH_BLK), lambda p, pb, kw: (p, chunk, 0, 0, 0)
        ),
    )
    flops = 2 * npairs * bins * CH_BLK * (2 * CH_BLK) * (segs * two * wins)
    out_bytes = npairs * bins * 2 * CH_BLK * CH_BLK * 4
    in_bytes = 4 * npairs * segs * bins * two * wins * CH_BLK * 2
    return pl.pallas_call(
        functools.partial(stack_kernel_for, blocks_per_half),
        grid_spec=grid_spec,
        out_shape=jax.ShapeDtypeStruct((npairs, all_bins, 2, CH_BLK, CH_BLK), jnp.float32),
        input_output_aliases=aliases,
        compiler_params=pltpu.CompilerParams(
            dimension_semantics=("arbitrary",), vmem_limit_bytes=48 * 1024 * 1024
        ),
        cost_estimate=pl.CostEstimate(
            flops=flops, bytes_accessed=out_bytes + in_bytes, transcendentals=0
        ),
    )(*operands)


def per_device(recording, fir_taps, kept_windows, pair_blocks):
    channels, length = recording.shape
    width = fir_taps.shape[0]
    sections = lax.axis_size("tm")
    tail_rows = from_behind(recording[:, length - width :], "tm", 1)
    windows_dev = length // WIN
    bins_dev = NF // sections
    small = max(bins_dev // 2, 1)
    chunks = [0, bins_dev - small, bins_dev] if bins_dev > 1 else [0, bins_dev]
    whitened = whiten_front(recording, tail_rows, fir_taps, kept_windows, chunks)
    result = None
    for lo, hi, part in zip(chunks[:-1], chunks[1:], whitened):
        outgoing = part.reshape(sections, hi - lo, 2, windows_dev, channels)
        by_freq = lax.all_to_all(outgoing, "tm", split_axis=0, concat_axis=0, tiled=True)
        partner = lax.ppermute(by_freq, "pair", [(0, 1), (1, 0)])
        result = stack_pairs(
            by_freq, partner, pair_blocks, kept_windows, lo // (hi - lo), bins_dev, result
        )
    return result


def solution(mesh):
    placed = (P(("groups", "pair"), "tm"), P(), P("groups"), P(("groups", "pair"), None))
    return jax.shard_map(
        per_device,
        mesh=mesh,
        in_specs=placed,
        out_specs=P(("groups", "pair"), "tm", None, None, None),
        check_vma=False,
    )
```

```python
import functools
import math

import jax
import jax.numpy as jnp
import ml_dtypes
import numpy as np
from jax import lax
from jax.experimental import pallas as pl
from jax.experimental.pallas import tpu as pltpu
from jax.sharding import PartitionSpec as P

CH_BLK = 128
WIN = 512
NF = 128
FLO = 8


whiten_eps = 1e-06


def from_behind(array, axis, by):
    count = lax.axis_size(axis)
    pairs = [(i, i + by) for i in range(count) if 0 <= i + by < count]
    return lax.ppermute(array, axis, pairs)


def exchange(outgoing, axis):
    count = lax.axis_size(axis)
    me = lax.axis_index(axis)
    pieces = [lax.dynamic_index_in_dim(outgoing, me, 0, keepdims=False)]
    for shift in range(1, count):
        piece = lax.dynamic_index_in_dim(outgoing, (me + shift) % count, 0, keepdims=False)
        pairs = [(i, (i + shift) % count) for i in range(count)]
        pieces.append(lax.ppermute(piece, axis, pairs))
    return jnp.stack(pieces)


def toeplitz(fir_taps):
    length = fir_taps.shape[0]
    reversed_taps = fir_taps[::-1]
    base_column = jnp.concatenate(
        [jnp.zeros((1,), fir_taps.dtype), reversed_taps, jnp.zeros((length,), fir_taps.dtype)]
    )
    flattened = jnp.tile(base_column, length)[: 2 * length * length]
    return flattened.reshape(length, 2 * length).T


def bandpass(recording, fir_taps, tail_rows):
    channels, length = recording.shape
    width = fir_taps.shape[0]
    current = recording.reshape(channels, length // width, width)
    previous = jnp.concatenate([tail_rows[:, None, :], current[:, :-1, :]], axis=1)
    extended = jnp.concatenate([previous, current], axis=2).reshape(
        channels * (length // width), 2 * width
    )
    product = jnp.dot(extended, toeplitz(fir_taps), preferred_element_type=jnp.float32)
    return product.reshape(channels, length).astype(jnp.bfloat16)


def dft_table(length, bins, lowest):
    samples = np.arange(length, dtype=np.int64)
    indices = lowest + np.arange(bins, dtype=np.int64)
    phase = (samples[:, None] * indices[None, :] % length).astype(np.float64) * (
        2.0 * math.pi / length
    )
    basis_table = np.stack([np.cos(phase), -np.sin(phase)], axis=2)
    return basis_table.reshape(length, 2 * bins).astype(ml_dtypes.bfloat16)


def front_kernel(cnt_ref, rec_ref, toep_ref, basis_ref, *rest):
    outs, f1_ref, (scr_ref, inv_ref) = rest[:-3], rest[-3], rest[-2:]
    tile, length = rec_ref.shape
    width = toep_ref.shape[1]
    bins2 = basis_ref.shape[1]
    windows = length // WIN
    toep = toep_ref[...]
    basis = basis_ref[...]
    count = cnt_ref[lax.axis_index("tm")]
    f1_ref[...] = jnp.dot(
        rec_ref[:, 0 : 2 * width], toep, preferred_element_type=jnp.float32
    ).astype(jnp.bfloat16)
    for h in range(tile // CH_BLK):
        scr_ref[h, pl.ds(0, bins2), :] = jnp.zeros((bins2, CH_BLK), jnp.float32)
    inv_ref[pl.ds(0, 1), :] = jnp.zeros((1, tile), jnp.float32)
    for w in range(1, windows):
        ext0 = rec_ref[:, WIN * w - width : WIN * w + width]
        ext1 = rec_ref[:, WIN * w : WIN * w + 2 * width]
        f0 = jnp.dot(ext0, toep, preferred_element_type=jnp.float32).astype(jnp.bfloat16)
        f1 = jnp.dot(ext1, toep, preferred_element_type=jnp.float32).astype(jnp.bfloat16)
        spec = jnp.dot(
            jnp.concatenate([f0, f1], axis=1), basis, preferred_element_type=jnp.float32
        ).T
        for h in range(tile // CH_BLK):
            scr_ref[h, pl.ds(bins2 * w, bins2), :] = spec[:, CH_BLK * h : CH_BLK * (h + 1)]
        power = jnp.sum(spec * spec, axis=0, keepdims=True) * (1.0 / bins2)
        keep = jnp.where(count > w, 1.0, 0.0).astype(jnp.float32)
        inv_ref[pl.ds(w, 1), :] = lax.rsqrt(power + whiten_eps) * keep
    scales = inv_ref[...]

    start = 0
    for o_ref in outs:

        def one_row(k, carry, o_ref=o_ref, start=start):
            for h in range(tile // CH_BLK):
                rows = scr_ref[h, pl.ds(start + k, windows, stride=bins2), :]
                part = rows * scales[:, CH_BLK * h : CH_BLK * (h + 1)]
                o_ref[k, :, CH_BLK * h : CH_BLK * (h + 1)] = part.astype(o_ref.dtype)
            return carry

        lax.fori_loop(0, o_ref.shape[0], one_row, 0, unroll=32)
        start += o_ref.shape[0]


def first_window_kernel(count_parts, cnt_ref, tail_ref, rec_ref, f1_ref, toep_ref, basis_ref, *rest):
    ins, outs, w0_ref = rest[:count_parts], rest[count_parts : 2 * count_parts], rest[-1]
    bins2 = basis_ref.shape[1]
    count = cnt_ref[lax.axis_index("tm")]
    ext0 = jnp.concatenate([tail_ref[...], rec_ref[...]], axis=1)
    f0 = jnp.dot(ext0, toep_ref[...], preferred_element_type=jnp.float32).astype(jnp.bfloat16)
    spec = jnp.dot(
        jnp.concatenate([f0, f1_ref[...]], axis=1), basis_ref[...], preferred_element_type=jnp.float32
    ).T
    power = jnp.sum(spec * spec, axis=0, keepdims=True) * (1.0 / bins2)
    keep = jnp.where(count > 0, 1.0, 0.0).astype(jnp.float32)
    w0_ref[...] = spec * (lax.rsqrt(power + whiten_eps) * keep)
    start = 0
    for i_ref, o_ref in zip(ins, outs):

        def one_row(k, carry, i_ref=i_ref, o_ref=o_ref, start=start):
            held = i_ref[k]
            first = w0_ref[pl.ds(start + k, 1), :].astype(held.dtype)
            rowid = lax.broadcasted_iota(jnp.int32, held.shape, 0)
            o_ref[k] = jnp.where(rowid == 0, first, held)
            return carry

        lax.fori_loop(0, o_ref.shape[0], one_row, 0, unroll=32)
        start += o_ref.shape[0]


def fill_first_window(parts, recording, tail_rows, f1, toep, basis, kept_count):
    channels, width = tail_rows.shape
    bins2 = basis.shape[1]
    count_parts = len(parts)
    full = lambda shape: pl.BlockSpec(shape, lambda i, c: (0,) * len(shape))
    grid_spec = pltpu.PrefetchScalarGridSpec(
        num_scalar_prefetch=1,
        grid=(1,),
        in_specs=[
            full(tail_rows.shape),
            pl.BlockSpec((channels, width), lambda i, c: (0, 0)),
            full(f1.shape),
            full(toep.shape),
            full(basis.shape),
        ]
        + [full(p.shape) for p in parts],
        out_specs=[full(p.shape) for p in parts],
        scratch_shapes=[pltpu.VMEM((bins2, channels), jnp.float32)],
    )
    return pl.pallas_call(
        functools.partial(first_window_kernel, count_parts),
        grid_spec=grid_spec,
        out_shape=[jax.ShapeDtypeStruct(p.shape, p.dtype) for p in parts],
        input_output_aliases={6 + i: i for i in range(count_parts)},
        compiler_params=pltpu.CompilerParams(
            dimension_semantics=("arbitrary",), vmem_limit_bytes=48 * 1024 * 1024
        ),
        cost_estimate=pl.CostEstimate(
            flops=2 * channels * 3 * (2 * width) * bins2,
            bytes_accessed=4 * sum(p.size for p in parts),
            transcendentals=channels,
        ),
    )(kept_count, tail_rows, recording, f1, toep, basis, *parts)


def whiten_front(recording, tail_rows, fir_taps, kept_count, chunks, tile=512):
    channels, length = recording.shape
    width = tail_rows.shape[1]
    windows = length // WIN
    toep = toeplitz(fir_taps)
    sections = lax.axis_size("tm")
    bins_dev = NF // sections
    basis = dft_table(WIN, NF, FLO).reshape(WIN, sections, bins_dev, 2)
    basis = np.concatenate(
        [basis[:, :, lo:hi].reshape(WIN, -1) for lo, hi in zip(chunks[:-1], chunks[1:])], axis=1
    )
    basis = jnp.asarray(basis)
    bins2 = basis.shape[1]
    rows = [sections * (hi - lo) * 2 for lo, hi in zip(chunks[:-1], chunks[1:])]
    grid_spec = pltpu.PrefetchScalarGridSpec(
        num_scalar_prefetch=1,
        grid=(channels // tile,),
        in_specs=[
            pl.BlockSpec((tile, length), lambda i, c: (i, 0)),
            pl.BlockSpec(toep.shape, lambda i, c: (0, 0)),
            pl.BlockSpec(basis.shape, lambda i, c: (0, 0)),
        ],
        out_specs=[pl.BlockSpec((r, windows, tile), lambda i, c: (0, 0, i)) for r in rows]
        + [pl.BlockSpec((tile, width), lambda i, c: (i, 0))],
        scratch_shapes=[
            pltpu.VMEM((tile // CH_BLK, windows * bins2, CH_BLK), jnp.float32),
            pltpu.VMEM((windows, tile), jnp.float32),
        ],
    )
    flops = 2 * channels * windows * 3 * (2 * width) * bins2 * 2
    *parts, f1 = pl.pallas_call(
        front_kernel,
        grid_spec=grid_spec,
        out_shape=[jax.ShapeDtypeStruct((r, windows, channels), jnp.bfloat16) for r in rows]
        + [jax.ShapeDtypeStruct((channels, width), jnp.bfloat16)],
        compiler_params=pltpu.CompilerParams(
            dimension_semantics=("arbitrary",), vmem_limit_bytes=48 * 1024 * 1024
        ),
        cost_estimate=pl.CostEstimate(
            flops=flops,
            bytes_accessed=channels * length * 2 + bins2 * windows * channels * 2,
            transcendentals=channels * windows,
        ),
    )(kept_count, recording, toep, basis)
    return fill_first_window(parts, recording, tail_rows, f1, toep, basis, kept_count)


def stack_kernel_for(half_blocks, pb_ref, kw_ref, am_ref, ap_ref, bm_ref, bp_ref, *rest):
    o_ref = rest[-1]
    sections = kw_ref.shape[0]
    total = kw_ref[0]
    for s in range(1, sections):
        total = total + kw_ref[s]
    scale = 1.0 / jnp.sqrt(jnp.full((1, 1), total, jnp.int32).astype(jnp.float32))
    segs, bins, _, wins, blk = am_ref.shape
    p = pl.program_id(0)
    mine = lax.axis_index("pair")
    left_mine = pb_ref[p, 0] // half_blocks == mine
    right_mine = pb_ref[p, 1] // half_blocks == mine

    def one_bin(jl, carry):
        left = jnp.where(left_mine, am_ref[:, jl], ap_ref[:, jl]).reshape(segs * 2 * wins, blk)
        right = jnp.where(right_mine, bm_ref[:, jl], bp_ref[:, jl])
        swapped = jnp.concatenate([right[:, 1:2], -right[:, 0:1]], axis=1)
        rhs = jnp.concatenate(
            [right.reshape(segs * 2 * wins, blk), swapped.reshape(segs * 2 * wins, blk)], axis=1
        )
        out = lax.dot_general(
            left, rhs, (((0,), (0,)), ((), ())), preferred_element_type=jnp.float32
        )
        o_ref[0, jl, 0] = out[:, :blk] * scale
        o_ref[0, jl, 1] = out[:, blk:] * scale
        return carry

    lax.fori_loop(0, bins, one_bin, 0, unroll=True)


def stack_pairs(local, partner, pair_blocks, kept_windows, chunk, all_bins, previous=None):
    segs, bins, two, wins, chans = local.shape
    blocks_per_half = chans // CH_BLK
    npairs = pair_blocks.shape[0]

    def left_map(p, pb, kw):
        return (0, 0, 0, 0, pb[p, 0] % blocks_per_half)

    def right_map(p, pb, kw):
        return (0, 0, 0, 0, pb[p, 1] % blocks_per_half)

    block = (segs, bins, two, wins, CH_BLK)
    in_specs = [pl.BlockSpec(block, left_map)] * 2 + [pl.BlockSpec(block, right_map)] * 2
    operands = [pair_blocks, kept_windows, local, partner, local, partner]
    aliases = {}
    if previous is not None:
        in_specs.append(pl.BlockSpec(memory_space=pl.ANY))
        operands.append(previous)
        aliases = {6: 0}
    grid_spec = pltpu.PrefetchScalarGridSpec(
        num_scalar_prefetch=2,
        grid=(npairs,),
        in_specs=in_specs,
        out_specs=pl.BlockSpec(
            (1, bins, 2, CH_BLK, CH_BLK), lambda p, pb, kw: (p, chunk, 0, 0, 0)
        ),
    )
    flops = 2 * npairs * bins * CH_BLK * (2 * CH_BLK) * (segs * two * wins)
    out_bytes = npairs * bins * 2 * CH_BLK * CH_BLK * 4
    in_bytes = 4 * npairs * segs * bins * two * wins * CH_BLK * 2
    return pl.pallas_call(
        functools.partial(stack_kernel_for, blocks_per_half),
        grid_spec=grid_spec,
        out_shape=jax.ShapeDtypeStruct((npairs, all_bins, 2, CH_BLK, CH_BLK), jnp.float32),
        input_output_aliases=aliases,
        compiler_params=pltpu.CompilerParams(
            dimension_semantics=("arbitrary",), vmem_limit_bytes=48 * 1024 * 1024
        ),
        cost_estimate=pl.CostEstimate(
            flops=flops, bytes_accessed=out_bytes + in_bytes, transcendentals=0
        ),
    )(*operands)


def per_device(recording, fir_taps, kept_windows, pair_blocks):
    channels, length = recording.shape
    width = fir_taps.shape[0]
    sections = lax.axis_size("tm")
    tail_rows = from_behind(recording[:, length - width :], "tm", 1)
    windows_dev = length // WIN
    bins_dev = NF // sections
    small = max(bins_dev // 2, 1)
    chunks = [0, bins_dev - small, bins_dev] if bins_dev > 1 else [0, bins_dev]
    whitened = whiten_front(recording, tail_rows, fir_taps, kept_windows, chunks)
    result = None
    for lo, hi, part in zip(chunks[:-1], chunks[1:], whitened):
        outgoing = part.reshape(sections, hi - lo, 2, windows_dev, channels)
        by_freq = lax.all_to_all(outgoing, "tm", split_axis=0, concat_axis=0, tiled=True)
        partner = lax.ppermute(by_freq, "pair", [(0, 1), (1, 0)])
        result = stack_pairs(
            by_freq, partner, pair_blocks, kept_windows, lo // (hi - lo), bins_dev, result
        )
    return result


def solution(mesh):
    placed = (P(("groups", "pair"), "tm"), P(), P("groups"), P(("groups", "pair"), None))
    return jax.shard_map(
        per_device,
        mesh=mesh,
        in_specs=placed,
        out_specs=P(("groups", "pair"), "tm", None, None, None),
        check_vma=False,
    )
```

```python
import functools
import math

import jax
import jax.numpy as jnp
import ml_dtypes
import numpy as np
from jax import lax
from jax.experimental import pallas as pl
from jax.experimental.pallas import tpu as pltpu
from jax.sharding import PartitionSpec as P

CH_BLK = 128
WIN = 512
NF = 128
FLO = 8


whiten_eps = 1e-06


def from_behind(array, axis, by):
    count = lax.axis_size(axis)
    pairs = [(i, i + by) for i in range(count) if 0 <= i + by < count]
    return lax.ppermute(array, axis, pairs)


def exchange(outgoing, axis):
    count = lax.axis_size(axis)
    me = lax.axis_index(axis)
    pieces = [lax.dynamic_index_in_dim(outgoing, me, 0, keepdims=False)]
    for shift in range(1, count):
        piece = lax.dynamic_index_in_dim(outgoing, (me + shift) % count, 0, keepdims=False)
        pairs = [(i, (i + shift) % count) for i in range(count)]
        pieces.append(lax.ppermute(piece, axis, pairs))
    return jnp.stack(pieces)


def toeplitz(fir_taps):
    length = fir_taps.shape[0]
    reversed_taps = fir_taps[::-1]
    base_column = jnp.concatenate(
        [jnp.zeros((1,), fir_taps.dtype), reversed_taps, jnp.zeros((length,), fir_taps.dtype)]
    )
    flattened = jnp.tile(base_column, length)[: 2 * length * length]
    return flattened.reshape(length, 2 * length).T


def bandpass(recording, fir_taps, tail_rows):
    channels, length = recording.shape
    width = fir_taps.shape[0]
    current = recording.reshape(channels, length // width, width)
    previous = jnp.concatenate([tail_rows[:, None, :], current[:, :-1, :]], axis=1)
    extended = jnp.concatenate([previous, current], axis=2).reshape(
        channels * (length // width), 2 * width
    )
    product = jnp.dot(extended, toeplitz(fir_taps), preferred_element_type=jnp.float32)
    return product.reshape(channels, length).astype(jnp.bfloat16)


def dft_table(length, bins, lowest):
    samples = np.arange(length, dtype=np.int64)
    indices = lowest + np.arange(bins, dtype=np.int64)
    phase = (samples[:, None] * indices[None, :] % length).astype(np.float64) * (
        2.0 * math.pi / length
    )
    basis_table = np.stack([np.cos(phase), -np.sin(phase)], axis=2)
    return basis_table.reshape(length, 2 * bins).astype(ml_dtypes.bfloat16)


def front_kernel(cnt_ref, rec_ref, toep_ref, basis_ref, *rest):
    outs, f1_ref, (scr_ref, inv_ref) = rest[:-3], rest[-3], rest[-2:]
    tile, length = rec_ref.shape
    width = toep_ref.shape[1]
    bins2 = basis_ref.shape[1]
    windows = length // WIN
    toep = toep_ref[...]
    basis = basis_ref[...]
    count = cnt_ref[lax.axis_index("tm")]
    f1_ref[...] = jnp.dot(
        rec_ref[:, 0 : 2 * width], toep, preferred_element_type=jnp.float32
    ).astype(jnp.bfloat16)
    for h in range(tile // CH_BLK):
        scr_ref[h, pl.ds(0, bins2), :] = jnp.zeros((bins2, CH_BLK), jnp.float32)
    inv_ref[pl.ds(0, 1), :] = jnp.zeros((1, tile), jnp.float32)
    for w in range(1, windows):
        ext0 = rec_ref[:, WIN * w - width : WIN * w + width]
        ext1 = rec_ref[:, WIN * w : WIN * w + 2 * width]
        f0 = jnp.dot(ext0, toep, preferred_element_type=jnp.float32).astype(jnp.bfloat16)
        f1 = jnp.dot(ext1, toep, preferred_element_type=jnp.float32).astype(jnp.bfloat16)
        spec = jnp.dot(
            jnp.concatenate([f0, f1], axis=1), basis, preferred_element_type=jnp.float32
        ).T
        for h in range(tile // CH_BLK):
            scr_ref[h, pl.ds(bins2 * w, bins2), :] = spec[:, CH_BLK * h : CH_BLK * (h + 1)]
        power = jnp.sum(spec * spec, axis=0, keepdims=True) * (1.0 / bins2)
        keep = jnp.where(count > w, 1.0, 0.0).astype(jnp.float32)
        inv_ref[pl.ds(w, 1), :] = lax.rsqrt(power + whiten_eps) * keep
    scales = inv_ref[...]

    start = 0
    for o_ref in outs:

        def one_row(k, carry, o_ref=o_ref, start=start):
            for h in range(tile // CH_BLK):
                rows = scr_ref[h, pl.ds(start + k, windows, stride=bins2), :]
                part = rows * scales[:, CH_BLK * h : CH_BLK * (h + 1)]
                o_ref[k, :, CH_BLK * h : CH_BLK * (h + 1)] = part.astype(o_ref.dtype)
            return carry

        lax.fori_loop(0, o_ref.shape[0], one_row, 0, unroll=64)
        start += o_ref.shape[0]


def first_window_kernel(count_parts, cnt_ref, tail_ref, rec_ref, f1_ref, toep_ref, basis_ref, *rest):
    ins, outs, w0_ref = rest[:count_parts], rest[count_parts : 2 * count_parts], rest[-1]
    bins2 = basis_ref.shape[1]
    count = cnt_ref[lax.axis_index("tm")]
    ext0 = jnp.concatenate([tail_ref[...], rec_ref[...]], axis=1)
    f0 = jnp.dot(ext0, toep_ref[...], preferred_element_type=jnp.float32).astype(jnp.bfloat16)
    spec = jnp.dot(
        jnp.concatenate([f0, f1_ref[...]], axis=1), basis_ref[...], preferred_element_type=jnp.float32
    ).T
    power = jnp.sum(spec * spec, axis=0, keepdims=True) * (1.0 / bins2)
    keep = jnp.where(count > 0, 1.0, 0.0).astype(jnp.float32)
    w0_ref[...] = spec * (lax.rsqrt(power + whiten_eps) * keep)
    start = 0
    for i_ref, o_ref in zip(ins, outs):

        def one_row(k, carry, i_ref=i_ref, o_ref=o_ref, start=start):
            held = i_ref[k]
            first = w0_ref[pl.ds(start + k, 1), :].astype(held.dtype)
            rowid = lax.broadcasted_iota(jnp.int32, held.shape, 0)
            o_ref[k] = jnp.where(rowid == 0, first, held)
            return carry

        lax.fori_loop(0, o_ref.shape[0], one_row, 0, unroll=8)
        start += o_ref.shape[0]


def fill_first_window(parts, recording, tail_rows, f1, toep, basis, kept_count):
    channels, width = tail_rows.shape
    bins2 = basis.shape[1]
    count_parts = len(parts)
    full = lambda shape: pl.BlockSpec(shape, lambda i, c: (0,) * len(shape))
    grid_spec = pltpu.PrefetchScalarGridSpec(
        num_scalar_prefetch=1,
        grid=(1,),
        in_specs=[
            full(tail_rows.shape),
            pl.BlockSpec((channels, width), lambda i, c: (0, 0)),
            full(f1.shape),
            full(toep.shape),
            full(basis.shape),
        ]
        + [full(p.shape) for p in parts],
        out_specs=[full(p.shape) for p in parts],
        scratch_shapes=[pltpu.VMEM((bins2, channels), jnp.float32)],
    )
    return pl.pallas_call(
        functools.partial(first_window_kernel, count_parts),
        grid_spec=grid_spec,
        out_shape=[jax.ShapeDtypeStruct(p.shape, p.dtype) for p in parts],
        input_output_aliases={6 + i: i for i in range(count_parts)},
        compiler_params=pltpu.CompilerParams(
            dimension_semantics=("arbitrary",), vmem_limit_bytes=48 * 1024 * 1024
        ),
        cost_estimate=pl.CostEstimate(
            flops=2 * channels * 3 * (2 * width) * bins2,
            bytes_accessed=4 * sum(p.size for p in parts),
            transcendentals=channels,
        ),
    )(kept_count, tail_rows, recording, f1, toep, basis, *parts)


def whiten_front(recording, tail_rows, fir_taps, kept_count, chunks, tile=512):
    channels, length = recording.shape
    width = tail_rows.shape[1]
    windows = length // WIN
    toep = toeplitz(fir_taps)
    sections = lax.axis_size("tm")
    bins_dev = NF // sections
    basis = dft_table(WIN, NF, FLO).reshape(WIN, sections, bins_dev, 2)
    basis = np.concatenate(
        [basis[:, :, lo:hi].reshape(WIN, -1) for lo, hi in zip(chunks[:-1], chunks[1:])], axis=1
    )
    basis = jnp.asarray(basis)
    bins2 = basis.shape[1]
    rows = [sections * (hi - lo) * 2 for lo, hi in zip(chunks[:-1], chunks[1:])]
    grid_spec = pltpu.PrefetchScalarGridSpec(
        num_scalar_prefetch=1,
        grid=(channels // tile,),
        in_specs=[
            pl.BlockSpec((tile, length), lambda i, c: (i, 0)),
            pl.BlockSpec(toep.shape, lambda i, c: (0, 0)),
            pl.BlockSpec(basis.shape, lambda i, c: (0, 0)),
        ],
        out_specs=[pl.BlockSpec((r, windows, tile), lambda i, c: (0, 0, i)) for r in rows]
        + [pl.BlockSpec((tile, width), lambda i, c: (i, 0))],
        scratch_shapes=[
            pltpu.VMEM((tile // CH_BLK, windows * bins2, CH_BLK), jnp.float32),
            pltpu.VMEM((windows, tile), jnp.float32),
        ],
    )
    flops = 2 * channels * windows * 3 * (2 * width) * bins2 * 2
    *parts, f1 = pl.pallas_call(
        front_kernel,
        grid_spec=grid_spec,
        out_shape=[jax.ShapeDtypeStruct((r, windows, channels), jnp.bfloat16) for r in rows]
        + [jax.ShapeDtypeStruct((channels, width), jnp.bfloat16)],
        compiler_params=pltpu.CompilerParams(
            dimension_semantics=("arbitrary",), vmem_limit_bytes=48 * 1024 * 1024
        ),
        cost_estimate=pl.CostEstimate(
            flops=flops,
            bytes_accessed=channels * length * 2 + bins2 * windows * channels * 2,
            transcendentals=channels * windows,
        ),
    )(kept_count, recording, toep, basis)
    return fill_first_window(parts, recording, tail_rows, f1, toep, basis, kept_count)


def stack_kernel_for(half_blocks, pb_ref, kw_ref, am_ref, ap_ref, bm_ref, bp_ref, *rest):
    o_ref = rest[-1]
    sections = kw_ref.shape[0]
    total = kw_ref[0]
    for s in range(1, sections):
        total = total + kw_ref[s]
    scale = 1.0 / jnp.sqrt(jnp.full((1, 1), total, jnp.int32).astype(jnp.float32))
    segs, bins, _, wins, blk = am_ref.shape
    p = pl.program_id(0)
    mine = lax.axis_index("pair")
    left_mine = pb_ref[p, 0] // half_blocks == mine
    right_mine = pb_ref[p, 1] // half_blocks == mine

    def one_bin(jl, carry):
        left = jnp.where(left_mine, am_ref[:, jl], ap_ref[:, jl]).reshape(segs * 2 * wins, blk)
        right = jnp.where(right_mine, bm_ref[:, jl], bp_ref[:, jl])
        swapped = jnp.concatenate([right[:, 1:2], -right[:, 0:1]], axis=1)
        rhs = jnp.concatenate(
            [right.reshape(segs * 2 * wins, blk), swapped.reshape(segs * 2 * wins, blk)], axis=1
        )
        out = lax.dot_general(
            left, rhs, (((0,), (0,)), ((), ())), preferred_element_type=jnp.float32
        )
        o_ref[0, jl, 0] = out[:, :blk] * scale
        o_ref[0, jl, 1] = out[:, blk:] * scale
        return carry

    lax.fori_loop(0, bins, one_bin, 0, unroll=True)


def stack_pairs(local, partner, pair_blocks, kept_windows, chunk, all_bins, previous=None):
    segs, bins, two, wins, chans = local.shape
    blocks_per_half = chans // CH_BLK
    npairs = pair_blocks.shape[0]

    def left_map(p, pb, kw):
        return (0, 0, 0, 0, pb[p, 0] % blocks_per_half)

    def right_map(p, pb, kw):
        return (0, 0, 0, 0, pb[p, 1] % blocks_per_half)

    block = (segs, bins, two, wins, CH_BLK)
    in_specs = [pl.BlockSpec(block, left_map)] * 2 + [pl.BlockSpec(block, right_map)] * 2
    operands = [pair_blocks, kept_windows, local, partner, local, partner]
    aliases = {}
    if previous is not None:
        in_specs.append(pl.BlockSpec(memory_space=pl.ANY))
        operands.append(previous)
        aliases = {6: 0}
    grid_spec = pltpu.PrefetchScalarGridSpec(
        num_scalar_prefetch=2,
        grid=(npairs,),
        in_specs=in_specs,
        out_specs=pl.BlockSpec(
            (1, bins, 2, CH_BLK, CH_BLK), lambda p, pb, kw: (p, chunk, 0, 0, 0)
        ),
    )
    flops = 2 * npairs * bins * CH_BLK * (2 * CH_BLK) * (segs * two * wins)
    out_bytes = npairs * bins * 2 * CH_BLK * CH_BLK * 4
    in_bytes = 4 * npairs * segs * bins * two * wins * CH_BLK * 2
    return pl.pallas_call(
        functools.partial(stack_kernel_for, blocks_per_half),
        grid_spec=grid_spec,
        out_shape=jax.ShapeDtypeStruct((npairs, all_bins, 2, CH_BLK, CH_BLK), jnp.float32),
        input_output_aliases=aliases,
        compiler_params=pltpu.CompilerParams(
            dimension_semantics=("arbitrary",), vmem_limit_bytes=48 * 1024 * 1024
        ),
        cost_estimate=pl.CostEstimate(
            flops=flops, bytes_accessed=out_bytes + in_bytes, transcendentals=0
        ),
    )(*operands)


def per_device(recording, fir_taps, kept_windows, pair_blocks):
    channels, length = recording.shape
    width = fir_taps.shape[0]
    sections = lax.axis_size("tm")
    tail_rows = from_behind(recording[:, length - width :], "tm", 1)
    windows_dev = length // WIN
    bins_dev = NF // sections
    small = max(bins_dev // 2, 1)
    chunks = [0, bins_dev - small, bins_dev] if bins_dev > 1 else [0, bins_dev]
    whitened = whiten_front(recording, tail_rows, fir_taps, kept_windows, chunks)
    result = None
    for lo, hi, part in zip(chunks[:-1], chunks[1:], whitened):
        outgoing = part.reshape(sections, hi - lo, 2, windows_dev, channels)
        by_freq = lax.all_to_all(outgoing, "tm", split_axis=0, concat_axis=0, tiled=True)
        partner = lax.ppermute(by_freq, "pair", [(0, 1), (1, 0)])
        result = stack_pairs(
            by_freq, partner, pair_blocks, kept_windows, lo // (hi - lo), bins_dev, result
        )
    return result


def solution(mesh):
    placed = (P(("groups", "pair"), "tm"), P(), P("groups"), P(("groups", "pair"), None))
    return jax.shard_map(
        per_device,
        mesh=mesh,
        in_specs=placed,
        out_specs=P(("groups", "pair"), "tm", None, None, None),
        check_vma=False,
    )
```

```python
import functools
import math

import jax
import jax.numpy as jnp
import ml_dtypes
import numpy as np
from jax import lax
from jax.experimental import pallas as pl
from jax.experimental.pallas import tpu as pltpu
from jax.sharding import PartitionSpec as P

CH_BLK = 128
WIN = 512
NF = 128
FLO = 8


whiten_eps = 1e-06


def from_behind(array, axis, by):
    count = lax.axis_size(axis)
    pairs = [(i, i + by) for i in range(count) if 0 <= i + by < count]
    return lax.ppermute(array, axis, pairs)


def exchange(outgoing, axis):
    count = lax.axis_size(axis)
    me = lax.axis_index(axis)
    pieces = [lax.dynamic_index_in_dim(outgoing, me, 0, keepdims=False)]
    for shift in range(1, count):
        piece = lax.dynamic_index_in_dim(outgoing, (me + shift) % count, 0, keepdims=False)
        pairs = [(i, (i + shift) % count) for i in range(count)]
        pieces.append(lax.ppermute(piece, axis, pairs))
    return jnp.stack(pieces)


def toeplitz(fir_taps):
    length = fir_taps.shape[0]
    reversed_taps = fir_taps[::-1]
    base_column = jnp.concatenate(
        [jnp.zeros((1,), fir_taps.dtype), reversed_taps, jnp.zeros((length,), fir_taps.dtype)]
    )
    flattened = jnp.tile(base_column, length)[: 2 * length * length]
    return flattened.reshape(length, 2 * length).T


def bandpass(recording, fir_taps, tail_rows):
    channels, length = recording.shape
    width = fir_taps.shape[0]
    current = recording.reshape(channels, length // width, width)
    previous = jnp.concatenate([tail_rows[:, None, :], current[:, :-1, :]], axis=1)
    extended = jnp.concatenate([previous, current], axis=2).reshape(
        channels * (length // width), 2 * width
    )
    product = jnp.dot(extended, toeplitz(fir_taps), preferred_element_type=jnp.float32)
    return product.reshape(channels, length).astype(jnp.bfloat16)


def dft_table(length, bins, lowest):
    samples = np.arange(length, dtype=np.int64)
    indices = lowest + np.arange(bins, dtype=np.int64)
    phase = (samples[:, None] * indices[None, :] % length).astype(np.float64) * (
        2.0 * math.pi / length
    )
    basis_table = np.stack([np.cos(phase), -np.sin(phase)], axis=2)
    return basis_table.reshape(length, 2 * bins).astype(ml_dtypes.bfloat16)


def front_kernel(cnt_ref, rec_ref, toep_ref, basis_ref, *rest):
    outs, f1_ref, (scr_ref, inv_ref) = rest[:-3], rest[-3], rest[-2:]
    tile, length = rec_ref.shape
    width = toep_ref.shape[1]
    bins2 = basis_ref.shape[1]
    windows = length // WIN
    toep = toep_ref[...]
    basis = basis_ref[...]
    count = cnt_ref[lax.axis_index("tm")]
    f1_ref[...] = jnp.dot(
        rec_ref[:, 0 : 2 * width], toep, preferred_element_type=jnp.float32
    ).astype(jnp.bfloat16)
    for h in range(tile // CH_BLK):
        scr_ref[h, pl.ds(0, bins2), :] = jnp.zeros((bins2, CH_BLK), jnp.float32)
    inv_ref[pl.ds(0, 1), :] = jnp.zeros((1, tile), jnp.float32)
    for w in range(1, windows):
        ext0 = rec_ref[:, WIN * w - width : WIN * w + width]
        ext1 = rec_ref[:, WIN * w : WIN * w + 2 * width]
        f0 = jnp.dot(ext0, toep, preferred_element_type=jnp.float32).astype(jnp.bfloat16)
        f1 = jnp.dot(ext1, toep, preferred_element_type=jnp.float32).astype(jnp.bfloat16)
        spec = jnp.dot(
            jnp.concatenate([f0, f1], axis=1), basis, preferred_element_type=jnp.float32
        ).T
        for h in range(tile // CH_BLK):
            scr_ref[h, pl.ds(bins2 * w, bins2), :] = spec[:, CH_BLK * h : CH_BLK * (h + 1)]
        power = jnp.sum(spec * spec, axis=0, keepdims=True) * (1.0 / bins2)
        keep = jnp.where(count > w, 1.0, 0.0).astype(jnp.float32)
        inv_ref[pl.ds(w, 1), :] = lax.rsqrt(power + whiten_eps) * keep
    scales = inv_ref[...]

    start = 0
    for o_ref in outs:

        def one_row(k, carry, o_ref=o_ref, start=start):
            for h in range(tile // CH_BLK):
                rows = scr_ref[h, pl.ds(start + k, windows, stride=bins2), :]
                part = rows * scales[:, CH_BLK * h : CH_BLK * (h + 1)]
                o_ref[k, :, CH_BLK * h : CH_BLK * (h + 1)] = part.astype(o_ref.dtype)
            return carry

        lax.fori_loop(0, o_ref.shape[0], one_row, 0, unroll=True)
        start += o_ref.shape[0]


def first_window_kernel(count_parts, cnt_ref, tail_ref, rec_ref, f1_ref, toep_ref, basis_ref, *rest):
    ins, outs, w0_ref = rest[:count_parts], rest[count_parts : 2 * count_parts], rest[-1]
    bins2 = basis_ref.shape[1]
    count = cnt_ref[lax.axis_index("tm")]
    ext0 = jnp.concatenate([tail_ref[...], rec_ref[...]], axis=1)
    f0 = jnp.dot(ext0, toep_ref[...], preferred_element_type=jnp.float32).astype(jnp.bfloat16)
    spec = jnp.dot(
        jnp.concatenate([f0, f1_ref[...]], axis=1), basis_ref[...], preferred_element_type=jnp.float32
    ).T
    power = jnp.sum(spec * spec, axis=0, keepdims=True) * (1.0 / bins2)
    keep = jnp.where(count > 0, 1.0, 0.0).astype(jnp.float32)
    w0_ref[...] = spec * (lax.rsqrt(power + whiten_eps) * keep)
    start = 0
    for i_ref, o_ref in zip(ins, outs):

        def one_row(k, carry, i_ref=i_ref, o_ref=o_ref, start=start):
            held = i_ref[k]
            first = w0_ref[pl.ds(start + k, 1), :].astype(held.dtype)
            rowid = lax.broadcasted_iota(jnp.int32, held.shape, 0)
            o_ref[k] = jnp.where(rowid == 0, first, held)
            return carry

        lax.fori_loop(0, o_ref.shape[0], one_row, 0, unroll=8)
        start += o_ref.shape[0]


def fill_first_window(parts, recording, tail_rows, f1, toep, basis, kept_count):
    channels, width = tail_rows.shape
    bins2 = basis.shape[1]
    count_parts = len(parts)
    full = lambda shape: pl.BlockSpec(shape, lambda i, c: (0,) * len(shape))
    grid_spec = pltpu.PrefetchScalarGridSpec(
        num_scalar_prefetch=1,
        grid=(1,),
        in_specs=[
            full(tail_rows.shape),
            pl.BlockSpec((channels, width), lambda i, c: (0, 0)),
            full(f1.shape),
            full(toep.shape),
            full(basis.shape),
        ]
        + [full(p.shape) for p in parts],
        out_specs=[full(p.shape) for p in parts],
        scratch_shapes=[pltpu.VMEM((bins2, channels), jnp.float32)],
    )
    return pl.pallas_call(
        functools.partial(first_window_kernel, count_parts),
        grid_spec=grid_spec,
        out_shape=[jax.ShapeDtypeStruct(p.shape, p.dtype) for p in parts],
        input_output_aliases={6 + i: i for i in range(count_parts)},
        compiler_params=pltpu.CompilerParams(
            dimension_semantics=("arbitrary",), vmem_limit_bytes=48 * 1024 * 1024
        ),
        cost_estimate=pl.CostEstimate(
            flops=2 * channels * 3 * (2 * width) * bins2,
            bytes_accessed=4 * sum(p.size for p in parts),
            transcendentals=channels,
        ),
    )(kept_count, tail_rows, recording, f1, toep, basis, *parts)


def whiten_front(recording, tail_rows, fir_taps, kept_count, chunks, tile=512):
    channels, length = recording.shape
    width = tail_rows.shape[1]
    windows = length // WIN
    toep = toeplitz(fir_taps)
    sections = lax.axis_size("tm")
    bins_dev = NF // sections
    basis = dft_table(WIN, NF, FLO).reshape(WIN, sections, bins_dev, 2)
    basis = np.concatenate(
        [basis[:, :, lo:hi].reshape(WIN, -1) for lo, hi in zip(chunks[:-1], chunks[1:])], axis=1
    )
    basis = jnp.asarray(basis)
    bins2 = basis.shape[1]
    rows = [sections * (hi - lo) * 2 for lo, hi in zip(chunks[:-1], chunks[1:])]
    grid_spec = pltpu.PrefetchScalarGridSpec(
        num_scalar_prefetch=1,
        grid=(channels // tile,),
        in_specs=[
            pl.BlockSpec((tile, length), lambda i, c: (i, 0)),
            pl.BlockSpec(toep.shape, lambda i, c: (0, 0)),
            pl.BlockSpec(basis.shape, lambda i, c: (0, 0)),
        ],
        out_specs=[pl.BlockSpec((r, windows, tile), lambda i, c: (0, 0, i)) for r in rows]
        + [pl.BlockSpec((tile, width), lambda i, c: (i, 0))],
        scratch_shapes=[
            pltpu.VMEM((tile // CH_BLK, windows * bins2, CH_BLK), jnp.float32),
            pltpu.VMEM((windows, tile), jnp.float32),
        ],
    )
    flops = 2 * channels * windows * 3 * (2 * width) * bins2 * 2
    *parts, f1 = pl.pallas_call(
        front_kernel,
        grid_spec=grid_spec,
        out_shape=[jax.ShapeDtypeStruct((r, windows, channels), jnp.bfloat16) for r in rows]
        + [jax.ShapeDtypeStruct((channels, width), jnp.bfloat16)],
        compiler_params=pltpu.CompilerParams(
            dimension_semantics=("arbitrary",), vmem_limit_bytes=48 * 1024 * 1024
        ),
        cost_estimate=pl.CostEstimate(
            flops=flops,
            bytes_accessed=channels * length * 2 + bins2 * windows * channels * 2,
            transcendentals=channels * windows,
        ),
    )(kept_count, recording, toep, basis)
    return fill_first_window(parts, recording, tail_rows, f1, toep, basis, kept_count)


def stack_kernel_for(half_blocks, pb_ref, kw_ref, am_ref, ap_ref, bm_ref, bp_ref, *rest):
    o_ref = rest[-1]
    sections = kw_ref.shape[0]
    total = kw_ref[0]
    for s in range(1, sections):
        total = total + kw_ref[s]
    scale = 1.0 / jnp.sqrt(jnp.full((1, 1), total, jnp.int32).astype(jnp.float32))
    segs, bins, _, wins, blk = am_ref.shape
    p = pl.program_id(0)
    mine = lax.axis_index("pair")
    left_mine = pb_ref[p, 0] // half_blocks == mine
    right_mine = pb_ref[p, 1] // half_blocks == mine

    def one_bin(jl, carry):
        left = jnp.where(left_mine, am_ref[:, jl], ap_ref[:, jl]).reshape(segs * 2 * wins, blk)
        right = jnp.where(right_mine, bm_ref[:, jl], bp_ref[:, jl])
        swapped = jnp.concatenate([right[:, 1:2], -right[:, 0:1]], axis=1)
        rhs = jnp.concatenate(
            [right.reshape(segs * 2 * wins, blk), swapped.reshape(segs * 2 * wins, blk)], axis=1
        )
        out = lax.dot_general(
            left, rhs, (((0,), (0,)), ((), ())), preferred_element_type=jnp.float32
        )
        o_ref[0, jl, 0] = out[:, :blk] * scale
        o_ref[0, jl, 1] = out[:, blk:] * scale
        return carry

    lax.fori_loop(0, bins, one_bin, 0, unroll=True)


def stack_pairs(local, partner, pair_blocks, kept_windows, chunk, all_bins, previous=None):
    segs, bins, two, wins, chans = local.shape
    blocks_per_half = chans // CH_BLK
    npairs = pair_blocks.shape[0]

    def left_map(p, pb, kw):
        return (0, 0, 0, 0, pb[p, 0] % blocks_per_half)

    def right_map(p, pb, kw):
        return (0, 0, 0, 0, pb[p, 1] % blocks_per_half)

    block = (segs, bins, two, wins, CH_BLK)
    in_specs = [pl.BlockSpec(block, left_map)] * 2 + [pl.BlockSpec(block, right_map)] * 2
    operands = [pair_blocks, kept_windows, local, partner, local, partner]
    aliases = {}
    if previous is not None:
        in_specs.append(pl.BlockSpec(memory_space=pl.ANY))
        operands.append(previous)
        aliases = {6: 0}
    grid_spec = pltpu.PrefetchScalarGridSpec(
        num_scalar_prefetch=2,
        grid=(npairs,),
        in_specs=in_specs,
        out_specs=pl.BlockSpec(
            (1, bins, 2, CH_BLK, CH_BLK), lambda p, pb, kw: (p, chunk, 0, 0, 0)
        ),
    )
    flops = 2 * npairs * bins * CH_BLK * (2 * CH_BLK) * (segs * two * wins)
    out_bytes = npairs * bins * 2 * CH_BLK * CH_BLK * 4
    in_bytes = 4 * npairs * segs * bins * two * wins * CH_BLK * 2
    return pl.pallas_call(
        functools.partial(stack_kernel_for, blocks_per_half),
        grid_spec=grid_spec,
        out_shape=jax.ShapeDtypeStruct((npairs, all_bins, 2, CH_BLK, CH_BLK), jnp.float32),
        input_output_aliases=aliases,
        compiler_params=pltpu.CompilerParams(
            dimension_semantics=("arbitrary",), vmem_limit_bytes=48 * 1024 * 1024
        ),
        cost_estimate=pl.CostEstimate(
            flops=flops, bytes_accessed=out_bytes + in_bytes, transcendentals=0
        ),
    )(*operands)


def per_device(recording, fir_taps, kept_windows, pair_blocks):
    channels, length = recording.shape
    width = fir_taps.shape[0]
    sections = lax.axis_size("tm")
    tail_rows = from_behind(recording[:, length - width :], "tm", 1)
    windows_dev = length // WIN
    bins_dev = NF // sections
    small = max(bins_dev // 2, 1)
    chunks = [0, bins_dev - small, bins_dev] if bins_dev > 1 else [0, bins_dev]
    whitened = whiten_front(recording, tail_rows, fir_taps, kept_windows, chunks)
    result = None
    for lo, hi, part in zip(chunks[:-1], chunks[1:], whitened):
        outgoing = part.reshape(sections, hi - lo, 2, windows_dev, channels)
        by_freq = lax.all_to_all(outgoing, "tm", split_axis=0, concat_axis=0, tiled=True)
        partner = lax.ppermute(by_freq, "pair", [(0, 1), (1, 0)])
        result = stack_pairs(
            by_freq, partner, pair_blocks, kept_windows, lo // (hi - lo), bins_dev, result
        )
    return result


def solution(mesh):
    placed = (P(("groups", "pair"), "tm"), P(), P("groups"), P(("groups", "pair"), None))
    return jax.shard_map(
        per_device,
        mesh=mesh,
        in_specs=placed,
        out_specs=P(("groups", "pair"), "tm", None, None, None),
        check_vma=False,
    )
```
